32 devices in a mesh: expert: 4 (over z), shard: 8 (over y, x, core).
Axes of the slice: x: 2, y: 2, z: 4, core: 2. Of those that a mesh axis runs over, the one named last changes fastest.
Arguments:
- tokens: bfloat16 [18912, 768], P(('expert', 'shard')), may hold values from -6 to 6
- image_counts: int32 [4, 8], P('expert', 'shard'), may hold values from 1 to 3, as said below
- routes: int32 [18912, 2], P(('expert', 'shard')), may hold values from 0 to 3, all different within a row; in each aligned block of 591 rows (0 to 590, 591 to 1181, ...) at most 376 rows name the same one
- w_qkv: bfloat16 [768, 2304], P('shard'), may hold values from -0.21875 to 0.21875
- w_out: bfloat16 [768, 768], P('shard'), may hold values from -1.5 to 1.5
- w_router: bfloat16 [768, 4], P('shard'), may hold values from -0.15625 to 0.15625
- gain_attn: bfloat16 [768], P('shard'), may hold values from 0.25 to 1.75
- gain_moe: bfloat16 [768], P('shard'), may hold values from 0.25 to 1.75
- w_in: bfloat16 [4, 768, 3072], P('expert', 'shard'), may hold values from -0.21875 to 0.21875
- w_back: bfloat16 [4, 3072, 768], P('expert', 'shard'), may hold values from -0.625 to 0.625
- cotangent: bfloat16 [18912, 768], P(('expert', 'shard')), may hold values from -6 to 6
Outputs:
- output: bfloat16 [18912, 768], P(('expert', 'shard'))
- grad_tokens: bfloat16 [18912, 768], P(('expert', 'shard'))
- grad_w_qkv: float32 [768, 2304], P('shard')
- grad_w_out: float32 [768, 768], P('shard')
- grad_w_router: float32 [768, 4], P('shard')
- grad_gain_attn: float32 [768], P('shard')
- grad_gain_moe: float32 [768], P('shard')
- grad_w_in: float32 [4, 768, 3072], P('expert', 'shard')
- grad_w_back: float32 [4, 3072, 768], P('expert', 'shard')
The draws below stay inside these ranges and needn't reach their ends.
Inputs may be any that keep to these rules, and one draw needn't show every extreme that they name: `image_counts`: each device holds between 1 and 3 live images; some device holds 3 and some holds 1. `routes`: the two experts of a token differ; among the rows of one device at most 376 name any one expert.
All inputs are finite; a program needn't handle non-finite values.
Results may differ from the reference program's by a relative error of at most 0.024.
Values may be sent and summed in bfloat16 or wider, within the bound.
No kernel may reach another device: no remote copies, remote signals or barrier semaphores. Data moves between devices by JAX's collectives and lax.ppermute only.
A program may use at most 256 MiB of HBM per device.

```python
import math
from functools import partial
import jax
import jax.numpy as jnp
import numpy as np
from jax import lax

D = 768
H = 12
HD = 64
FF = 3072
SEQ = 197
TOP = 2
IMG_DEV = 3
EXPERTS = 4
ROWS_DEV = 591
TOKENS = 18912
CAP = 376
N_EXPERT = 4
N_SHARD = 8


def draw_image_counts(key, part):
    devices = N_EXPERT * N_SHARD
    first_key, second_key, third_key = jax.random.split(key, 3)
    counts = jax.random.randint(first_key, (devices,), 1, IMG_DEV + 1)
    full_at = jax.random.randint(second_key, (), 0, devices)
    step_by = jax.random.randint(third_key, (), 1, devices)
    counts = counts.at[full_at].set(IMG_DEV).at[(full_at + step_by) % devices].set(1)
    return counts.reshape(N_EXPERT, N_SHARD).astype(jnp.int32)


def level_of(rng, extent, cuts, smallest, top_value):
    factor_of = 1.0
    for dim, parts in cuts:
        draws = jax.random.uniform(jax.random.fold_in(jax.random.fold_in(rng, 6), dim), (parts,), jnp.float32, smallest / len(cuts), top_value / len(cuts))
        factor_of = factor_of * jnp.repeat(jnp.exp(draws), extent[dim] // parts).reshape((-1,) + (1,) * (len(extent) - 1 - dim))
    return factor_of


def deal_out(key, own, number, rows, number_of, top, most, lean):
    order = jax.random.permutation(key, number_of)
    crowded, usual = portions_of(number_of, rows * top, most, lean, True), portions_of(number_of, rows * top, most, lean, False)
    places = jnp.arange(number_of)

    def named(tallies, rotation):
        used = int((tallies > 0).sum())
        fixed = max(1, used // 4)
        moved = fixed + (places - fixed + rotation * (used - fixed)) % max(1, number_of - fixed)
        return jnp.zeros((number_of,), jnp.int32).at[order[jnp.where(places < fixed, places, moved)]].set(jnp.asarray(tallies, jnp.int32))

    tallies = jnp.where(number % 4 == 0, named(crowded, number // 4), named(usual, number - number // 4 - 1))
    mixed = jax.random.permutation(jax.random.fold_in(own, 3), number_of)
    donor, sink = mixed[0:number_of // 2 * 2:2], mixed[1:number_of // 2 * 2:2]
    slack = jnp.minimum(tallies[donor] - 1, most - tallies[sink]) // 2
    slack = jnp.where((donor == order[0]) | (sink == order[0]) | (tallies[sink] == 0), 0, jnp.maximum(slack, 0))
    moved = jax.random.randint(jax.random.fold_in(own, 4), (number_of // 2,), 0, 1 << 20) % (slack + 1)
    tallies = tallies.at[donor].add(-moved).at[sink].add(moved)
    labels = jnp.searchsorted(jnp.cumsum(tallies), jnp.arange(rows * top), side="right").astype(jnp.int32)
    grid = labels.reshape(top, rows).T
    grid = grid[jax.random.permutation(jax.random.fold_in(own, 1), rows)]
    rotation = jax.random.randint(jax.random.fold_in(own, 2), (rows, 1), 0, top)
    return jnp.take_along_axis(grid, (jnp.arange(top)[None, :] + rotation) % top, axis=1)


def portions_of(number_of, total, reach, slope, full):
    portions = [(1 << 20) // math.isqrt(standing ** slope) + 1 for standing in range(1, number_of + 1)]
    largest = reach if full else min(reach, max(-(-total // number_of), total * portions[0] // sum(portions)))
    least = 1 if total - largest >= number_of - 1 else 0
    given, spare = [largest] + [least] * (number_of - 1), total - largest - least * (number_of - 1)
    while spare > 0:
        candidates = [i for i in range(1, number_of) if given[i] < largest] or [i for i in range(1, number_of) if given[i] < reach]
        whole, remaining = sum([portions[i] for i in candidates]), spare
        for i in candidates:
            more = min(reach - given[i], max(1, remaining * portions[i] // whole), spare)
            given[i] = given[i] + more
            spare = spare - more
    return np.array(given)


def scatter_about(key, extent, deviation, bound, shards=(), kind=jnp.bfloat16):
    gain = level_of(key, extent, shards, -0.22, 0.18) if shards else 1.0
    result = jax.random.normal(key, extent, jnp.float32) * deviation * gain
    return jnp.minimum(jnp.maximum(result, -bound), bound).astype(kind)


def setup_inputs(seed: int = 0) -> dict:
    splits = jax.random.split(jax.random.key(seed), 12)
    tokens = scatter_about(splits[0], (TOKENS, D), 1.0, 6.0, ((0, 32),))
    image_counts = draw_image_counts(jax.random.fold_in(splits[11], 71), 0)
    routes_keys = jax.random.split(jax.random.fold_in(splits[2], 1), TOKENS // ROWS_DEV)
    routes_turns = jax.random.permutation(jax.random.fold_in(splits[2], 3), TOKENS // ROWS_DEV)
    routes = jax.vmap(lambda own, number: deal_out(jax.random.fold_in(splits[2], 2), own, number, ROWS_DEV, EXPERTS, TOP, CAP, 2))(routes_keys, routes_turns).reshape((TOKENS, TOP))
    w_qkv = scatter_about(splits[3], (D, 3 * D), D ** -0.5, 0.21875, ((0, 8),))
    w_out = scatter_about(splits[4], (D, D), (D // 48) ** -0.5, 1.5, ((0, 8),))
    w_router = scatter_about(splits[5], (D, EXPERTS), (2 * D) ** -0.5, 0.15625, ((0, 8),))
    gain_attn = jnp.clip(1.0 + 0.15 * jax.random.normal(splits[6], (D,), jnp.float32), 0.25, 1.75).astype(jnp.bfloat16)
    gain_moe = jnp.clip(1.0 + 0.15 * jax.random.normal(splits[7], (D,), jnp.float32), 0.25, 1.75).astype(jnp.bfloat16)
    w_in = scatter_about(splits[8], (EXPERTS, D, FF), D ** -0.5, 0.21875, ((0, 4), (1, 8)))
    w_back = scatter_about(splits[9], (EXPERTS, FF, D), (FF // 32) ** -0.5, 0.625, ((0, 4), (1, 8)))
    cotangent = scatter_about(splits[10], (TOKENS, D), 1.0, 6.0, ((0, 32),))
    return {"tokens": tokens, "image_counts": image_counts, "routes": routes, "w_qkv": w_qkv, "w_out": w_out, "w_router": w_router, "gain_attn": gain_attn, "gain_moe": gain_moe, "w_in": w_in, "w_back": w_back, "cotangent": cotangent}


@jax.custom_vjp
def low(v):
    return lax.optimization_barrier(v.astype(jnp.bfloat16)).astype(jnp.float32)

@jax.custom_vjp
def low_back(v):
    return v

def low_keep(v):
    return (low(v), None)

def low_pass(kept, grad):
    return (grad,)

def back_keep(v):
    return (v, None)

def back_low(kept, grad):
    return (low(grad),)
low.defvjp(low_keep, low_pass)
low_back.defvjp(back_keep, back_low)
PRECISE = lax.Precision.HIGHEST
EPSILON = 1e-06

def layer_norm(values, norm_gain):
    row_mean = lax.optimization_barrier(jnp.mean(values, axis=-1, keepdims=True))
    centered = values - row_mean
    variance = lax.optimization_barrier(jnp.mean(centered * centered, axis=-1, keepdims=True))
    return centered * lax.rsqrt(variance + EPSILON) * norm_gain

def normalize_rows(scores):
    row_top = lax.optimization_barrier(jnp.max(scores, axis=-1, keepdims=True))
    exp_scores = jnp.exp(scores - row_top)
    return exp_scores / lax.optimization_barrier(jnp.sum(exp_scores, axis=-1, keepdims=True))

def attend_block(normed, w_qkv):
    projected = low_back(low(jnp.dot(normed, w_qkv, precision=PRECISE)))
    split_heads = projected.reshape(IMG_DEV, SEQ, 3, H, HD)
    queries = split_heads[:, :, 0]
    keys_part = split_heads[:, :, 1]
    values_part = split_heads[:, :, 2]
    scores = low_back(jnp.einsum('ishd,ithd->ihst', queries, keys_part, precision=PRECISE) * HD ** (-0.5))
    attn_probs = normalize_rows(scores)
    mixed_rows = jnp.einsum('ihst,ithd->ishd', low(attn_probs), values_part, precision=PRECISE)
    return low_back(low(mixed_rows.reshape(ROWS_DEV, D)))

def expert_block(slab_rows, first_weight, second_weight):
    pre_act = low_back(jnp.dot(slab_rows, first_weight, precision=PRECISE))
    activated = low(jax.nn.gelu(pre_act, approximate=False))
    return low_back(low(jnp.dot(activated, second_weight, precision=PRECISE)))

def expert_slabs(packed):
    slabs, first_weight, second_weight = packed
    return lax.map(jax.checkpoint(partial(expert_block, first_weight=first_weight, second_weight=second_weight)), slabs)

def slot_positions(routes, live_int):
    devices = TOKENS // ROWS_DEV
    expert_ids = jnp.arange(EXPERTS, dtype=jnp.int32)
    pick_table = (routes[:, :, None] == expert_ids).astype(jnp.int32) * live_int[:, None, None]
    per_device = pick_table.reshape(devices, ROWS_DEV * TOP, EXPERTS)
    before = jnp.cumsum(per_device, axis=1) - per_device
    slot_index = lax.optimization_barrier(jnp.sum(before * per_device, axis=2)).reshape(TOKENS, TOP)
    device_ids = (jnp.arange(TOKENS, dtype=jnp.int32) // ROWS_DEV)[:, None]
    position = routes * (devices * CAP) + device_ids * CAP + slot_index
    return jnp.where(live_int[:, None] > 0, position, EXPERTS * devices * CAP).astype(jnp.int32)

def forward(tokens, w_qkv, w_out, w_router, gain_attn, gain_moe, w_in, w_back, live_rows, routes, positions):
    devices = TOKENS // ROWS_DEV
    total_slots = EXPERTS * devices * CAP
    attn_in = low(layer_norm(tokens, gain_attn))
    mixed_rows = lax.map(jax.checkpoint(partial(attend_block, w_qkv=w_qkv)), attn_in.reshape(devices, ROWS_DEV, D)).reshape(TOKENS, D)
    hidden_state = tokens + low_back(jnp.dot(mixed_rows, w_out, precision=PRECISE))
    moe_in = low(layer_norm(hidden_state, gain_moe))
    logits = low_back(jnp.dot(moe_in, w_router, precision=PRECISE))
    router_probs = normalize_rows(logits)
    chosen = jnp.take_along_axis(router_probs, routes, axis=1)
    buffer = jnp.zeros((total_slots, D), jnp.float32)
    buffer = buffer.at[positions[:, 0]].add(moe_in, mode='drop').at[positions[:, 1]].add(moe_in, mode='drop')
    buffer = low_back(buffer).reshape(EXPERTS, devices, CAP, D)
    produced = lax.map(expert_slabs, (buffer, w_in, w_back)).reshape(total_slots, D)
    safe_index = jnp.minimum(positions, total_slots - 1)
    moe_out = chosen[:, 0:1] * produced[safe_index[:, 0]] + chosen[:, 1:2] * produced[safe_index[:, 1]]
    return live_rows[:, None] * (hidden_state + live_rows[:, None] * moe_out)

def reference(tokens, image_counts, routes, w_qkv, w_out, w_router, gain_attn, gain_moe, w_in, w_back, cotangent):
    devices = TOKENS // ROWS_DEV
    row_ids = jnp.arange(TOKENS, dtype=jnp.int32)
    device_counts = image_counts.reshape(devices)
    live_int = (row_ids % ROWS_DEV // SEQ < device_counts[row_ids // ROWS_DEV]).astype(jnp.int32)
    live_rows = live_int.astype(jnp.float32)
    positions = slot_positions(routes, live_int)
    params = tuple((argument.astype(jnp.float32) for argument in (tokens, w_qkv, w_out, w_router, gain_attn, gain_moe, w_in, w_back)))
    output, pullback = jax.vjp(partial(forward, live_rows=live_rows, routes=routes, positions=positions), *params)
    grads = pullback(cotangent.astype(jnp.float32))
    return (output.astype(jnp.bfloat16), grads[0].astype(jnp.bfloat16), grads[1], grads[2], grads[3], grads[4], grads[5], grads[6], grads[7])
```

```python
import jax
import jax.numpy as jnp
from jax import lax
from jax.sharding import PartitionSpec as P

H = 12
HD = 64
SEQ = 197


EPSILON = 1e-06
ROW_CONTRACT = (((0,), (0,)), ((), ()))
COL_CONTRACT = (((1,), (1,)), ((), ()))


def layer_norm(values, norm_gain):
    row_mean = jnp.mean(values, axis=-1, keepdims=True)
    centered = values - row_mean
    variance = jnp.mean(centered * centered, axis=-1, keepdims=True)
    return centered * lax.rsqrt(variance + EPSILON) * norm_gain


def normalize_rows(scores):
    row_top = jnp.max(scores, axis=-1, keepdims=True)
    exp_scores = jnp.exp(scores - row_top)
    return exp_scores / jnp.sum(exp_scores, axis=-1, keepdims=True)


def gelu_exact(values):
    return jax.nn.gelu(values, approximate=False)


def shards(
    tokens,
    image_counts,
    routes,
    w_qkv,
    w_out,
    w_router,
    gain_attn,
    gain_moe,
    w_in,
    w_back,
    cotangent,
):
    rows, width = tokens.shape
    experts = lax.axis_size("expert")
    capacity = 8 * (5 * rows // (16 * experts)) + 8
    overflow = experts * capacity
    images = rows // SEQ
    qkv_cols = w_qkv.shape[1]
    n_route = w_router.shape[1]
    ff = w_in.shape[2]
    score_scale = HD ** (-0.5)
    row_ids = jnp.arange(rows, dtype=jnp.int32)
    live_int = (row_ids // SEQ < image_counts[0, 0]).astype(jnp.int32)
    live_rows = live_int.astype(jnp.float32)

    dense_local = jnp.concatenate(
        [w_qkv, w_out, w_router, gain_attn[:, None], gain_moe[:, None]], axis=1
    )
    dense_full = lax.all_gather(dense_local, "shard", axis=0, tiled=True)
    full_qkv = dense_full[:, :qkv_cols]
    full_out = dense_full[:, qkv_cols : qkv_cols + width]
    full_router = dense_full[:, qkv_cols + width : qkv_cols + width + n_route]
    gain_one = dense_full[:, -2].astype(jnp.float32)
    gain_two = dense_full[:, -1].astype(jnp.float32)

    back_rows = w_back.shape[1]
    expert_local = jnp.stack(
        [w_in[0], w_back[0].reshape(back_rows * width // ff, ff)], axis=0
    )
    expert_full = lax.all_gather(expert_local, "shard", axis=1, tiled=True)
    expert_first = expert_full[0]
    expert_second = expert_full[1].reshape(ff, width)

    token_f = tokens.astype(jnp.float32)
    attn_in = layer_norm(token_f, gain_one).astype(jnp.bfloat16)
    projected = jnp.dot(attn_in, full_qkv, preferred_element_type=jnp.float32).astype(jnp.bfloat16)
    split_heads = projected.reshape(images, SEQ, 3, H, HD)
    queries = split_heads[:, :, 0]
    keys_part = split_heads[:, :, 1]
    values_part = split_heads[:, :, 2]
    scores = (
        jnp.einsum("ishd,ithd->ihst", queries, keys_part, preferred_element_type=jnp.float32)
        * score_scale
    )
    row_top = jnp.max(scores, axis=-1, keepdims=True)
    log_total = row_top + jnp.log(jnp.sum(jnp.exp(scores - row_top), axis=-1, keepdims=True))
    attn_probs = jnp.exp(scores - log_total)
    probs_low = attn_probs.astype(jnp.bfloat16)
    mixed_rows = (
        jnp.einsum(
            "ihst,ithd->ishd",
            probs_low,
            values_part,
            preferred_element_type=jnp.float32,
        )
        .reshape(rows, width)
        .astype(jnp.bfloat16)
    )
    hidden_state = token_f + jnp.dot(mixed_rows, full_out, preferred_element_type=jnp.float32)
    moe_in = layer_norm(hidden_state, gain_two).astype(jnp.bfloat16)
    logits = jnp.dot(moe_in, full_router, preferred_element_type=jnp.float32)
    router_probs = normalize_rows(logits)
    expert_ids = jnp.arange(experts, dtype=jnp.int32)
    choose = (routes[:, :, None] == expert_ids).astype(jnp.float32)
    chosen = jnp.sum(choose * router_probs[:, None, :], axis=2)
    pick_table = (routes[:, :, None] == expert_ids).astype(jnp.int32) * live_int[:, None, None]
    flat_picks = pick_table.reshape(rows * 2, experts)
    before = jnp.cumsum(flat_picks, axis=0) - flat_picks
    slot_index = jnp.sum(before * flat_picks, axis=1).reshape(rows, 2)
    position = jnp.where(live_int[:, None] > 0, routes * capacity + slot_index, overflow)

    slot_ids = jnp.arange(overflow, dtype=jnp.int32)[:, None]
    take_first = (slot_ids == position[None, :, 0]).astype(jnp.bfloat16)
    take_second = (slot_ids == position[None, :, 1]).astype(jnp.bfloat16)

    grad_out = cotangent.astype(jnp.float32) * live_rows[:, None]
    weighted = chosen * live_rows[:, None]
    grad_picked = (weighted[:, :, None] * grad_out[:, None, :]).astype(jnp.bfloat16)

    sent_rows = jnp.dot(
        take_first + take_second, moe_in, preferred_element_type=jnp.float32
    ).astype(jnp.bfloat16)
    sent_grad = (
        jnp.dot(take_first, grad_picked[:, 0], preferred_element_type=jnp.float32)
        + jnp.dot(take_second, grad_picked[:, 1], preferred_element_type=jnp.float32)
    ).astype(jnp.bfloat16)
    outgoing = jnp.concatenate([sent_rows, sent_grad], axis=1).reshape(
        experts, capacity, 2 * width
    )
    arrived = lax.all_to_all(outgoing, "expert", split_axis=0, concat_axis=0, tiled=True)
    arrived = arrived.reshape(overflow, 2 * width)
    flat_arrived = arrived[:, :width]
    flat_grad = arrived[:, width:]

    pre_act = jnp.dot(flat_arrived, expert_first, preferred_element_type=jnp.float32)
    activated, gelu_back = jax.vjp(gelu_exact, pre_act)
    activated = activated.astype(jnp.bfloat16)
    produced = jnp.dot(activated, expert_second, preferred_element_type=jnp.float32).astype(
        jnp.bfloat16
    )
    hidden_grad = lax.dot_general(
        flat_grad, expert_second, COL_CONTRACT, preferred_element_type=jnp.float32
    )
    pre_grad = gelu_back(hidden_grad)[0].astype(jnp.bfloat16)
    row_grad = lax.dot_general(
        pre_grad, expert_first, COL_CONTRACT, preferred_element_type=jnp.float32
    ).astype(jnp.bfloat16)
    grad_second = lax.dot_general(
        activated, flat_grad, ROW_CONTRACT, preferred_element_type=jnp.float32
    )
    grad_first = lax.dot_general(
        flat_arrived, pre_grad, ROW_CONTRACT, preferred_element_type=jnp.float32
    )
    expert_grads = jnp.stack(
        [grad_first, grad_second.reshape(width, ff)], axis=0
    ).astype(jnp.bfloat16)
    expert_share = lax.psum_scatter(
        expert_grads, "shard", scatter_dimension=1, tiled=True
    ).astype(jnp.float32)
    grad_in_share = expert_share[0][None]
    grad_back_share = expert_share[1].reshape(back_rows, width)[None]

    returning = jnp.concatenate([produced, row_grad], axis=1).reshape(
        experts, capacity, 2 * width
    )
    returned = lax.all_to_all(returning, "expert", split_axis=0, concat_axis=0, tiled=True)
    returned = returned.reshape(overflow, 2 * width)
    picked_first = lax.dot_general(
        take_first, returned, ROW_CONTRACT, preferred_element_type=jnp.float32
    )
    picked_second = lax.dot_general(
        take_second, returned, ROW_CONTRACT, preferred_element_type=jnp.float32
    )
    moe_out = (
        weighted[:, 0:1] * picked_first[:, :width] + weighted[:, 1:2] * picked_second[:, :width]
    )
    output = (live_rows[:, None] * (hidden_state + moe_out)).astype(jnp.bfloat16)
    grad_chosen = jnp.stack(
        [
            jnp.sum(grad_out * picked_first[:, :width], axis=1),
            jnp.sum(grad_out * picked_second[:, :width], axis=1),
        ],
        axis=1,
    ) * live_rows[:, None]
    expert_part = (picked_first[:, width:] + picked_second[:, width:]) * live_rows[:, None]
    prob_sum = jnp.sum(choose * grad_chosen[:, :, None], axis=1)
    logit_grad = (
        router_probs * (prob_sum - jnp.sum(router_probs * prob_sum, axis=-1, keepdims=True))
    ).astype(jnp.bfloat16)
    grad_router = lax.dot_general(
        moe_in, logit_grad, ROW_CONTRACT, preferred_element_type=jnp.float32
    )
    moe_in_grad = expert_part + lax.dot_general(
        logit_grad, full_router, COL_CONTRACT, preferred_element_type=jnp.float32
    )
    norm_value, norm_back = jax.vjp(layer_norm, hidden_state, gain_two)
    state_part, grad_gain_two = norm_back(moe_in_grad)
    state_grad = grad_out + state_part
    branch_grad = state_grad.astype(jnp.bfloat16)
    grad_wout = lax.dot_general(
        mixed_rows, branch_grad, ROW_CONTRACT, preferred_element_type=jnp.float32
    )
    mixed_grad = lax.dot_general(
        branch_grad, full_out, COL_CONTRACT, preferred_element_type=jnp.float32
    )
    mixed_grad = mixed_grad.astype(jnp.bfloat16).reshape(images, SEQ, H, HD)
    grad_values = jnp.einsum(
        "ihst,ishd->ithd",
        probs_low,
        mixed_grad,
        preferred_element_type=jnp.float32,
    )
    prob_grad = jnp.einsum(
        "ishd,ithd->ihst", mixed_grad, values_part, preferred_element_type=jnp.float32
    )
    score_grad = (
        attn_probs * (prob_grad - jnp.sum(attn_probs * prob_grad, axis=-1, keepdims=True))
    ).astype(jnp.bfloat16)
    grad_queries = (
        jnp.einsum("ihst,ithd->ishd", score_grad, keys_part, preferred_element_type=jnp.float32)
        * score_scale
    )
    grad_keys = (
        jnp.einsum("ihst,ishd->ithd", score_grad, queries, preferred_element_type=jnp.float32)
        * score_scale
    )
    projected_grad = (
        jnp.stack([grad_queries, grad_keys, grad_values], axis=2)
        .reshape(rows, 3 * width)
        .astype(jnp.bfloat16)
    )
    grad_qkv = lax.dot_general(
        attn_in, projected_grad, ROW_CONTRACT, preferred_element_type=jnp.float32
    )
    attn_in_grad = lax.dot_general(
        projected_grad, full_qkv, COL_CONTRACT, preferred_element_type=jnp.float32
    )
    first_value, first_back = jax.vjp(layer_norm, token_f, gain_one)
    token_part, grad_gain_one = first_back(attn_in_grad)
    grad_tokens = (state_grad + token_part).astype(jnp.bfloat16)

    dense_grads = jnp.concatenate(
        [grad_qkv, grad_wout, grad_router, grad_gain_one[:, None], grad_gain_two[:, None]],
        axis=1,
    ).astype(jnp.bfloat16)
    dense_share = lax.psum_scatter(dense_grads, "shard", scatter_dimension=0, tiled=True)
    dense_total = lax.psum(dense_share, "expert").astype(jnp.float32)
    return (
        output,
        grad_tokens,
        dense_total[:, :qkv_cols],
        dense_total[:, qkv_cols : qkv_cols + width],
        dense_total[:, qkv_cols + width : qkv_cols + width + n_route],
        dense_total[:, -2],
        dense_total[:, -1],
        grad_in_share,
        grad_back_share,
    )


def solution(mesh):
    return jax.shard_map(
        shards,
        mesh=mesh,
        in_specs=(
            P(("expert", "shard"), None),
            P("expert", "shard"),
            P(("expert", "shard"), None),
            P("shard", None),
            P("shard", None),
            P("shard", None),
            P("shard"),
            P("shard"),
            P("expert", "shard", None),
            P("expert", "shard", None),
            P(("expert", "shard"), None),
        ),
        out_specs=(
            P(("expert", "shard"), None),
            P(("expert", "shard"), None),
            P("shard", None),
            P("shard", None),
            P("shard", None),
            P("shard"),
            P("shard"),
            P("expert", "shard", None),
            P("expert", "shard", None),
        ),
        check_vma=False,
    )
```

```python
import jax
import jax.numpy as jnp
from jax import lax
from jax.sharding import PartitionSpec as P

H = 12
HD = 64
SEQ = 197


EPSILON = 1e-06
ROW_CONTRACT = (((0,), (0,)), ((), ()))
COL_CONTRACT = (((1,), (1,)), ((), ()))


def layer_norm(values, norm_gain):
    row_mean = jnp.mean(values, axis=-1, keepdims=True)
    centered = values - row_mean
    variance = jnp.mean(centered * centered, axis=-1, keepdims=True)
    return centered * lax.rsqrt(variance + EPSILON) * norm_gain


def normalize_rows(scores):
    row_top = jnp.max(scores, axis=-1, keepdims=True)
    exp_scores = jnp.exp(scores - row_top)
    return exp_scores / jnp.sum(exp_scores, axis=-1, keepdims=True)


def gelu_exact(values):
    return jax.nn.gelu(values, approximate=False)


def shards(
    tokens,
    image_counts,
    routes,
    w_qkv,
    w_out,
    w_router,
    gain_attn,
    gain_moe,
    w_in,
    w_back,
    cotangent,
):
    rows, width = tokens.shape
    experts = lax.axis_size("expert")
    capacity = 8 * (5 * rows // (16 * experts)) + 8
    overflow = experts * capacity
    images = rows // SEQ
    qkv_cols = w_qkv.shape[1]
    n_route = w_router.shape[1]
    ff = w_in.shape[2]
    score_scale = HD ** (-0.5)
    row_ids = jnp.arange(rows, dtype=jnp.int32)
    live_int = (row_ids // SEQ < image_counts[0, 0]).astype(jnp.int32)
    live_rows = live_int.astype(jnp.float32)

    dense_local = jnp.concatenate(
        [w_qkv, w_out, w_router, gain_attn[:, None], gain_moe[:, None]], axis=1
    )
    dense_full = lax.all_gather(dense_local, "shard", axis=0, tiled=True)
    full_qkv = dense_full[:, :qkv_cols]
    full_out = dense_full[:, qkv_cols : qkv_cols + width]
    full_router = dense_full[:, qkv_cols + width : qkv_cols + width + n_route]
    gain_one = dense_full[:, -2].astype(jnp.float32)
    gain_two = dense_full[:, -1].astype(jnp.float32)

    back_rows = w_back.shape[1]
    expert_local = jnp.stack(
        [w_in[0], w_back[0].reshape(back_rows * width // ff, ff)], axis=0
    )
    expert_full = lax.all_gather(expert_local, "shard", axis=1, tiled=True)
    expert_first = expert_full[0]
    expert_second = expert_full[1].reshape(ff, width)

    token_f = tokens.astype(jnp.float32)
    attn_in = layer_norm(token_f, gain_one).astype(jnp.bfloat16)
    projected = jnp.dot(attn_in, full_qkv, preferred_element_type=jnp.float32).astype(jnp.bfloat16)
    split_heads = projected.reshape(images, SEQ, 3, H, HD)
    queries = split_heads[:, :, 0]
    keys_part = split_heads[:, :, 1]
    values_part = split_heads[:, :, 2]
    scores = (
        jnp.einsum("ishd,ithd->ihst", queries, keys_part, preferred_element_type=jnp.float32)
        * score_scale
    )
    row_top = jnp.max(scores, axis=-1, keepdims=True)
    log_total = row_top + jnp.log(jnp.sum(jnp.exp(scores - row_top), axis=-1, keepdims=True))
    attn_probs = jnp.exp(scores - log_total)
    probs_low = attn_probs.astype(jnp.bfloat16)
    mixed_rows = (
        jnp.einsum(
            "ihst,ithd->ishd",
            probs_low,
            values_part,
            preferred_element_type=jnp.float32,
        )
        .reshape(rows, width)
        .astype(jnp.bfloat16)
    )
    hidden_state = token_f + jnp.dot(mixed_rows, full_out, preferred_element_type=jnp.float32)
    moe_in = layer_norm(hidden_state, gain_two).astype(jnp.bfloat16)
    logits = jnp.dot(moe_in, full_router, preferred_element_type=jnp.float32)
    router_probs = normalize_rows(logits)
    expert_ids = jnp.arange(experts, dtype=jnp.int32)
    choose = (routes[:, :, None] == expert_ids).astype(jnp.float32)
    chosen = jnp.sum(choose * router_probs[:, None, :], axis=2)
    pick_table = (routes[:, :, None] == expert_ids).astype(jnp.int32) * live_int[:, None, None]
    flat_picks = pick_table.reshape(rows * 2, experts)
    before = jnp.cumsum(flat_picks, axis=0) - flat_picks
    slot_index = jnp.sum(before * flat_picks, axis=1).reshape(rows, 2)
    position = jnp.where(live_int[:, None] > 0, routes * capacity + slot_index, overflow)

    half_cap = 8 * ((capacity + 15) // 16)
    chunk_sizes = [half_cap, capacity - half_cap] if capacity > half_cap else [capacity]
    chunk_starts = [sum(chunk_sizes[:k]) for k in range(len(chunk_sizes))]
    slot_ids = jnp.concatenate(
        [
            (
                jnp.arange(experts, dtype=jnp.int32)[:, None] * capacity
                + start
                + jnp.arange(size, dtype=jnp.int32)[None, :]
            ).reshape(-1)
            for start, size in zip(chunk_starts, chunk_sizes)
        ]
    )[:, None]
    take_first = (slot_ids == position[None, :, 0]).astype(jnp.bfloat16)
    take_second = (slot_ids == position[None, :, 1]).astype(jnp.bfloat16)

    grad_out = cotangent.astype(jnp.float32) * live_rows[:, None]
    weighted = chosen * live_rows[:, None]
    grad_picked = (weighted[:, :, None] * grad_out[:, None, :]).astype(jnp.bfloat16)

    sent_rows = jnp.dot(
        take_first + take_second, moe_in, preferred_element_type=jnp.float32
    ).astype(jnp.bfloat16)
    sent_grad = (
        jnp.dot(take_first, grad_picked[:, 0], preferred_element_type=jnp.float32)
        + jnp.dot(take_second, grad_picked[:, 1], preferred_element_type=jnp.float32)
    ).astype(jnp.bfloat16)
    outgoing = jnp.concatenate([sent_rows, sent_grad], axis=1)

    grad_first = None
    grad_second = None
    returned_parts = []
    for start, size in zip(chunk_starts, chunk_sizes):
        arrived = lax.all_to_all(
            outgoing[experts * start : experts * (start + size)].reshape(
                experts, size, 2 * width
            ),
            "expert",
            split_axis=0,
            concat_axis=0,
            tiled=True,
        ).reshape(experts * size, 2 * width)
        flat_arrived = arrived[:, :width]
        flat_grad = arrived[:, width:]
        pre_act = jnp.dot(flat_arrived, expert_first, preferred_element_type=jnp.float32)
        activated, gelu_back = jax.vjp(gelu_exact, pre_act)
        activated = activated.astype(jnp.bfloat16)
        produced = jnp.dot(
            activated, expert_second, preferred_element_type=jnp.float32
        ).astype(jnp.bfloat16)
        hidden_grad = lax.dot_general(
            flat_grad, expert_second, COL_CONTRACT, preferred_element_type=jnp.float32
        )
        pre_grad = gelu_back(hidden_grad)[0].astype(jnp.bfloat16)
        row_grad = lax.dot_general(
            pre_grad, expert_first, COL_CONTRACT, preferred_element_type=jnp.float32
        ).astype(jnp.bfloat16)
        part_second = lax.dot_general(
            activated, flat_grad, ROW_CONTRACT, preferred_element_type=jnp.float32
        )
        part_first = lax.dot_general(
            flat_arrived, pre_grad, ROW_CONTRACT, preferred_element_type=jnp.float32
        )
        grad_first = part_first if grad_first is None else grad_first + part_first
        grad_second = part_second if grad_second is None else grad_second + part_second
        returning = jnp.concatenate([produced, row_grad], axis=1).reshape(
            experts, size, 2 * width
        )
        returned_parts.append(
            lax.all_to_all(returning, "expert", split_axis=0, concat_axis=0, tiled=True)
        )

    expert_grads = jnp.stack(
        [grad_first, grad_second.reshape(width, ff)], axis=0
    ).astype(jnp.bfloat16)
    expert_share = lax.psum_scatter(
        expert_grads, "shard", scatter_dimension=1, tiled=True
    ).astype(jnp.float32)
    grad_in_share = expert_share[0][None]
    grad_back_share = expert_share[1].reshape(back_rows, width)[None]

    returned = jnp.concatenate(
        [part.reshape(-1, 2 * width) for part in returned_parts], axis=0
    )
    picked_first = lax.dot_general(
        take_first, returned, ROW_CONTRACT, preferred_element_type=jnp.float32
    )
    picked_second = lax.dot_general(
        take_second, returned, ROW_CONTRACT, preferred_element_type=jnp.float32
    )
    moe_out = (
        weighted[:, 0:1] * picked_first[:, :width] + weighted[:, 1:2] * picked_second[:, :width]
    )
    output = (live_rows[:, None] * (hidden_state + moe_out)).astype(jnp.bfloat16)
    grad_chosen = jnp.stack(
        [
            jnp.sum(grad_out * picked_first[:, :width], axis=1),
            jnp.sum(grad_out * picked_second[:, :width], axis=1),
        ],
        axis=1,
    ) * live_rows[:, None]
    expert_part = (picked_first[:, width:] + picked_second[:, width:]) * live_rows[:, None]
    prob_sum = jnp.sum(choose * grad_chosen[:, :, None], axis=1)
    logit_grad = (
        router_probs * (prob_sum - jnp.sum(router_probs * prob_sum, axis=-1, keepdims=True))
    ).astype(jnp.bfloat16)
    grad_router = lax.dot_general(
        moe_in, logit_grad, ROW_CONTRACT, preferred_element_type=jnp.float32
    )
    moe_in_grad = expert_part + lax.dot_general(
        logit_grad, full_router, COL_CONTRACT, preferred_element_type=jnp.float32
    )
    norm_value, norm_back = jax.vjp(layer_norm, hidden_state, gain_two)
    state_part, grad_gain_two = norm_back(moe_in_grad)
    state_grad = grad_out + state_part
    branch_grad = state_grad.astype(jnp.bfloat16)
    grad_wout = lax.dot_general(
        mixed_rows, branch_grad, ROW_CONTRACT, preferred_element_type=jnp.float32
    )
    mixed_grad = lax.dot_general(
        branch_grad, full_out, COL_CONTRACT, preferred_element_type=jnp.float32
    )
    mixed_grad = mixed_grad.astype(jnp.bfloat16).reshape(images, SEQ, H, HD)
    grad_values = jnp.einsum(
        "ihst,ishd->ithd",
        probs_low,
        mixed_grad,
        preferred_element_type=jnp.float32,
    )
    prob_grad = jnp.einsum(
        "ishd,ithd->ihst", mixed_grad, values_part, preferred_element_type=jnp.float32
    )
    score_grad = (
        attn_probs * (prob_grad - jnp.sum(attn_probs * prob_grad, axis=-1, keepdims=True))
    ).astype(jnp.bfloat16)
    grad_queries = (
        jnp.einsum("ihst,ithd->ishd", score_grad, keys_part, preferred_element_type=jnp.float32)
        * score_scale
    )
    grad_keys = (
        jnp.einsum("ihst,ishd->ithd", score_grad, queries, preferred_element_type=jnp.float32)
        * score_scale
    )
    projected_grad = (
        jnp.stack([grad_queries, grad_keys, grad_values], axis=2)
        .reshape(rows, 3 * width)
        .astype(jnp.bfloat16)
    )
    grad_qkv = lax.dot_general(
        attn_in, projected_grad, ROW_CONTRACT, preferred_element_type=jnp.float32
    )
    attn_in_grad = lax.dot_general(
        projected_grad, full_qkv, COL_CONTRACT, preferred_element_type=jnp.float32
    )
    first_value, first_back = jax.vjp(layer_norm, token_f, gain_one)
    token_part, grad_gain_one = first_back(attn_in_grad)
    grad_tokens = (state_grad + token_part).astype(jnp.bfloat16)

    dense_grads = jnp.concatenate(
        [grad_qkv, grad_wout, grad_router, grad_gain_one[:, None], grad_gain_two[:, None]],
        axis=1,
    ).astype(jnp.bfloat16)
    dense_share = lax.psum_scatter(dense_grads, "shard", scatter_dimension=0, tiled=True)
    dense_total = lax.psum(dense_share, "expert").astype(jnp.float32)
    return (
        output,
        grad_tokens,
        dense_total[:, :qkv_cols],
        dense_total[:, qkv_cols : qkv_cols + width],
        dense_total[:, qkv_cols + width : qkv_cols + width + n_route],
        dense_total[:, -2],
        dense_total[:, -1],
        grad_in_share,
        grad_back_share,
    )


def solution(mesh):
    return jax.shard_map(
        shards,
        mesh=mesh,
        in_specs=(
            P(("expert", "shard"), None),
            P("expert", "shard"),
            P(("expert", "shard"), None),
            P("shard", None),
            P("shard", None),
            P("shard", None),
            P("shard"),
            P("shard"),
            P("expert", "shard", None),
            P("expert", "shard", None),
            P(("expert", "shard"), None),
        ),
        out_specs=(
            P(("expert", "shard"), None),
            P(("expert", "shard"), None),
            P("shard", None),
            P("shard", None),
            P("shard", None),
            P("shard"),
            P("shard"),
            P("expert", "shard", None),
            P("expert", "shard", None),
        ),
        check_vma=False,
    )
```

```python
import jax
import jax.numpy as jnp
from jax import lax
from jax.sharding import PartitionSpec as P

H = 12
HD = 64
SEQ = 197


EPSILON = 1e-06
ROW_CONTRACT = (((0,), (0,)), ((), ()))
COL_CONTRACT = (((1,), (1,)), ((), ()))


def layer_norm(values, norm_gain):
    row_mean = jnp.mean(values, axis=-1, keepdims=True)
    centered = values - row_mean
    variance = jnp.mean(centered * centered, axis=-1, keepdims=True)
    return centered * lax.rsqrt(variance + EPSILON) * norm_gain


def normalize_rows(scores):
    row_top = jnp.max(scores, axis=-1, keepdims=True)
    exp_scores = jnp.exp(scores - row_top)
    return exp_scores / jnp.sum(exp_scores, axis=-1, keepdims=True)


def gelu_exact(values):
    return jax.nn.gelu(values, approximate=False)


def shards(
    tokens,
    image_counts,
    routes,
    w_qkv,
    w_out,
    w_router,
    gain_attn,
    gain_moe,
    w_in,
    w_back,
    cotangent,
):
    rows, width = tokens.shape
    experts = lax.axis_size("expert")
    capacity = 8 * (5 * rows // (16 * experts)) + 8
    overflow = experts * capacity
    images = rows // SEQ
    qkv_cols = w_qkv.shape[1]
    n_route = w_router.shape[1]
    ff = w_in.shape[2]
    score_scale = HD ** (-0.5)
    row_ids = jnp.arange(rows, dtype=jnp.int32)
    live_int = (row_ids // SEQ < image_counts[0, 0]).astype(jnp.int32)
    live_rows = live_int.astype(jnp.float32)

    dense_local = jnp.concatenate(
        [w_qkv, w_out, w_router, gain_attn[:, None], gain_moe[:, None]], axis=1
    )
    dense_full = lax.all_gather(dense_local, "shard", axis=0, tiled=True)
    full_qkv = dense_full[:, :qkv_cols]
    full_out = dense_full[:, qkv_cols : qkv_cols + width]
    full_router = dense_full[:, qkv_cols + width : qkv_cols + width + n_route]
    gain_one = dense_full[:, -2].astype(jnp.float32)
    gain_two = dense_full[:, -1].astype(jnp.float32)

    back_rows = w_back.shape[1]
    expert_local = jnp.stack(
        [w_in[0], w_back[0].reshape(back_rows * width // ff, ff)], axis=0
    )
    expert_full = lax.all_gather(expert_local, "shard", axis=1, tiled=True)
    expert_first = expert_full[0]
    expert_second = expert_full[1].reshape(ff, width)

    token_f = tokens.astype(jnp.float32)
    attn_in = layer_norm(token_f, gain_one).astype(jnp.bfloat16)
    projected = jnp.dot(attn_in, full_qkv, preferred_element_type=jnp.float32).astype(jnp.bfloat16)
    split_heads = projected.reshape(images, SEQ, 3, H, HD)
    queries = split_heads[:, :, 0]
    keys_part = split_heads[:, :, 1]
    values_part = split_heads[:, :, 2]
    scores = (
        jnp.einsum("ishd,ithd->ihst", queries, keys_part, preferred_element_type=jnp.float32)
        * score_scale
    )
    row_top = jnp.max(scores, axis=-1, keepdims=True)
    log_total = row_top + jnp.log(jnp.sum(jnp.exp(scores - row_top), axis=-1, keepdims=True))
    attn_probs = jnp.exp(scores - log_total)
    probs_low = attn_probs.astype(jnp.bfloat16)
    mixed_rows = (
        jnp.einsum(
            "ihst,ithd->ishd",
            probs_low,
            values_part,
            preferred_element_type=jnp.float32,
        )
        .reshape(rows, width)
        .astype(jnp.bfloat16)
    )
    hidden_state = token_f + jnp.dot(mixed_rows, full_out, preferred_element_type=jnp.float32)
    moe_in = layer_norm(hidden_state, gain_two).astype(jnp.bfloat16)
    logits = jnp.dot(moe_in, full_router, preferred_element_type=jnp.float32)
    router_probs = normalize_rows(logits)
    expert_ids = jnp.arange(experts, dtype=jnp.int32)
    choose = (routes[:, :, None] == expert_ids).astype(jnp.float32)
    chosen = jnp.sum(choose * router_probs[:, None, :], axis=2)
    pick_table = (routes[:, :, None] == expert_ids).astype(jnp.int32) * live_int[:, None, None]
    flat_picks = pick_table.reshape(rows * 2, experts)
    before = jnp.cumsum(flat_picks, axis=0) - flat_picks
    slot_index = jnp.sum(before * flat_picks, axis=1).reshape(rows, 2)
    position = jnp.where(live_int[:, None] > 0, routes * capacity + slot_index, overflow)

    half_cap = 8 * ((capacity + 15) // 16)
    chunk_sizes = [half_cap, capacity - half_cap] if capacity > half_cap else [capacity]
    chunk_starts = [sum(chunk_sizes[:k]) for k in range(len(chunk_sizes))]
    slot_ids = jnp.concatenate(
        [
            (
                jnp.arange(experts, dtype=jnp.int32)[:, None] * capacity
                + start
                + jnp.arange(size, dtype=jnp.int32)[None, :]
            ).reshape(-1)
            for start, size in zip(chunk_starts, chunk_sizes)
        ]
    )[:, None]
    take_first = (slot_ids == position[None, :, 0]).astype(jnp.bfloat16)
    take_second = (slot_ids == position[None, :, 1]).astype(jnp.bfloat16)

    grad_out = cotangent.astype(jnp.float32) * live_rows[:, None]
    weighted = chosen * live_rows[:, None]
    grad_picked = (weighted[:, :, None] * grad_out[:, None, :]).astype(jnp.bfloat16)

    sent_rows = jnp.dot(
        take_first + take_second, moe_in, preferred_element_type=jnp.float32
    ).astype(jnp.bfloat16)
    sent_grad = (
        jnp.dot(take_first, grad_picked[:, 0], preferred_element_type=jnp.float32)
        + jnp.dot(take_second, grad_picked[:, 1], preferred_element_type=jnp.float32)
    ).astype(jnp.bfloat16)
    outgoing = jnp.concatenate([sent_rows, sent_grad], axis=1)

    grad_first = None
    grad_second = None
    returned_parts = []
    for start, size in zip(chunk_starts, chunk_sizes):
        arrived = lax.all_to_all(
            outgoing[experts * start : experts * (start + size)].reshape(
                experts, size, 2 * width
            ),
            "expert",
            split_axis=0,
            concat_axis=0,
            tiled=True,
        ).reshape(experts * size, 2 * width)
        flat_arrived = arrived[:, :width]
        flat_grad = arrived[:, width:]
        pre_act = jnp.dot(flat_arrived, expert_first, preferred_element_type=jnp.float32)
        activated, gelu_back = jax.vjp(gelu_exact, pre_act)
        activated = activated.astype(jnp.bfloat16)
        produced = jnp.dot(
            activated, expert_second, preferred_element_type=jnp.float32
        ).astype(jnp.bfloat16)
        hidden_grad = lax.dot_general(
            flat_grad, expert_second, COL_CONTRACT, preferred_element_type=jnp.float32
        )
        pre_grad = gelu_back(hidden_grad)[0].astype(jnp.bfloat16)
        row_grad = lax.dot_general(
            pre_grad, expert_first, COL_CONTRACT, preferred_element_type=jnp.float32
        ).astype(jnp.bfloat16)
        part_second = lax.dot_general(
            activated, flat_grad, ROW_CONTRACT, preferred_element_type=jnp.float32
        )
        part_first = lax.dot_general(
            flat_arrived, pre_grad, ROW_CONTRACT, preferred_element_type=jnp.float32
        )
        grad_first = part_first if grad_first is None else grad_first + part_first
        grad_second = part_second if grad_second is None else grad_second + part_second
        returning = jnp.concatenate([produced, row_grad], axis=1).reshape(
            experts, size, 2 * width
        )
        returned_parts.append(
            lax.all_to_all(returning, "expert", split_axis=0, concat_axis=0, tiled=True)
        )

    expert_grads = jnp.stack(
        [grad_first, grad_second.reshape(width, ff)], axis=0
    ).astype(jnp.bfloat16)
    expert_share = lax.psum_scatter(expert_grads, "shard", scatter_dimension=1, tiled=True)
    expert_share = expert_share.astype(jnp.float32)
    grad_in_share = expert_share[0][None]
    grad_back_share = expert_share[1].reshape(back_rows, width)[None]

    returned = jnp.concatenate(
        [part.reshape(-1, 2 * width) for part in returned_parts], axis=0
    )
    picked_first = lax.dot_general(
        take_first, returned, ROW_CONTRACT, preferred_element_type=jnp.float32
    )
    picked_second = lax.dot_general(
        take_second, returned, ROW_CONTRACT, preferred_element_type=jnp.float32
    )
    moe_out = (
        weighted[:, 0:1] * picked_first[:, :width] + weighted[:, 1:2] * picked_second[:, :width]
    )
    output = (live_rows[:, None] * (hidden_state + moe_out)).astype(jnp.bfloat16)
    grad_chosen = jnp.stack(
        [
            jnp.sum(grad_out * picked_first[:, :width], axis=1),
            jnp.sum(grad_out * picked_second[:, :width], axis=1),
        ],
        axis=1,
    ) * live_rows[:, None]
    expert_part = (picked_first[:, width:] + picked_second[:, width:]) * live_rows[:, None]
    prob_sum = jnp.sum(choose * grad_chosen[:, :, None], axis=1)
    logit_grad = (
        router_probs * (prob_sum - jnp.sum(router_probs * prob_sum, axis=-1, keepdims=True))
    ).astype(jnp.bfloat16)
    grad_router = lax.dot_general(
        moe_in, logit_grad, ROW_CONTRACT, preferred_element_type=jnp.float32
    )
    moe_in_grad = expert_part + lax.dot_general(
        logit_grad, full_router, COL_CONTRACT, preferred_element_type=jnp.float32
    )
    _, norm_back = jax.vjp(layer_norm, hidden_state, gain_two)
    state_part, grad_gain_two = norm_back(moe_in_grad)
    state_grad = grad_out + state_part
    branch_grad = state_grad.astype(jnp.bfloat16)
    grad_wout = lax.dot_general(
        mixed_rows, branch_grad, ROW_CONTRACT, preferred_element_type=jnp.float32
    )
    mixed_grad = lax.dot_general(
        branch_grad, full_out, COL_CONTRACT, preferred_element_type=jnp.float32
    )
    mixed_grad = mixed_grad.astype(jnp.bfloat16).reshape(images, SEQ, H, HD)
    grad_values = jnp.einsum(
        "ihst,ishd->ithd",
        probs_low,
        mixed_grad,
        preferred_element_type=jnp.float32,
    )
    prob_grad = jnp.einsum(
        "ishd,ithd->ihst", mixed_grad, values_part, preferred_element_type=jnp.float32
    )
    score_grad = (
        attn_probs * (prob_grad - jnp.sum(attn_probs * prob_grad, axis=-1, keepdims=True))
    ).astype(jnp.bfloat16)
    grad_queries = (
        jnp.einsum("ihst,ithd->ishd", score_grad, keys_part, preferred_element_type=jnp.float32)
        * score_scale
    )
    grad_keys = (
        jnp.einsum("ihst,ishd->ithd", score_grad, queries, preferred_element_type=jnp.float32)
        * score_scale
    )
    projected_grad = (
        jnp.stack([grad_queries, grad_keys, grad_values], axis=2)
        .reshape(rows, 3 * width)
        .astype(jnp.bfloat16)
    )
    grad_qkv = lax.dot_general(
        attn_in, projected_grad, ROW_CONTRACT, preferred_element_type=jnp.float32
    )
    attn_in_grad = lax.dot_general(
        projected_grad, full_qkv, COL_CONTRACT, preferred_element_type=jnp.float32
    )
    _, first_back = jax.vjp(layer_norm, token_f, gain_one)
    token_part, grad_gain_one = first_back(attn_in_grad)
    grad_tokens = (state_grad + token_part).astype(jnp.bfloat16)

    dense_grads = jnp.concatenate(
        [grad_qkv, grad_wout, grad_router, grad_gain_one[:, None], grad_gain_two[:, None]],
        axis=1,
    ).astype(jnp.bfloat16)
    dense_share = lax.psum_scatter(dense_grads, "shard", scatter_dimension=0, tiled=True)
    dense_total = lax.psum(dense_share, "expert").astype(jnp.float32)
    return (
        output,
        grad_tokens,
        dense_total[:, :qkv_cols],
        dense_total[:, qkv_cols : qkv_cols + width],
        dense_total[:, qkv_cols + width : qkv_cols + width + n_route],
        dense_total[:, -2],
        dense_total[:, -1],
        grad_in_share,
        grad_back_share,
    )


def solution(mesh):
    return _mapped(mesh)


def _mapped(mesh):
    return jax.shard_map(
        shards,
        mesh=mesh,
        in_specs=(
            P(("expert", "shard"), None),
            P("expert", "shard"),
            P(("expert", "shard"), None),
            P("shard", None),
            P("shard", None),
            P("shard", None),
            P("shard"),
            P("shard"),
            P("expert", "shard", None),
            P("expert", "shard", None),
            P(("expert", "shard"), None),
        ),
        out_specs=(
            P(("expert", "shard"), None),
            P(("expert", "shard"), None),
            P("shard", None),
            P("shard", None),
            P("shard", None),
            P("shard"),
            P("shard"),
            P("expert", "shard", None),
            P("expert", "shard", None),
        ),
        check_vma=False,
    )
```

```python
import jax
import jax.numpy as jnp
from jax import lax
from jax.sharding import PartitionSpec as P

H = 12
HD = 64
SEQ = 197


EPSILON = 1e-06
ROW_CONTRACT = (((0,), (0,)), ((), ()))
COL_CONTRACT = (((1,), (1,)), ((), ()))


def layer_norm(values, norm_gain):
    row_mean = jnp.mean(values, axis=-1, keepdims=True)
    centered = values - row_mean
    variance = jnp.mean(centered * centered, axis=-1, keepdims=True)
    return centered * lax.rsqrt(variance + EPSILON) * norm_gain


def normalize_rows(scores):
    row_top = jnp.max(scores, axis=-1, keepdims=True)
    exp_scores = jnp.exp(scores - row_top)
    return exp_scores / jnp.sum(exp_scores, axis=-1, keepdims=True)


def gelu_exact(values):
    return jax.nn.gelu(values, approximate=False)


def shards(
    tokens,
    image_counts,
    routes,
    w_qkv,
    w_out,
    w_router,
    gain_attn,
    gain_moe,
    w_in,
    w_back,
    cotangent,
):
    rows, width = tokens.shape
    experts = lax.axis_size("expert")
    capacity = 8 * (5 * rows // (16 * experts)) + 8
    overflow = experts * capacity
    images = rows // SEQ
    qkv_cols = w_qkv.shape[1]
    n_route = w_router.shape[1]
    ff = w_in.shape[2]
    score_scale = HD ** (-0.5)
    row_ids = jnp.arange(rows, dtype=jnp.int32)
    live_int = (row_ids // SEQ < image_counts[0, 0]).astype(jnp.int32)
    live_rows = live_int.astype(jnp.float32)

    dense_local = jnp.concatenate(
        [w_qkv, w_out, w_router, gain_attn[:, None], gain_moe[:, None]], axis=1
    )
    dense_full = lax.all_gather(dense_local, "shard", axis=0, tiled=True)
    full_qkv = dense_full[:, :qkv_cols]
    full_out = dense_full[:, qkv_cols : qkv_cols + width]
    full_router = dense_full[:, qkv_cols + width : qkv_cols + width + n_route]
    gain_one = dense_full[:, -2].astype(jnp.float32)
    gain_two = dense_full[:, -1].astype(jnp.float32)

    back_rows = w_back.shape[1]
    expert_local = jnp.stack(
        [w_in[0], w_back[0].reshape(back_rows * width // ff, ff)], axis=0
    )
    expert_full = lax.all_gather(expert_local, "shard", axis=1, tiled=True)
    expert_first = expert_full[0]
    expert_second = expert_full[1].reshape(ff, width)

    token_f = tokens.astype(jnp.float32)
    attn_in = layer_norm(token_f, gain_one).astype(jnp.bfloat16)
    projected = jnp.dot(attn_in, full_qkv, preferred_element_type=jnp.float32).astype(jnp.bfloat16)
    split_heads = projected.reshape(images, SEQ, 3, H, HD)
    queries = split_heads[:, :, 0]
    keys_part = split_heads[:, :, 1]
    values_part = split_heads[:, :, 2]
    scores = (
        jnp.einsum("ishd,ithd->ihst", queries, keys_part, preferred_element_type=jnp.float32)
        * score_scale
    )
    row_top = jnp.max(scores, axis=-1, keepdims=True)
    log_total = row_top + jnp.log(jnp.sum(jnp.exp(scores - row_top), axis=-1, keepdims=True))
    attn_probs = jnp.exp(scores - log_total)
    probs_low = attn_probs.astype(jnp.bfloat16)
    mixed_rows = (
        jnp.einsum(
            "ihst,ithd->ishd",
            probs_low,
            values_part,
            preferred_element_type=jnp.float32,
        )
        .reshape(rows, width)
        .astype(jnp.bfloat16)
    )
    hidden_state = token_f + jnp.dot(mixed_rows, full_out, preferred_element_type=jnp.float32)
    moe_in = layer_norm(hidden_state, gain_two).astype(jnp.bfloat16)
    logits = jnp.dot(moe_in, full_router, preferred_element_type=jnp.float32)
    router_probs = normalize_rows(logits)
    expert_ids = jnp.arange(experts, dtype=jnp.int32)
    choose = (routes[:, :, None] == expert_ids).astype(jnp.float32)
    chosen = jnp.sum(choose * router_probs[:, None, :], axis=2)
    pick_table = (routes[:, :, None] == expert_ids).astype(jnp.int32) * live_int[:, None, None]
    flat_picks = pick_table.reshape(rows * 2, experts)
    before = jnp.cumsum(flat_picks, axis=0) - flat_picks
    slot_index = jnp.sum(before * flat_picks, axis=1).reshape(rows, 2)
    position = jnp.where(live_int[:, None] > 0, routes * capacity + slot_index, overflow)

    n_chunks = 4
    part_cap = 8 * ((capacity + 8 * n_chunks - 1) // (8 * n_chunks))
    chunk_sizes = [min(part_cap, capacity - k * part_cap) for k in range(n_chunks)]
    chunk_sizes = [size for size in chunk_sizes if size > 0]
    chunk_starts = [sum(chunk_sizes[:k]) for k in range(len(chunk_sizes))]
    slot_ids = jnp.concatenate(
        [
            (
                jnp.arange(experts, dtype=jnp.int32)[:, None] * capacity
                + start
                + jnp.arange(size, dtype=jnp.int32)[None, :]
            ).reshape(-1)
            for start, size in zip(chunk_starts, chunk_sizes)
        ]
    )[:, None]
    take_first = (slot_ids == position[None, :, 0]).astype(jnp.bfloat16)
    take_second = (slot_ids == position[None, :, 1]).astype(jnp.bfloat16)

    grad_out = cotangent.astype(jnp.float32) * live_rows[:, None]
    weighted = chosen * live_rows[:, None]
    grad_picked = (weighted[:, :, None] * grad_out[:, None, :]).astype(jnp.bfloat16)

    sent_rows = jnp.dot(
        take_first + take_second, moe_in, preferred_element_type=jnp.float32
    ).astype(jnp.bfloat16)
    sent_grad = (
        jnp.dot(take_first, grad_picked[:, 0], preferred_element_type=jnp.float32)
        + jnp.dot(take_second, grad_picked[:, 1], preferred_element_type=jnp.float32)
    ).astype(jnp.bfloat16)
    outgoing = jnp.concatenate([sent_rows, sent_grad], axis=1)

    grad_first = None
    grad_second = None
    returned_parts = []
    for start, size in zip(chunk_starts, chunk_sizes):
        arrived = lax.all_to_all(
            outgoing[experts * start : experts * (start + size)].reshape(
                experts, size, 2 * width
            ),
            "expert",
            split_axis=0,
            concat_axis=0,
            tiled=True,
        ).reshape(experts * size, 2 * width)
        flat_arrived = arrived[:, :width]
        flat_grad = arrived[:, width:]
        pre_act = jnp.dot(flat_arrived, expert_first, preferred_element_type=jnp.float32)
        activated, gelu_back = jax.vjp(gelu_exact, pre_act)
        activated = activated.astype(jnp.bfloat16)
        produced = jnp.dot(
            activated, expert_second, preferred_element_type=jnp.float32
        ).astype(jnp.bfloat16)
        hidden_grad = lax.dot_general(
            flat_grad, expert_second, COL_CONTRACT, preferred_element_type=jnp.float32
        )
        pre_grad = gelu_back(hidden_grad)[0].astype(jnp.bfloat16)
        row_grad = lax.dot_general(
            pre_grad, expert_first, COL_CONTRACT, preferred_element_type=jnp.float32
        ).astype(jnp.bfloat16)
        part_second = lax.dot_general(
            activated, flat_grad, ROW_CONTRACT, preferred_element_type=jnp.float32
        )
        part_first = lax.dot_general(
            flat_arrived, pre_grad, ROW_CONTRACT, preferred_element_type=jnp.float32
        )
        grad_first = part_first if grad_first is None else grad_first + part_first
        grad_second = part_second if grad_second is None else grad_second + part_second
        returning = jnp.concatenate([produced, row_grad], axis=1).reshape(
            experts, size, 2 * width
        )
        returned_parts.append(
            lax.all_to_all(returning, "expert", split_axis=0, concat_axis=0, tiled=True)
        )

    expert_grads = jnp.stack(
        [grad_first, grad_second.reshape(width, ff)], axis=0
    ).astype(jnp.bfloat16)
    expert_share = lax.psum_scatter(expert_grads, "shard", scatter_dimension=1, tiled=True)
    expert_share = expert_share.astype(jnp.float32)
    grad_in_share = expert_share[0][None]
    grad_back_share = expert_share[1].reshape(back_rows, width)[None]

    returned = jnp.concatenate(
        [part.reshape(-1, 2 * width) for part in returned_parts], axis=0
    )
    picked_first = lax.dot_general(
        take_first, returned, ROW_CONTRACT, preferred_element_type=jnp.float32
    )
    picked_second = lax.dot_general(
        take_second, returned, ROW_CONTRACT, preferred_element_type=jnp.float32
    )
    moe_out = (
        weighted[:, 0:1] * picked_first[:, :width] + weighted[:, 1:2] * picked_second[:, :width]
    )
    output = (live_rows[:, None] * (hidden_state + moe_out)).astype(jnp.bfloat16)
    grad_chosen = jnp.stack(
        [
            jnp.sum(grad_out * picked_first[:, :width], axis=1),
            jnp.sum(grad_out * picked_second[:, :width], axis=1),
        ],
        axis=1,
    ) * live_rows[:, None]
    expert_part = (picked_first[:, width:] + picked_second[:, width:]) * live_rows[:, None]
    prob_sum = jnp.sum(choose * grad_chosen[:, :, None], axis=1)
    logit_grad = (
        router_probs * (prob_sum - jnp.sum(router_probs * prob_sum, axis=-1, keepdims=True))
    ).astype(jnp.bfloat16)
    grad_router = lax.dot_general(
        moe_in, logit_grad, ROW_CONTRACT, preferred_element_type=jnp.float32
    )
    moe_in_grad = expert_part + lax.dot_general(
        logit_grad, full_router, COL_CONTRACT, preferred_element_type=jnp.float32
    )
    _, norm_back = jax.vjp(layer_norm, hidden_state, gain_two)
    state_part, grad_gain_two = norm_back(moe_in_grad)
    state_grad = grad_out + state_part
    branch_grad = state_grad.astype(jnp.bfloat16)
    grad_wout = lax.dot_general(
        mixed_rows, branch_grad, ROW_CONTRACT, preferred_element_type=jnp.float32
    )
    mixed_grad = lax.dot_general(
        branch_grad, full_out, COL_CONTRACT, preferred_element_type=jnp.float32
    )
    mixed_grad = mixed_grad.astype(jnp.bfloat16).reshape(images, SEQ, H, HD)
    grad_values = jnp.einsum(
        "ihst,ishd->ithd",
        probs_low,
        mixed_grad,
        preferred_element_type=jnp.float32,
    )
    prob_grad = jnp.einsum(
        "ishd,ithd->ihst", mixed_grad, values_part, preferred_element_type=jnp.float32
    )
    score_grad = (
        attn_probs * (prob_grad - jnp.sum(attn_probs * prob_grad, axis=-1, keepdims=True))
    ).astype(jnp.bfloat16)
    grad_queries = (
        jnp.einsum("ihst,ithd->ishd", score_grad, keys_part, preferred_element_type=jnp.float32)
        * score_scale
    )
    grad_keys = (
        jnp.einsum("ihst,ishd->ithd", score_grad, queries, preferred_element_type=jnp.float32)
        * score_scale
    )
    projected_grad = (
        jnp.stack([grad_queries, grad_keys, grad_values], axis=2)
        .reshape(rows, 3 * width)
        .astype(jnp.bfloat16)
    )
    grad_qkv = lax.dot_general(
        attn_in, projected_grad, ROW_CONTRACT, preferred_element_type=jnp.float32
    )
    attn_in_grad = lax.dot_general(
        projected_grad, full_qkv, COL_CONTRACT, preferred_element_type=jnp.float32
    )
    _, first_back = jax.vjp(layer_norm, token_f, gain_one)
    token_part, grad_gain_one = first_back(attn_in_grad)
    grad_tokens = (state_grad + token_part).astype(jnp.bfloat16)

    dense_grads = jnp.concatenate(
        [grad_qkv, grad_wout, grad_router, grad_gain_one[:, None], grad_gain_two[:, None]],
        axis=1,
    ).astype(jnp.bfloat16)
    dense_share = lax.psum_scatter(dense_grads, "shard", scatter_dimension=0, tiled=True)
    dense_total = lax.psum(dense_share, "expert").astype(jnp.float32)
    return (
        output,
        grad_tokens,
        dense_total[:, :qkv_cols],
        dense_total[:, qkv_cols : qkv_cols + width],
        dense_total[:, qkv_cols + width : qkv_cols + width + n_route],
        dense_total[:, -2],
        dense_total[:, -1],
        grad_in_share,
        grad_back_share,
    )


def solution(mesh):
    return _mapped(mesh)


def _mapped(mesh):
    return jax.shard_map(
        shards,
        mesh=mesh,
        in_specs=(
            P(("expert", "shard"), None),
            P("expert", "shard"),
            P(("expert", "shard"), None),
            P("shard", None),
            P("shard", None),
            P("shard", None),
            P("shard"),
            P("shard"),
            P("expert", "shard", None),
            P("expert", "shard", None),
            P(("expert", "shard"), None),
        ),
        out_specs=(
            P(("expert", "shard"), None),
            P(("expert", "shard"), None),
            P("shard", None),
            P("shard", None),
            P("shard", None),
            P("shard"),
            P("shard"),
            P("expert", "shard", None),
            P("expert", "shard", None),
        ),
        check_vma=False,
    )
```

```python
import jax
import numpy as np
import jax.numpy as jnp
from jax import lax
from jax.sharding import PartitionSpec as P

H = 12
HD = 64
SEQ = 197


EPSILON = 1e-06
ROW_CONTRACT = (((0,), (0,)), ((), ()))
COL_CONTRACT = (((1,), (1,)), ((), ()))


def layer_norm(values, norm_gain):
    row_mean = jnp.mean(values, axis=-1, keepdims=True)
    centered = values - row_mean
    variance = jnp.mean(centered * centered, axis=-1, keepdims=True)
    return centered * lax.rsqrt(variance + EPSILON) * norm_gain


def normalize_rows(scores):
    row_top = jnp.max(scores, axis=-1, keepdims=True)
    exp_scores = jnp.exp(scores - row_top)
    return exp_scores / jnp.sum(exp_scores, axis=-1, keepdims=True)


def gelu_parts(values):
    sqrt_half = np.float32(np.sqrt(0.5))
    tail = lax.erfc(-values * sqrt_half)
    density = jnp.exp(-0.5 * values * values) * np.float32(1.0 / np.sqrt(2.0 * np.pi))
    return 0.5 * values * tail, 0.5 * tail + values * density


def shards(
    tokens,
    image_counts,
    routes,
    w_qkv,
    w_out,
    w_router,
    gain_attn,
    gain_moe,
    w_in,
    w_back,
    cotangent,
):
    rows, width = tokens.shape
    experts = lax.axis_size("expert")
    capacity = 8 * (5 * rows // (16 * experts)) + 8
    overflow = experts * capacity
    images = rows // SEQ
    qkv_cols = w_qkv.shape[1]
    n_route = w_router.shape[1]
    ff = w_in.shape[2]
    score_scale = HD ** (-0.5)
    row_ids = jnp.arange(rows, dtype=jnp.int32)
    live_int = (row_ids // SEQ < image_counts[0, 0]).astype(jnp.int32)
    live_rows = live_int.astype(jnp.float32)

    dense_local = jnp.concatenate(
        [w_qkv, w_out, w_router, gain_attn[:, None], gain_moe[:, None]], axis=1
    )
    dense_full = lax.all_gather(dense_local, "shard", axis=0, tiled=True)
    full_qkv = dense_full[:, :qkv_cols]
    full_out = dense_full[:, qkv_cols : qkv_cols + width]
    full_router = dense_full[:, qkv_cols + width : qkv_cols + width + n_route]
    gain_one = dense_full[:, -2].astype(jnp.float32)
    gain_two = dense_full[:, -1].astype(jnp.float32)

    back_rows = w_back.shape[1]
    expert_local = jnp.stack(
        [w_in[0], w_back[0].reshape(back_rows * width // ff, ff)], axis=0
    )
    expert_full = lax.all_gather(expert_local, "shard", axis=1, tiled=True)
    expert_first = expert_full[0]
    expert_second = expert_full[1].reshape(ff, width)

    token_f = tokens.astype(jnp.float32)
    attn_in = layer_norm(token_f, gain_one).astype(jnp.bfloat16)
    projected = jnp.dot(attn_in, full_qkv, preferred_element_type=jnp.float32).astype(jnp.bfloat16)
    split_heads = projected.reshape(images, SEQ, 3, H, HD)
    queries = split_heads[:, :, 0]
    keys_part = split_heads[:, :, 1]
    values_part = split_heads[:, :, 2]
    scores = (
        jnp.einsum("ishd,ithd->ihst", queries, keys_part, preferred_element_type=jnp.float32)
        * score_scale
    )
    row_top = jnp.max(scores, axis=-1, keepdims=True)
    log_total = row_top + jnp.log(jnp.sum(jnp.exp(scores - row_top), axis=-1, keepdims=True))
    attn_probs = jnp.exp(scores - log_total)
    probs_low = attn_probs.astype(jnp.bfloat16)
    mixed_rows = (
        jnp.einsum(
            "ihst,ithd->ishd",
            probs_low,
            values_part,
            preferred_element_type=jnp.float32,
        )
        .reshape(rows, width)
        .astype(jnp.bfloat16)
    )
    hidden_state = token_f + jnp.dot(mixed_rows, full_out, preferred_element_type=jnp.float32)
    moe_in = layer_norm(hidden_state, gain_two).astype(jnp.bfloat16)
    logits = jnp.dot(moe_in, full_router, preferred_element_type=jnp.float32)
    router_probs = normalize_rows(logits)
    expert_ids = jnp.arange(experts, dtype=jnp.int32)
    choose = (routes[:, :, None] == expert_ids).astype(jnp.float32)
    chosen = jnp.sum(choose * router_probs[:, None, :], axis=2)
    pick_table = (routes[:, :, None] == expert_ids).astype(jnp.int32) * live_int[:, None, None]
    flat_picks = pick_table.reshape(rows * 2, experts)
    before = jnp.cumsum(flat_picks, axis=0) - flat_picks
    slot_index = jnp.sum(before * flat_picks, axis=1).reshape(rows, 2)
    position = jnp.where(live_int[:, None] > 0, routes * capacity + slot_index, overflow)

    n_chunks = 2
    part_cap = 8 * ((capacity + 8 * n_chunks - 1) // (8 * n_chunks))
    chunk_sizes = [min(part_cap, capacity - k * part_cap) for k in range(n_chunks)]
    chunk_sizes = [size for size in chunk_sizes if size > 0]
    chunk_starts = [sum(chunk_sizes[:k]) for k in range(len(chunk_sizes))]
    slot_ids = jnp.concatenate(
        [
            (
                jnp.arange(experts, dtype=jnp.int32)[:, None] * capacity
                + start
                + jnp.arange(size, dtype=jnp.int32)[None, :]
            ).reshape(-1)
            for start, size in zip(chunk_starts, chunk_sizes)
        ]
    )[:, None]
    take_first = (slot_ids == position[None, :, 0]).astype(jnp.bfloat16)
    take_second = (slot_ids == position[None, :, 1]).astype(jnp.bfloat16)

    grad_out = cotangent.astype(jnp.float32) * live_rows[:, None]
    weighted = chosen * live_rows[:, None]
    grad_picked = (weighted[:, :, None] * grad_out[:, None, :]).astype(jnp.bfloat16)

    sent_rows = jnp.dot(
        take_first + take_second, moe_in, preferred_element_type=jnp.float32
    ).astype(jnp.bfloat16)
    sent_grad = (
        jnp.dot(take_first, grad_picked[:, 0], preferred_element_type=jnp.float32)
        + jnp.dot(take_second, grad_picked[:, 1], preferred_element_type=jnp.float32)
    ).astype(jnp.bfloat16)
    outgoing = jnp.concatenate([sent_rows, sent_grad], axis=1)

    grad_first = None
    grad_second = None
    returned_parts = []
    for start, size in zip(chunk_starts, chunk_sizes):
        arrived = lax.all_to_all(
            outgoing[experts * start : experts * (start + size)].reshape(
                experts, size, 2 * width
            ),
            "expert",
            split_axis=0,
            concat_axis=0,
            tiled=True,
        ).reshape(experts * size, 2 * width)
        flat_arrived = arrived[:, :width]
        flat_grad = arrived[:, width:]
        hidden_grad = lax.dot_general(
            flat_grad, expert_second, COL_CONTRACT, preferred_element_type=jnp.float32
        )
        pre_act = jnp.dot(flat_arrived, expert_first, preferred_element_type=jnp.float32)
        activated, slope = gelu_parts(pre_act)
        activated = activated.astype(jnp.bfloat16)
        pre_grad = (hidden_grad * slope).astype(jnp.bfloat16)
        produced = jnp.dot(
            activated, expert_second, preferred_element_type=jnp.float32
        ).astype(jnp.bfloat16)
        row_grad = lax.dot_general(
            pre_grad, expert_first, COL_CONTRACT, preferred_element_type=jnp.float32
        ).astype(jnp.bfloat16)
        part_second = lax.dot_general(
            activated, flat_grad, ROW_CONTRACT, preferred_element_type=jnp.float32
        )
        part_first = lax.dot_general(
            flat_arrived, pre_grad, ROW_CONTRACT, preferred_element_type=jnp.float32
        )
        grad_first = part_first if grad_first is None else grad_first + part_first
        grad_second = part_second if grad_second is None else grad_second + part_second
        returning = jnp.concatenate([produced, row_grad], axis=1).reshape(
            experts, size, 2 * width
        )
        returned_parts.append(
            lax.all_to_all(returning, "expert", split_axis=0, concat_axis=0, tiled=True)
        )

    expert_grads = jnp.stack(
        [grad_first, grad_second.reshape(width, ff)], axis=0
    ).astype(jnp.bfloat16)
    expert_share = lax.psum_scatter(expert_grads, "shard", scatter_dimension=1, tiled=True)
    expert_share = expert_share.astype(jnp.float32)
    grad_in_share = expert_share[0][None]
    grad_back_share = expert_share[1].reshape(back_rows, width)[None]

    returned = jnp.concatenate(
        [part.reshape(-1, 2 * width) for part in returned_parts], axis=0
    )
    picked_first = lax.dot_general(
        take_first, returned, ROW_CONTRACT, preferred_element_type=jnp.float32
    )
    picked_second = lax.dot_general(
        take_second, returned, ROW_CONTRACT, preferred_element_type=jnp.float32
    )
    moe_out = (
        weighted[:, 0:1] * picked_first[:, :width] + weighted[:, 1:2] * picked_second[:, :width]
    )
    output = (live_rows[:, None] * (hidden_state + moe_out)).astype(jnp.bfloat16)
    grad_chosen = jnp.stack(
        [
            jnp.sum(grad_out * picked_first[:, :width], axis=1),
            jnp.sum(grad_out * picked_second[:, :width], axis=1),
        ],
        axis=1,
    ) * live_rows[:, None]
    expert_part = (picked_first[:, width:] + picked_second[:, width:]) * live_rows[:, None]
    prob_sum = jnp.sum(choose * grad_chosen[:, :, None], axis=1)
    logit_grad = (
        router_probs * (prob_sum - jnp.sum(router_probs * prob_sum, axis=-1, keepdims=True))
    ).astype(jnp.bfloat16)
    grad_router = lax.dot_general(
        moe_in, logit_grad, ROW_CONTRACT, preferred_element_type=jnp.float32
    )
    moe_in_grad = expert_part + lax.dot_general(
        logit_grad, full_router, COL_CONTRACT, preferred_element_type=jnp.float32
    )
    _, norm_back = jax.vjp(layer_norm, hidden_state, gain_two)
    state_part, grad_gain_two = norm_back(moe_in_grad)
    state_grad = grad_out + state_part
    branch_grad = state_grad.astype(jnp.bfloat16)
    grad_wout = lax.dot_general(
        mixed_rows, branch_grad, ROW_CONTRACT, preferred_element_type=jnp.float32
    )
    mixed_grad = lax.dot_general(
        branch_grad, full_out, COL_CONTRACT, preferred_element_type=jnp.float32
    )
    mixed_grad = mixed_grad.astype(jnp.bfloat16).reshape(images, SEQ, H, HD)
    grad_values = jnp.einsum(
        "ihst,ishd->ithd",
        probs_low,
        mixed_grad,
        preferred_element_type=jnp.float32,
    )
    prob_grad = jnp.einsum(
        "ishd,ithd->ihst", mixed_grad, values_part, preferred_element_type=jnp.float32
    )
    score_grad = (
        attn_probs * (prob_grad - jnp.sum(attn_probs * prob_grad, axis=-1, keepdims=True))
    ).astype(jnp.bfloat16)
    grad_queries = (
        jnp.einsum("ihst,ithd->ishd", score_grad, keys_part, preferred_element_type=jnp.float32)
        * score_scale
    )
    grad_keys = (
        jnp.einsum("ihst,ishd->ithd", score_grad, queries, preferred_element_type=jnp.float32)
        * score_scale
    )
    projected_grad = (
        jnp.stack([grad_queries, grad_keys, grad_values], axis=2)
        .reshape(rows, 3 * width)
        .astype(jnp.bfloat16)
    )
    grad_qkv = lax.dot_general(
        attn_in, projected_grad, ROW_CONTRACT, preferred_element_type=jnp.float32
    )
    attn_in_grad = lax.dot_general(
        projected_grad, full_qkv, COL_CONTRACT, preferred_element_type=jnp.float32
    )
    _, first_back = jax.vjp(layer_norm, token_f, gain_one)
    token_part, grad_gain_one = first_back(attn_in_grad)
    grad_tokens = (state_grad + token_part).astype(jnp.bfloat16)

    dense_grads = jnp.concatenate(
        [grad_qkv, grad_wout, grad_router, grad_gain_one[:, None], grad_gain_two[:, None]],
        axis=1,
    ).astype(jnp.bfloat16)
    dense_share = lax.psum_scatter(dense_grads, "shard", scatter_dimension=0, tiled=True)
    dense_total = lax.psum(dense_share, "expert").astype(jnp.float32)
    return (
        output,
        grad_tokens,
        dense_total[:, :qkv_cols],
        dense_total[:, qkv_cols : qkv_cols + width],
        dense_total[:, qkv_cols + width : qkv_cols + width + n_route],
        dense_total[:, -2],
        dense_total[:, -1],
        grad_in_share,
        grad_back_share,
    )


def solution(mesh):
    return _mapped(mesh)


def _mapped(mesh):
    return jax.shard_map(
        shards,
        mesh=mesh,
        in_specs=(
            P(("expert", "shard"), None),
            P("expert", "shard"),
            P(("expert", "shard"), None),
            P("shard", None),
            P("shard", None),
            P("shard", None),
            P("shard"),
            P("shard"),
            P("expert", "shard", None),
            P("expert", "shard", None),
            P(("expert", "shard"), None),
        ),
        out_specs=(
            P(("expert", "shard"), None),
            P(("expert", "shard"), None),
            P("shard", None),
            P("shard", None),
            P("shard", None),
            P("shard"),
            P("shard"),
            P("expert", "shard", None),
            P("expert", "shard", None),
        ),
        check_vma=False,
    )
```

```python
import functools

import jax
import numpy as np
import jax.numpy as jnp
from jax import lax
from jax.experimental import pallas as pl
from jax.experimental.pallas import tpu as pltpu
from jax.sharding import PartitionSpec as P

HD = 64
SEQ = 197


EPSILON = 1e-06
ROW_CONTRACT = (((0,), (0,)), ((), ()))
COL_CONTRACT = (((1,), (1,)), ((), ()))


def _image_of(idx, images):
    count = jnp.zeros(idx.shape, jnp.int32)
    for i in range(1, images + 1):
        count = count + (idx >= i * SEQ).astype(jnp.int32)
    return count


def _same_image(size, images):
    rows = lax.broadcasted_iota(jnp.int32, (size, size), 0)
    cols = lax.broadcasted_iota(jnp.int32, (size, size), 1)
    return _image_of(rows, images) == _image_of(cols, images)


def _softmax_masked(qj, k, same):
    s = lax.dot_general(qj, k, COL_CONTRACT, preferred_element_type=jnp.float32) * (HD ** -0.5)
    s = jnp.where(same, s, -jnp.inf)
    top = jnp.max(s, axis=1, keepdims=True)
    e = jnp.exp(s - top)
    return e / jnp.sum(e, axis=1, keepdims=True)


def attn_fwd_kernel(q_ref, k_ref, v_ref, o_ref, *, images):
    R = q_ref.shape[0]
    q = q_ref[...]
    k = k_ref[...]
    v = v_ref[...]
    same = _same_image(R, images)
    lane = lax.broadcasted_iota(jnp.int32, (1, 2 * HD), 1)
    out = jnp.zeros((R, 2 * HD), jnp.float32)
    for j in range(2):
        in_head = (lane >= HD) == (j == 1)
        p = _softmax_masked(jnp.where(in_head, q, jnp.zeros_like(q)), k, same)
        o = jnp.dot(p.astype(jnp.bfloat16), v, preferred_element_type=jnp.float32)
        out = jnp.where(in_head, o, out)
    o_ref[...] = out.astype(o_ref.dtype)


def attn_bwd_kernel(q_ref, k_ref, v_ref, g_ref, dq_ref, dk_ref, dv_ref, *, images):
    R = q_ref.shape[0]
    q = q_ref[...]
    k = k_ref[...]
    v = v_ref[...]
    g = g_ref[...]
    same = _same_image(R, images)
    lane = lax.broadcasted_iota(jnp.int32, (1, 2 * HD), 1)
    dq = jnp.zeros((R, 2 * HD), jnp.float32)
    dk = jnp.zeros((R, 2 * HD), jnp.float32)
    dv = jnp.zeros((R, 2 * HD), jnp.float32)
    for j in range(2):
        in_head = (lane >= HD) == (j == 1)
        p = _softmax_masked(jnp.where(in_head, q, jnp.zeros_like(q)), k, same)
        gj = jnp.where(in_head, g, jnp.zeros_like(g))
        dp = lax.dot_general(gj, v, COL_CONTRACT, preferred_element_type=jnp.float32)
        ds = (p * (dp - jnp.sum(p * dp, axis=1, keepdims=True))).astype(jnp.bfloat16)
        dq_j = jnp.dot(ds, k, preferred_element_type=jnp.float32) * (HD ** -0.5)
        dk_j = lax.dot_general(ds, q, ROW_CONTRACT, preferred_element_type=jnp.float32) * (HD ** -0.5)
        dv_j = lax.dot_general(p.astype(jnp.bfloat16), g, ROW_CONTRACT, preferred_element_type=jnp.float32)
        dq = jnp.where(in_head, dq_j, dq)
        dk = jnp.where(in_head, dk_j, dk)
        dv = jnp.where(in_head, dv_j, dv)
    dq_ref[...] = dq.astype(dq_ref.dtype)
    dk_ref[...] = dk.astype(dk_ref.dtype)
    dv_ref[...] = dv.astype(dv_ref.dtype)


def attention_fwd(projected, images):
    R = projected.shape[0]
    W = projected.shape[1] // 3
    pairs = W // (2 * HD)
    blk = lambda off: pl.BlockSpec((R, 2 * HD), lambda h: (0, off + h))
    return pl.pallas_call(
        functools.partial(attn_fwd_kernel, images=images),
        grid=(pairs,),
        in_specs=[blk(0), blk(pairs), blk(2 * pairs)],
        out_specs=blk(0),
        out_shape=jax.ShapeDtypeStruct((R, W), jnp.bfloat16),
        compiler_params=pltpu.CompilerParams(vmem_limit_bytes=48 * 1024 * 1024),
    )(projected, projected, projected)


def attention_bwd(projected, mixed_grad, images):
    R = projected.shape[0]
    W = projected.shape[1] // 3
    pairs = W // (2 * HD)
    blk = lambda off: pl.BlockSpec((R, 2 * HD), lambda h: (0, off + h))
    out = jax.ShapeDtypeStruct((R, W), jnp.bfloat16)
    return pl.pallas_call(
        functools.partial(attn_bwd_kernel, images=images),
        grid=(pairs,),
        in_specs=[blk(0), blk(pairs), blk(2 * pairs), blk(0)],
        out_specs=[blk(0), blk(0), blk(0)],
        out_shape=[out, out, out],
        compiler_params=pltpu.CompilerParams(vmem_limit_bytes=48 * 1024 * 1024),
    )(projected, projected, projected, mixed_grad)


def layer_norm(values, norm_gain):
    row_mean = jnp.mean(values, axis=-1, keepdims=True)
    centered = values - row_mean
    variance = jnp.mean(centered * centered, axis=-1, keepdims=True)
    return centered * lax.rsqrt(variance + EPSILON) * norm_gain


def normalize_rows(scores):
    row_top = jnp.max(scores, axis=-1, keepdims=True)
    exp_scores = jnp.exp(scores - row_top)
    return exp_scores / jnp.sum(exp_scores, axis=-1, keepdims=True)


def gelu_parts(values):
    sqrt_half = np.float32(np.sqrt(0.5))
    tail = lax.erfc(-values * sqrt_half)
    density = jnp.exp(-0.5 * values * values) * np.float32(1.0 / np.sqrt(2.0 * np.pi))
    return 0.5 * values * tail, 0.5 * tail + values * density


def shards(
    tokens,
    image_counts,
    routes,
    w_qkv,
    w_out,
    w_router,
    gain_attn,
    gain_moe,
    w_in,
    w_back,
    cotangent,
):
    rows, width = tokens.shape
    experts = lax.axis_size("expert")
    capacity = 8 * (5 * rows // (16 * experts)) + 8
    overflow = experts * capacity
    images = rows // SEQ
    qkv_cols = w_qkv.shape[1]
    n_route = w_router.shape[1]
    ff = w_in.shape[2]
    row_ids = jnp.arange(rows, dtype=jnp.int32)
    live_int = (row_ids // SEQ < image_counts[0, 0]).astype(jnp.int32)
    live_rows = live_int.astype(jnp.float32)

    dense_local = jnp.concatenate(
        [w_qkv, w_out, w_router, gain_attn[:, None], gain_moe[:, None]], axis=1
    )
    dense_full = lax.all_gather(dense_local, "shard", axis=0, tiled=True)
    full_qkv = dense_full[:, :qkv_cols]
    full_out = dense_full[:, qkv_cols : qkv_cols + width]
    full_router = dense_full[:, qkv_cols + width : qkv_cols + width + n_route]
    gain_one = dense_full[:, -2].astype(jnp.float32)
    gain_two = dense_full[:, -1].astype(jnp.float32)

    back_rows = w_back.shape[1]
    expert_local = jnp.stack(
        [w_in[0], w_back[0].reshape(back_rows * width // ff, ff)], axis=0
    )
    expert_full = lax.all_gather(expert_local, "shard", axis=1, tiled=True)
    expert_first = expert_full[0]
    expert_second = expert_full[1].reshape(ff, width)

    token_f = tokens.astype(jnp.float32)
    attn_in = layer_norm(token_f, gain_one).astype(jnp.bfloat16)
    projected = jnp.dot(attn_in, full_qkv, preferred_element_type=jnp.float32).astype(jnp.bfloat16)
    pad_rows = -(-rows // 128) * 128
    projected_pad = jnp.pad(projected, ((0, pad_rows - rows), (0, 0)))
    mixed_rows = attention_fwd(projected_pad, images)[:rows]
    hidden_state = token_f + jnp.dot(mixed_rows, full_out, preferred_element_type=jnp.float32)
    moe_in = layer_norm(hidden_state, gain_two).astype(jnp.bfloat16)
    logits = jnp.dot(moe_in, full_router, preferred_element_type=jnp.float32)
    router_probs = normalize_rows(logits)
    expert_ids = jnp.arange(experts, dtype=jnp.int32)
    choose = (routes[:, :, None] == expert_ids).astype(jnp.float32)
    chosen = jnp.sum(choose * router_probs[:, None, :], axis=2)
    pick_table = (routes[:, :, None] == expert_ids).astype(jnp.int32) * live_int[:, None, None]
    flat_picks = pick_table.reshape(rows * 2, experts)
    before = jnp.cumsum(flat_picks, axis=0) - flat_picks
    slot_index = jnp.sum(before * flat_picks, axis=1).reshape(rows, 2)
    position = jnp.where(live_int[:, None] > 0, routes * capacity + slot_index, overflow)

    n_chunks = 2
    part_cap = 8 * ((capacity + 8 * n_chunks - 1) // (8 * n_chunks))
    chunk_sizes = [min(part_cap, capacity - k * part_cap) for k in range(n_chunks)]
    chunk_sizes = [size for size in chunk_sizes if size > 0]
    chunk_starts = [sum(chunk_sizes[:k]) for k in range(len(chunk_sizes))]
    slot_ids = jnp.concatenate(
        [
            (
                jnp.arange(experts, dtype=jnp.int32)[:, None] * capacity
                + start
                + jnp.arange(size, dtype=jnp.int32)[None, :]
            ).reshape(-1)
            for start, size in zip(chunk_starts, chunk_sizes)
        ]
    )[:, None]
    take_first = (slot_ids == position[None, :, 0]).astype(jnp.bfloat16)
    take_second = (slot_ids == position[None, :, 1]).astype(jnp.bfloat16)

    grad_out = cotangent.astype(jnp.float32) * live_rows[:, None]
    weighted = chosen * live_rows[:, None]
    grad_picked = (weighted[:, :, None] * grad_out[:, None, :]).astype(jnp.bfloat16)

    sent_rows = jnp.dot(
        take_first + take_second, moe_in, preferred_element_type=jnp.float32
    ).astype(jnp.bfloat16)
    sent_grad = (
        jnp.dot(take_first, grad_picked[:, 0], preferred_element_type=jnp.float32)
        + jnp.dot(take_second, grad_picked[:, 1], preferred_element_type=jnp.float32)
    ).astype(jnp.bfloat16)
    outgoing = jnp.concatenate([sent_rows, sent_grad], axis=1)

    grad_first = None
    grad_second = None
    returned_parts = []
    for start, size in zip(chunk_starts, chunk_sizes):
        arrived = lax.all_to_all(
            outgoing[experts * start : experts * (start + size)].reshape(
                experts, size, 2 * width
            ),
            "expert",
            split_axis=0,
            concat_axis=0,
            tiled=True,
        ).reshape(experts * size, 2 * width)
        flat_arrived = arrived[:, :width]
        flat_grad = arrived[:, width:]
        hidden_grad = lax.dot_general(
            flat_grad, expert_second, COL_CONTRACT, preferred_element_type=jnp.float32
        )
        pre_act = jnp.dot(flat_arrived, expert_first, preferred_element_type=jnp.float32)
        activated, slope = gelu_parts(pre_act)
        activated = activated.astype(jnp.bfloat16)
        pre_grad = (hidden_grad * slope).astype(jnp.bfloat16)
        produced = jnp.dot(
            activated, expert_second, preferred_element_type=jnp.float32
        ).astype(jnp.bfloat16)
        row_grad = lax.dot_general(
            pre_grad, expert_first, COL_CONTRACT, preferred_element_type=jnp.float32
        ).astype(jnp.bfloat16)
        part_second = lax.dot_general(
            activated, flat_grad, ROW_CONTRACT, preferred_element_type=jnp.float32
        )
        part_first = lax.dot_general(
            flat_arrived, pre_grad, ROW_CONTRACT, preferred_element_type=jnp.float32
        )
        grad_first = part_first if grad_first is None else grad_first + part_first
        grad_second = part_second if grad_second is None else grad_second + part_second
        returning = jnp.concatenate([produced, row_grad], axis=1).reshape(
            experts, size, 2 * width
        )
        returned_parts.append(
            lax.all_to_all(returning, "expert", split_axis=0, concat_axis=0, tiled=True)
        )

    expert_grads = jnp.stack(
        [grad_first, grad_second.reshape(width, ff)], axis=0
    ).astype(jnp.bfloat16)
    expert_share = lax.psum_scatter(expert_grads, "shard", scatter_dimension=1, tiled=True)
    expert_share = expert_share.astype(jnp.float32)
    grad_in_share = expert_share[0][None]
    grad_back_share = expert_share[1].reshape(back_rows, width)[None]

    returned = jnp.concatenate(
        [part.reshape(-1, 2 * width) for part in returned_parts], axis=0
    )
    picked_first = lax.dot_general(
        take_first, returned, ROW_CONTRACT, preferred_element_type=jnp.float32
    )
    picked_second = lax.dot_general(
        take_second, returned, ROW_CONTRACT, preferred_element_type=jnp.float32
    )
    moe_out = (
        weighted[:, 0:1] * picked_first[:, :width] + weighted[:, 1:2] * picked_second[:, :width]
    )
    output = (live_rows[:, None] * (hidden_state + moe_out)).astype(jnp.bfloat16)
    grad_chosen = jnp.stack(
        [
            jnp.sum(grad_out * picked_first[:, :width], axis=1),
            jnp.sum(grad_out * picked_second[:, :width], axis=1),
        ],
        axis=1,
    ) * live_rows[:, None]
    expert_part = (picked_first[:, width:] + picked_second[:, width:]) * live_rows[:, None]
    prob_sum = jnp.sum(choose * grad_chosen[:, :, None], axis=1)
    logit_grad = (
        router_probs * (prob_sum - jnp.sum(router_probs * prob_sum, axis=-1, keepdims=True))
    ).astype(jnp.bfloat16)
    grad_router = lax.dot_general(
        moe_in, logit_grad, ROW_CONTRACT, preferred_element_type=jnp.float32
    )
    moe_in_grad = expert_part + lax.dot_general(
        logit_grad, full_router, COL_CONTRACT, preferred_element_type=jnp.float32
    )
    _, norm_back = jax.vjp(layer_norm, hidden_state, gain_two)
    state_part, grad_gain_two = norm_back(moe_in_grad)
    state_grad = grad_out + state_part
    branch_grad = state_grad.astype(jnp.bfloat16)
    grad_wout = lax.dot_general(
        mixed_rows, branch_grad, ROW_CONTRACT, preferred_element_type=jnp.float32
    )
    mixed_grad = lax.dot_general(
        branch_grad, full_out, COL_CONTRACT, preferred_element_type=jnp.float32
    )
    mixed_grad = jnp.pad(mixed_grad.astype(jnp.bfloat16), ((0, pad_rows - rows), (0, 0)))
    grad_q, grad_k, grad_v = attention_bwd(projected_pad, mixed_grad, images)
    projected_grad = jnp.concatenate([grad_q, grad_k, grad_v], axis=1)[:rows]
    grad_qkv = lax.dot_general(
        attn_in, projected_grad, ROW_CONTRACT, preferred_element_type=jnp.float32
    )
    attn_in_grad = lax.dot_general(
        projected_grad, full_qkv, COL_CONTRACT, preferred_element_type=jnp.float32
    )
    _, first_back = jax.vjp(layer_norm, token_f, gain_one)
    token_part, grad_gain_one = first_back(attn_in_grad)
    grad_tokens = (state_grad + token_part).astype(jnp.bfloat16)

    dense_grads = jnp.concatenate(
        [grad_qkv, grad_wout, grad_router, grad_gain_one[:, None], grad_gain_two[:, None]],
        axis=1,
    ).astype(jnp.bfloat16)
    dense_share = lax.psum_scatter(dense_grads, "shard", scatter_dimension=0, tiled=True)
    dense_total = lax.psum(dense_share, "expert").astype(jnp.float32)
    return (
        output,
        grad_tokens,
        dense_total[:, :qkv_cols],
        dense_total[:, qkv_cols : qkv_cols + width],
        dense_total[:, qkv_cols + width : qkv_cols + width + n_route],
        dense_total[:, -2],
        dense_total[:, -1],
        grad_in_share,
        grad_back_share,
    )


def solution(mesh):
    return _mapped(mesh)


def _mapped(mesh):
    return jax.shard_map(
        shards,
        mesh=mesh,
        in_specs=(
            P(("expert", "shard"), None),
            P("expert", "shard"),
            P(("expert", "shard"), None),
            P("shard", None),
            P("shard", None),
            P("shard", None),
            P("shard"),
            P("shard"),
            P("expert", "shard", None),
            P("expert", "shard", None),
            P(("expert", "shard"), None),
        ),
        out_specs=(
            P(("expert", "shard"), None),
            P(("expert", "shard"), None),
            P("shard", None),
            P("shard", None),
            P("shard", None),
            P("shard"),
            P("shard"),
            P("expert", "shard", None),
            P("expert", "shard", None),
        ),
        check_vma=False,
    )
```

```python
import functools

import jax
import numpy as np
import jax.numpy as jnp
from jax import lax
from jax.experimental import pallas as pl
from jax.experimental.pallas import tpu as pltpu
from jax.sharding import PartitionSpec as P

HD = 64
SEQ = 197


EPSILON = 1e-06
ROW_CONTRACT = (((0,), (0,)), ((), ()))
COL_CONTRACT = (((1,), (1,)), ((), ()))


def _image_of(idx, images):
    count = jnp.zeros(idx.shape, jnp.int32)
    for i in range(1, images + 1):
        count = count + (idx >= i * SEQ).astype(jnp.int32)
    return count


def _same_image(size, images):
    rows = lax.broadcasted_iota(jnp.int32, (size, size), 0)
    cols = lax.broadcasted_iota(jnp.int32, (size, size), 1)
    return _image_of(rows, images) == _image_of(cols, images)


def _softmax_masked(qj, k, same):
    s = lax.dot_general(qj, k, COL_CONTRACT, preferred_element_type=jnp.float32) * (HD ** -0.5)
    s = jnp.where(same, s, -jnp.inf)
    top = jnp.max(s, axis=1, keepdims=True)
    e = jnp.exp(s - top)
    return e / jnp.sum(e, axis=1, keepdims=True)


def attn_fwd_kernel(q_ref, k_ref, v_ref, o_ref, *, images):
    R = q_ref.shape[0]
    q = q_ref[...]
    k = k_ref[...]
    v = v_ref[...]
    same = _same_image(R, images)
    lane = lax.broadcasted_iota(jnp.int32, (1, 2 * HD), 1)
    out = jnp.zeros((R, 2 * HD), jnp.float32)
    for j in range(2):
        in_head = (lane >= HD) == (j == 1)
        p = _softmax_masked(jnp.where(in_head, q, jnp.zeros_like(q)), k, same)
        o = jnp.dot(p.astype(jnp.bfloat16), v, preferred_element_type=jnp.float32)
        out = jnp.where(in_head, o, out)
    o_ref[...] = out.astype(o_ref.dtype)


def attn_bwd_kernel(q_ref, k_ref, v_ref, g_ref, dq_ref, dk_ref, dv_ref, *, images):
    R = q_ref.shape[0]
    q = q_ref[...]
    k = k_ref[...]
    v = v_ref[...]
    g = g_ref[...]
    same = _same_image(R, images)
    lane = lax.broadcasted_iota(jnp.int32, (1, 2 * HD), 1)
    dq = jnp.zeros((R, 2 * HD), jnp.float32)
    dk = jnp.zeros((R, 2 * HD), jnp.float32)
    dv = jnp.zeros((R, 2 * HD), jnp.float32)
    for j in range(2):
        in_head = (lane >= HD) == (j == 1)
        p = _softmax_masked(jnp.where(in_head, q, jnp.zeros_like(q)), k, same)
        gj = jnp.where(in_head, g, jnp.zeros_like(g))
        dp = lax.dot_general(gj, v, COL_CONTRACT, preferred_element_type=jnp.float32)
        ds = (p * (dp - jnp.sum(p * dp, axis=1, keepdims=True))).astype(jnp.bfloat16)
        dq_j = jnp.dot(ds, k, preferred_element_type=jnp.float32) * (HD ** -0.5)
        dk_j = lax.dot_general(ds, q, ROW_CONTRACT, preferred_element_type=jnp.float32) * (HD ** -0.5)
        dv_j = lax.dot_general(p.astype(jnp.bfloat16), g, ROW_CONTRACT, preferred_element_type=jnp.float32)
        dq = jnp.where(in_head, dq_j, dq)
        dk = jnp.where(in_head, dk_j, dk)
        dv = jnp.where(in_head, dv_j, dv)
    dq_ref[...] = dq.astype(dq_ref.dtype)
    dk_ref[...] = dk.astype(dk_ref.dtype)
    dv_ref[...] = dv.astype(dv_ref.dtype)


def attention_fwd(projected, images):
    R = projected.shape[0]
    W = projected.shape[1] // 3
    pairs = W // (2 * HD)
    blk = lambda off: pl.BlockSpec((R, 2 * HD), lambda h: (0, off + h))
    return pl.pallas_call(
        functools.partial(attn_fwd_kernel, images=images),
        grid=(pairs,),
        in_specs=[blk(0), blk(pairs), blk(2 * pairs)],
        out_specs=blk(0),
        out_shape=jax.ShapeDtypeStruct((R, W), jnp.bfloat16),
        compiler_params=pltpu.CompilerParams(vmem_limit_bytes=48 * 1024 * 1024),
    )(projected, projected, projected)


def attention_bwd(projected, mixed_grad, images):
    R = projected.shape[0]
    W = projected.shape[1] // 3
    pairs = W // (2 * HD)
    blk = lambda off: pl.BlockSpec((R, 2 * HD), lambda h: (0, off + h))
    out = jax.ShapeDtypeStruct((R, W), jnp.bfloat16)
    return pl.pallas_call(
        functools.partial(attn_bwd_kernel, images=images),
        grid=(pairs,),
        in_specs=[blk(0), blk(pairs), blk(2 * pairs), blk(0)],
        out_specs=[blk(0), blk(0), blk(0)],
        out_shape=[out, out, out],
        compiler_params=pltpu.CompilerParams(vmem_limit_bytes=48 * 1024 * 1024),
    )(projected, projected, projected, mixed_grad)


def _exchange(values, bits_left, bit, axis_name, size, index):
    axis = bits_left.index(bit)
    mine = (index >> bit) & 1
    keep = lax.dynamic_index_in_dim(values, mine, axis, keepdims=False)
    send = lax.dynamic_index_in_dim(values, 1 - mine, axis, keepdims=False)
    pairs = [(i, i ^ (1 << bit)) for i in range(size)]
    got = lax.ppermute(send.astype(jnp.bfloat16), axis_name, pairs)
    return keep + got.astype(jnp.float32), [b for b in bits_left if b != bit]


def shard_reduce_scatter(values, axis_name, split_col):
    size = lax.axis_size(axis_name)
    index = lax.axis_index(axis_name)
    n_bits = size.bit_length() - 1
    block = values.shape[0] // size
    bits = list(range(n_bits - 1, -1, -1))
    values = values.astype(jnp.float32).reshape([2] * n_bits + [block, values.shape[1]])
    values, bits = _exchange(values, bits, 0, axis_name, size, index)
    first, second = values[..., :split_col], values[..., split_col:]
    first_bits, second_bits = list(bits), list(bits)
    for up, down in zip(range(1, n_bits), range(n_bits - 1, 0, -1)):
        first, first_bits = _exchange(first, first_bits, up, axis_name, size, index)
        second, second_bits = _exchange(second, second_bits, down, axis_name, size, index)
    return jnp.concatenate([first, second], axis=-1)


def layer_norm(values, norm_gain):
    row_mean = jnp.mean(values, axis=-1, keepdims=True)
    centered = values - row_mean
    variance = jnp.mean(centered * centered, axis=-1, keepdims=True)
    return centered * lax.rsqrt(variance + EPSILON) * norm_gain


def normalize_rows(scores):
    row_top = jnp.max(scores, axis=-1, keepdims=True)
    exp_scores = jnp.exp(scores - row_top)
    return exp_scores / jnp.sum(exp_scores, axis=-1, keepdims=True)


def gelu_parts(values):
    sqrt_half = np.float32(np.sqrt(0.5))
    tail = lax.erfc(-values * sqrt_half)
    density = jnp.exp(-0.5 * values * values) * np.float32(1.0 / np.sqrt(2.0 * np.pi))
    return 0.5 * values * tail, 0.5 * tail + values * density


def shards(
    tokens,
    image_counts,
    routes,
    w_qkv,
    w_out,
    w_router,
    gain_attn,
    gain_moe,
    w_in,
    w_back,
    cotangent,
):
    rows, width = tokens.shape
    experts = lax.axis_size("expert")
    capacity = 8 * (5 * rows // (16 * experts)) + 8
    overflow = experts * capacity
    images = rows // SEQ
    qkv_cols = w_qkv.shape[1]
    n_route = w_router.shape[1]
    ff = w_in.shape[2]
    row_ids = jnp.arange(rows, dtype=jnp.int32)
    live_int = (row_ids // SEQ < image_counts[0, 0]).astype(jnp.int32)
    live_rows = live_int.astype(jnp.float32)

    dense_local = jnp.concatenate(
        [w_qkv, w_out, w_router, gain_attn[:, None], gain_moe[:, None]], axis=1
    )
    dense_full = lax.all_gather(dense_local, "shard", axis=0, tiled=True)
    full_qkv = dense_full[:, :qkv_cols]
    full_out = dense_full[:, qkv_cols : qkv_cols + width]
    full_router = dense_full[:, qkv_cols + width : qkv_cols + width + n_route]
    gain_one = dense_full[:, -2].astype(jnp.float32)
    gain_two = dense_full[:, -1].astype(jnp.float32)

    back_rows = w_back.shape[1]
    expert_local = jnp.stack(
        [w_in[0], w_back[0].reshape(back_rows * width // ff, ff)], axis=0
    )
    expert_full = lax.all_gather(expert_local, "shard", axis=1, tiled=True)
    expert_first = expert_full[0]
    expert_second = expert_full[1].reshape(ff, width)

    token_f = tokens.astype(jnp.float32)
    attn_in = lax.optimization_barrier(layer_norm(token_f, gain_one).astype(jnp.bfloat16))
    projected = jnp.dot(attn_in, full_qkv, preferred_element_type=jnp.float32).astype(jnp.bfloat16)
    pad_rows = -(-rows // 128) * 128
    projected_pad = jnp.pad(projected, ((0, pad_rows - rows), (0, 0)))
    mixed_rows = attention_fwd(projected_pad, images)[:rows]
    hidden_state = token_f + jnp.dot(mixed_rows, full_out, preferred_element_type=jnp.float32)
    moe_in = layer_norm(hidden_state, gain_two).astype(jnp.bfloat16)
    logits = jnp.dot(moe_in, full_router, preferred_element_type=jnp.float32)
    router_probs = normalize_rows(logits)
    expert_ids = jnp.arange(experts, dtype=jnp.int32)
    choose = (routes[:, :, None] == expert_ids).astype(jnp.float32)
    chosen = jnp.sum(choose * router_probs[:, None, :], axis=2)
    pick_table = (routes[:, :, None] == expert_ids).astype(jnp.int32) * live_int[:, None, None]
    flat_picks = pick_table.reshape(rows * 2, experts)
    before = jnp.cumsum(flat_picks, axis=0) - flat_picks
    slot_index = jnp.sum(before * flat_picks, axis=1).reshape(rows, 2)
    position = jnp.where(live_int[:, None] > 0, routes * capacity + slot_index, overflow)

    n_chunks = 2
    part_cap = 8 * ((capacity + 8 * n_chunks - 1) // (8 * n_chunks))
    chunk_sizes = [min(part_cap, capacity - k * part_cap) for k in range(n_chunks)]
    chunk_sizes = [size for size in chunk_sizes if size > 0]
    chunk_starts = [sum(chunk_sizes[:k]) for k in range(len(chunk_sizes))]
    slot_ids = jnp.concatenate(
        [
            (
                jnp.arange(experts, dtype=jnp.int32)[:, None] * capacity
                + start
                + jnp.arange(size, dtype=jnp.int32)[None, :]
            ).reshape(-1)
            for start, size in zip(chunk_starts, chunk_sizes)
        ]
    )[:, None]
    take_first = (slot_ids == position[None, :, 0]).astype(jnp.bfloat16)
    take_second = (slot_ids == position[None, :, 1]).astype(jnp.bfloat16)

    grad_out = cotangent.astype(jnp.float32) * live_rows[:, None]
    weighted = chosen * live_rows[:, None]
    grad_picked = (weighted[:, :, None] * grad_out[:, None, :]).astype(jnp.bfloat16)

    sent_rows = jnp.dot(
        take_first + take_second, moe_in, preferred_element_type=jnp.float32
    ).astype(jnp.bfloat16)
    sent_grad = (
        jnp.dot(take_first, grad_picked[:, 0], preferred_element_type=jnp.float32)
        + jnp.dot(take_second, grad_picked[:, 1], preferred_element_type=jnp.float32)
    ).astype(jnp.bfloat16)
    outgoing = jnp.concatenate([sent_rows, sent_grad], axis=1)

    grad_first = None
    grad_second = None
    returned_parts = []
    for start, size in zip(chunk_starts, chunk_sizes):
        arrived = lax.all_to_all(
            outgoing[experts * start : experts * (start + size)].reshape(
                experts, size, 2 * width
            ),
            "expert",
            split_axis=0,
            concat_axis=0,
            tiled=True,
        ).reshape(experts * size, 2 * width)
        flat_arrived = arrived[:, :width]
        flat_grad = arrived[:, width:]
        hidden_grad = lax.dot_general(
            flat_grad, expert_second, COL_CONTRACT, preferred_element_type=jnp.float32
        )
        pre_act = jnp.dot(flat_arrived, expert_first, preferred_element_type=jnp.float32)
        activated, slope = gelu_parts(pre_act)
        activated = activated.astype(jnp.bfloat16)
        pre_grad = (hidden_grad * slope).astype(jnp.bfloat16)
        produced = jnp.dot(
            activated, expert_second, preferred_element_type=jnp.float32
        ).astype(jnp.bfloat16)
        row_grad = lax.dot_general(
            pre_grad, expert_first, COL_CONTRACT, preferred_element_type=jnp.float32
        ).astype(jnp.bfloat16)
        part_second = lax.dot_general(
            activated, flat_grad, ROW_CONTRACT, preferred_element_type=jnp.float32
        )
        part_first = lax.dot_general(
            flat_arrived, pre_grad, ROW_CONTRACT, preferred_element_type=jnp.float32
        )
        grad_first = part_first if grad_first is None else grad_first + part_first
        grad_second = part_second if grad_second is None else grad_second + part_second
        returning = jnp.concatenate([produced, row_grad], axis=1).reshape(
            experts, size, 2 * width
        )
        returned_parts.append(
            lax.all_to_all(returning, "expert", split_axis=0, concat_axis=0, tiled=True)
        )

    expert_grads = jnp.stack(
        [grad_first, grad_second.reshape(width, ff)], axis=0
    ).astype(jnp.bfloat16)
    expert_share = lax.psum_scatter(expert_grads, "shard", scatter_dimension=1, tiled=True)
    expert_share = expert_share.astype(jnp.float32)
    grad_in_share = expert_share[0][None]
    grad_back_share = expert_share[1].reshape(back_rows, width)[None]

    returned = jnp.concatenate(
        [part.reshape(-1, 2 * width) for part in returned_parts], axis=0
    )
    picked_first = lax.dot_general(
        take_first, returned, ROW_CONTRACT, preferred_element_type=jnp.float32
    )
    picked_second = lax.dot_general(
        take_second, returned, ROW_CONTRACT, preferred_element_type=jnp.float32
    )
    moe_out = (
        weighted[:, 0:1] * picked_first[:, :width] + weighted[:, 1:2] * picked_second[:, :width]
    )
    output = (live_rows[:, None] * (hidden_state + moe_out)).astype(jnp.bfloat16)
    grad_chosen = jnp.stack(
        [
            jnp.sum(grad_out * picked_first[:, :width], axis=1),
            jnp.sum(grad_out * picked_second[:, :width], axis=1),
        ],
        axis=1,
    ) * live_rows[:, None]
    expert_part = (picked_first[:, width:] + picked_second[:, width:]) * live_rows[:, None]
    prob_sum = jnp.sum(choose * grad_chosen[:, :, None], axis=1)
    logit_grad = (
        router_probs * (prob_sum - jnp.sum(router_probs * prob_sum, axis=-1, keepdims=True))
    ).astype(jnp.bfloat16)
    grad_router = lax.dot_general(
        moe_in, logit_grad, ROW_CONTRACT, preferred_element_type=jnp.float32
    )
    moe_in_grad = expert_part + lax.dot_general(
        logit_grad, full_router, COL_CONTRACT, preferred_element_type=jnp.float32
    )
    _, norm_back = jax.vjp(layer_norm, hidden_state, gain_two)
    state_part, grad_gain_two = norm_back(moe_in_grad)
    state_grad = grad_out + state_part
    branch_grad = state_grad.astype(jnp.bfloat16)
    grad_wout = lax.dot_general(
        mixed_rows, branch_grad, ROW_CONTRACT, preferred_element_type=jnp.float32
    )
    mixed_grad = lax.dot_general(
        branch_grad, full_out, COL_CONTRACT, preferred_element_type=jnp.float32
    )
    mixed_grad = jnp.pad(mixed_grad.astype(jnp.bfloat16), ((0, pad_rows - rows), (0, 0)))
    grad_q, grad_k, grad_v = attention_bwd(projected_pad, mixed_grad, images)
    projected_grad = jnp.concatenate([grad_q, grad_k, grad_v], axis=1)
    attn_in_pad = jnp.pad(attn_in, ((0, pad_rows - rows), (0, 0)))
    grad_qkv = lax.dot_general(
        attn_in_pad, projected_grad, ROW_CONTRACT, preferred_element_type=jnp.float32
    )
    attn_in_grad = lax.dot_general(
        projected_grad[:rows], full_qkv, COL_CONTRACT, preferred_element_type=jnp.float32
    )
    _, first_back = jax.vjp(layer_norm, token_f, gain_one)
    token_part, grad_gain_one = first_back(attn_in_grad)
    grad_tokens = (state_grad + token_part).astype(jnp.bfloat16)

    small = jnp.concatenate(
        [grad_router, grad_gain_one[:, None], grad_gain_two[:, None]], axis=1
    )
    small = jnp.pad(small, ((0, 0), (0, 128 - small.shape[1])))
    dense_grads = jnp.concatenate([grad_qkv, grad_wout, small], axis=1)
    dense_share = shard_reduce_scatter(dense_grads, "shard", 128 * (dense_grads.shape[1] // 256))
    dense_total = lax.psum(dense_share.astype(jnp.bfloat16), "expert").astype(jnp.float32)
    return (
        output,
        grad_tokens,
        dense_total[:, :qkv_cols],
        dense_total[:, qkv_cols : qkv_cols + width],
        dense_total[:, qkv_cols + width : qkv_cols + width + n_route],
        dense_total[:, qkv_cols + width + n_route],
        dense_total[:, qkv_cols + width + n_route + 1],
        grad_in_share,
        grad_back_share,
    )


def solution(mesh):
    return _mapped(mesh)


def _mapped(mesh):
    return jax.shard_map(
        shards,
        mesh=mesh,
        in_specs=(
            P(("expert", "shard"), None),
            P("expert", "shard"),
            P(("expert", "shard"), None),
            P("shard", None),
            P("shard", None),
            P("shard", None),
            P("shard"),
            P("shard"),
            P("expert", "shard", None),
            P("expert", "shard", None),
            P(("expert", "shard"), None),
        ),
        out_specs=(
            P(("expert", "shard"), None),
            P(("expert", "shard"), None),
            P("shard", None),
            P("shard", None),
            P("shard", None),
            P("shard"),
            P("shard"),
            P("expert", "shard", None),
            P("expert", "shard", None),
        ),
        check_vma=False,
    )
```

```python
import functools

import jax
import numpy as np
import jax.numpy as jnp
from jax import lax
from jax.experimental import pallas as pl
from jax.experimental.pallas import tpu as pltpu
from jax.sharding import PartitionSpec as P

HD = 64
SEQ = 197


EPSILON = 1e-06
ROW_CONTRACT = (((0,), (0,)), ((), ()))
COL_CONTRACT = (((1,), (1,)), ((), ()))


def _softmax_masked(qj, k, valid):
    s = lax.dot_general(qj, k, COL_CONTRACT, preferred_element_type=jnp.float32) * (HD ** -0.5)
    s = jnp.where(valid, s, -jnp.inf)
    top = jnp.max(s, axis=1, keepdims=True)
    e = jnp.exp(s - top)
    return e / jnp.sum(e, axis=1, keepdims=True)


def attn_fwd_kernel(q_ref, k_ref, v_ref, o_ref, *, images, slot):
    valid = lax.broadcasted_iota(jnp.int32, (slot, slot), 1) < SEQ
    lane = lax.broadcasted_iota(jnp.int32, (1, 2 * HD), 1)
    for i in range(images):
        rows = pl.ds(i * slot, slot)
        q = q_ref[rows, :]
        k = k_ref[rows, :]
        v = v_ref[rows, :]
        out = jnp.zeros((slot, 2 * HD), jnp.float32)
        for j in range(2):
            in_head = (lane >= HD) == (j == 1)
            p = _softmax_masked(jnp.where(in_head, q, jnp.zeros_like(q)), k, valid)
            o = jnp.dot(p.astype(jnp.bfloat16), v, preferred_element_type=jnp.float32)
            out = jnp.where(in_head, o, out)
        o_ref[rows, :] = out.astype(o_ref.dtype)


def attn_bwd_kernel(q_ref, k_ref, v_ref, g_ref, dq_ref, dk_ref, dv_ref, *, images, slot):
    valid = lax.broadcasted_iota(jnp.int32, (slot, slot), 1) < SEQ
    lane = lax.broadcasted_iota(jnp.int32, (1, 2 * HD), 1)
    for i in range(images):
        rows = pl.ds(i * slot, slot)
        q = q_ref[rows, :]
        k = k_ref[rows, :]
        v = v_ref[rows, :]
        g = g_ref[rows, :]
        dq = jnp.zeros((slot, 2 * HD), jnp.float32)
        dk = jnp.zeros((slot, 2 * HD), jnp.float32)
        dv = jnp.zeros((slot, 2 * HD), jnp.float32)
        for j in range(2):
            in_head = (lane >= HD) == (j == 1)
            p = _softmax_masked(jnp.where(in_head, q, jnp.zeros_like(q)), k, valid)
            gj = jnp.where(in_head, g, jnp.zeros_like(g))
            dp = lax.dot_general(gj, v, COL_CONTRACT, preferred_element_type=jnp.float32)
            ds = (p * (dp - jnp.sum(p * dp, axis=1, keepdims=True))).astype(jnp.bfloat16)
            dq_j = jnp.dot(ds, k, preferred_element_type=jnp.float32) * (HD ** -0.5)
            dk_j = lax.dot_general(ds, q, ROW_CONTRACT, preferred_element_type=jnp.float32) * (HD ** -0.5)
            dv_j = lax.dot_general(
                p.astype(jnp.bfloat16), g, ROW_CONTRACT, preferred_element_type=jnp.float32
            )
            dq = jnp.where(in_head, dq_j, dq)
            dk = jnp.where(in_head, dk_j, dk)
            dv = jnp.where(in_head, dv_j, dv)
        dq_ref[rows, :] = dq.astype(dq_ref.dtype)
        dk_ref[rows, :] = dk.astype(dk_ref.dtype)
        dv_ref[rows, :] = dv.astype(dv_ref.dtype)


def attention_fwd(projected, images, slot):
    R = projected.shape[0]
    W = projected.shape[1] // 3
    pairs = W // (2 * HD)
    blk = lambda off: pl.BlockSpec((R, 2 * HD), lambda h: (0, off + h))
    return pl.pallas_call(
        functools.partial(attn_fwd_kernel, images=images, slot=slot),
        grid=(pairs,),
        in_specs=[blk(0), blk(pairs), blk(2 * pairs)],
        out_specs=blk(0),
        out_shape=jax.ShapeDtypeStruct((R, W), jnp.bfloat16),
        compiler_params=pltpu.CompilerParams(vmem_limit_bytes=48 * 1024 * 1024),
    )(projected, projected, projected)


def attention_bwd(projected, mixed_grad, images, slot):
    R = projected.shape[0]
    W = projected.shape[1] // 3
    pairs = W // (2 * HD)
    blk = lambda off: pl.BlockSpec((R, 2 * HD), lambda h: (0, off + h))
    out = jax.ShapeDtypeStruct((R, W), jnp.bfloat16)
    return pl.pallas_call(
        functools.partial(attn_bwd_kernel, images=images, slot=slot),
        grid=(pairs,),
        in_specs=[blk(0), blk(pairs), blk(2 * pairs), blk(0)],
        out_specs=[blk(0), blk(0), blk(0)],
        out_shape=[out, out, out],
        compiler_params=pltpu.CompilerParams(vmem_limit_bytes=48 * 1024 * 1024),
    )(projected, projected, projected, mixed_grad)


def to_slots(values, images, slot):
    cols = values.shape[1]
    spaced = jnp.pad(values.reshape(images, SEQ, cols), ((0, 0), (0, slot - SEQ), (0, 0)))
    return spaced.reshape(images * slot, cols)


def from_slots(values, images, slot):
    cols = values.shape[1]
    return values.reshape(images, slot, cols)[:, :SEQ].reshape(images * SEQ, cols)


def _exchange(values, bits_left, bit, axis_name, size, index):
    axis = bits_left.index(bit)
    mine = (index >> bit) & 1
    keep = lax.dynamic_index_in_dim(values, mine, axis, keepdims=False)
    send = lax.dynamic_index_in_dim(values, 1 - mine, axis, keepdims=False)
    pairs = [(i, i ^ (1 << bit)) for i in range(size)]
    got = lax.ppermute(send.astype(jnp.bfloat16), axis_name, pairs)
    return keep + got.astype(jnp.float32), [b for b in bits_left if b != bit]


def shard_reduce_scatter(values, axis_name, split_col):
    size = lax.axis_size(axis_name)
    index = lax.axis_index(axis_name)
    n_bits = size.bit_length() - 1
    block = values.shape[0] // size
    bits = list(range(n_bits - 1, -1, -1))
    values = values.astype(jnp.float32).reshape([2] * n_bits + [block, values.shape[1]])
    values, bits = _exchange(values, bits, 0, axis_name, size, index)
    first, second = values[..., :split_col], values[..., split_col:]
    first_bits, second_bits = list(bits), list(bits)
    for up, down in zip(range(1, n_bits), range(n_bits - 1, 0, -1)):
        first, first_bits = _exchange(first, first_bits, up, axis_name, size, index)
        second, second_bits = _exchange(second, second_bits, down, axis_name, size, index)
    return jnp.concatenate([first, second], axis=-1)


def layer_norm(values, norm_gain):
    row_mean = jnp.mean(values, axis=-1, keepdims=True)
    centered = values - row_mean
    variance = jnp.mean(centered * centered, axis=-1, keepdims=True)
    return centered * lax.rsqrt(variance + EPSILON) * norm_gain


def normalize_rows(scores):
    row_top = jnp.max(scores, axis=-1, keepdims=True)
    exp_scores = jnp.exp(scores - row_top)
    return exp_scores / jnp.sum(exp_scores, axis=-1, keepdims=True)


def gelu_parts(values):
    sqrt_half = np.float32(np.sqrt(0.5))
    tail = lax.erfc(-values * sqrt_half)
    density = jnp.exp(-0.5 * values * values) * np.float32(1.0 / np.sqrt(2.0 * np.pi))
    return 0.5 * values * tail, 0.5 * tail + values * density


def shards(
    tokens,
    image_counts,
    routes,
    w_qkv,
    w_out,
    w_router,
    gain_attn,
    gain_moe,
    w_in,
    w_back,
    cotangent,
):
    rows, width = tokens.shape
    experts = lax.axis_size("expert")
    capacity = 8 * (5 * rows // (16 * experts)) + 8
    overflow = experts * capacity
    images = rows // SEQ
    qkv_cols = w_qkv.shape[1]
    n_route = w_router.shape[1]
    ff = w_in.shape[2]
    row_ids = jnp.arange(rows, dtype=jnp.int32)
    live_int = (row_ids // SEQ < image_counts[0, 0]).astype(jnp.int32)
    live_rows = live_int.astype(jnp.float32)

    dense_local = jnp.concatenate(
        [w_qkv, w_out, w_router, gain_attn[:, None], gain_moe[:, None]], axis=1
    )
    dense_full = lax.all_gather(dense_local, "shard", axis=0, tiled=True)
    full_qkv = dense_full[:, :qkv_cols]
    full_out = dense_full[:, qkv_cols : qkv_cols + width]
    full_router = dense_full[:, qkv_cols + width : qkv_cols + width + n_route]
    gain_one = dense_full[:, -2].astype(jnp.float32)
    gain_two = dense_full[:, -1].astype(jnp.float32)

    back_rows = w_back.shape[1]
    expert_local = jnp.stack(
        [w_in[0], w_back[0].reshape(back_rows * width // ff, ff)], axis=0
    )
    expert_full = lax.all_gather(expert_local, "shard", axis=1, tiled=True)
    expert_first = expert_full[0]
    expert_second = expert_full[1].reshape(ff, width)

    token_f = tokens.astype(jnp.float32)
    attn_in = lax.optimization_barrier(layer_norm(token_f, gain_one).astype(jnp.bfloat16))
    projected = jnp.dot(attn_in, full_qkv, preferred_element_type=jnp.float32).astype(jnp.bfloat16)
    slot = -(-SEQ // 16) * 16
    projected_pad = to_slots(projected, images, slot)
    mixed_rows = from_slots(attention_fwd(projected_pad, images, slot), images, slot)
    hidden_state = token_f + jnp.dot(mixed_rows, full_out, preferred_element_type=jnp.float32)
    moe_in = layer_norm(hidden_state, gain_two).astype(jnp.bfloat16)
    logits = jnp.dot(moe_in, full_router, preferred_element_type=jnp.float32)
    router_probs = normalize_rows(logits)
    expert_ids = jnp.arange(experts, dtype=jnp.int32)
    choose = (routes[:, :, None] == expert_ids).astype(jnp.float32)
    chosen = jnp.sum(choose * router_probs[:, None, :], axis=2)
    pick_table = (routes[:, :, None] == expert_ids).astype(jnp.int32) * live_int[:, None, None]
    flat_picks = pick_table.reshape(rows * 2, experts)
    before = jnp.cumsum(flat_picks, axis=0) - flat_picks
    slot_index = jnp.sum(before * flat_picks, axis=1).reshape(rows, 2)
    position = jnp.where(live_int[:, None] > 0, routes * capacity + slot_index, overflow)

    n_chunks = 2
    part_cap = 8 * ((capacity + 8 * n_chunks - 1) // (8 * n_chunks))
    chunk_sizes = [min(part_cap, capacity - k * part_cap) for k in range(n_chunks)]
    chunk_sizes = [size for size in chunk_sizes if size > 0]
    chunk_starts = [sum(chunk_sizes[:k]) for k in range(len(chunk_sizes))]
    slot_ids = jnp.concatenate(
        [
            (
                jnp.arange(experts, dtype=jnp.int32)[:, None] * capacity
                + start
                + jnp.arange(size, dtype=jnp.int32)[None, :]
            ).reshape(-1)
            for start, size in zip(chunk_starts, chunk_sizes)
        ]
    )[:, None]
    take_first = (slot_ids == position[None, :, 0]).astype(jnp.bfloat16)
    take_second = (slot_ids == position[None, :, 1]).astype(jnp.bfloat16)

    grad_out = cotangent.astype(jnp.float32) * live_rows[:, None]
    weighted = chosen * live_rows[:, None]
    grad_picked = (weighted[:, :, None] * grad_out[:, None, :]).astype(jnp.bfloat16)

    sent_rows = jnp.dot(
        take_first + take_second, moe_in, preferred_element_type=jnp.float32
    ).astype(jnp.bfloat16)
    sent_grad = (
        jnp.dot(take_first, grad_picked[:, 0], preferred_element_type=jnp.float32)
        + jnp.dot(take_second, grad_picked[:, 1], preferred_element_type=jnp.float32)
    ).astype(jnp.bfloat16)
    outgoing = jnp.concatenate([sent_rows, sent_grad], axis=1)

    grad_first = None
    grad_second = None
    returned_parts = []
    for start, size in zip(chunk_starts, chunk_sizes):
        arrived = lax.all_to_all(
            outgoing[experts * start : experts * (start + size)].reshape(
                experts, size, 2 * width
            ),
            "expert",
            split_axis=0,
            concat_axis=0,
            tiled=True,
        ).reshape(experts * size, 2 * width)
        flat_arrived = arrived[:, :width]
        flat_grad = arrived[:, width:]
        hidden_grad = lax.dot_general(
            flat_grad, expert_second, COL_CONTRACT, preferred_element_type=jnp.float32
        )
        pre_act = jnp.dot(flat_arrived, expert_first, preferred_element_type=jnp.float32)
        activated, slope = gelu_parts(pre_act)
        activated = activated.astype(jnp.bfloat16)
        pre_grad = (hidden_grad * slope).astype(jnp.bfloat16)
        produced = jnp.dot(
            activated, expert_second, preferred_element_type=jnp.float32
        ).astype(jnp.bfloat16)
        row_grad = lax.dot_general(
            pre_grad, expert_first, COL_CONTRACT, preferred_element_type=jnp.float32
        ).astype(jnp.bfloat16)
        part_second = lax.dot_general(
            activated, flat_grad, ROW_CONTRACT, preferred_element_type=jnp.float32
        )
        part_first = lax.dot_general(
            flat_arrived, pre_grad, ROW_CONTRACT, preferred_element_type=jnp.float32
        )
        grad_first = part_first if grad_first is None else grad_first + part_first
        grad_second = part_second if grad_second is None else grad_second + part_second
        returning = jnp.concatenate([produced, row_grad], axis=1).reshape(
            experts, size, 2 * width
        )
        returned_parts.append(
            lax.all_to_all(returning, "expert", split_axis=0, concat_axis=0, tiled=True)
        )

    expert_grads = jnp.stack(
        [grad_first, grad_second.reshape(width, ff)], axis=0
    ).astype(jnp.bfloat16)
    expert_share = lax.psum_scatter(expert_grads, "shard", scatter_dimension=1, tiled=True)
    expert_share = expert_share.astype(jnp.float32)
    grad_in_share = expert_share[0][None]
    grad_back_share = expert_share[1].reshape(back_rows, width)[None]

    returned = jnp.concatenate(
        [part.reshape(-1, 2 * width) for part in returned_parts], axis=0
    )
    picked_first = lax.dot_general(
        take_first, returned, ROW_CONTRACT, preferred_element_type=jnp.float32
    )
    picked_second = lax.dot_general(
        take_second, returned, ROW_CONTRACT, preferred_element_type=jnp.float32
    )
    moe_out = (
        weighted[:, 0:1] * picked_first[:, :width] + weighted[:, 1:2] * picked_second[:, :width]
    )
    output = (live_rows[:, None] * (hidden_state + moe_out)).astype(jnp.bfloat16)
    grad_chosen = jnp.stack(
        [
            jnp.sum(grad_out * picked_first[:, :width], axis=1),
            jnp.sum(grad_out * picked_second[:, :width], axis=1),
        ],
        axis=1,
    ) * live_rows[:, None]
    expert_part = (picked_first[:, width:] + picked_second[:, width:]) * live_rows[:, None]
    prob_sum = jnp.sum(choose * grad_chosen[:, :, None], axis=1)
    logit_grad = (
        router_probs * (prob_sum - jnp.sum(router_probs * prob_sum, axis=-1, keepdims=True))
    ).astype(jnp.bfloat16)
    grad_router = lax.dot_general(
        moe_in, logit_grad, ROW_CONTRACT, preferred_element_type=jnp.float32
    )
    moe_in_grad = expert_part + lax.dot_general(
        logit_grad, full_router, COL_CONTRACT, preferred_element_type=jnp.float32
    )
    _, norm_back = jax.vjp(layer_norm, hidden_state, gain_two)
    state_part, grad_gain_two = norm_back(moe_in_grad)
    state_grad = grad_out + state_part
    branch_grad = state_grad.astype(jnp.bfloat16)
    grad_wout = lax.dot_general(
        mixed_rows, branch_grad, ROW_CONTRACT, preferred_element_type=jnp.float32
    )
    mixed_grad = lax.dot_general(
        branch_grad, full_out, COL_CONTRACT, preferred_element_type=jnp.float32
    )
    mixed_grad = to_slots(mixed_grad.astype(jnp.bfloat16), images, slot)
    grad_q, grad_k, grad_v = attention_bwd(projected_pad, mixed_grad, images, slot)
    projected_grad = jnp.concatenate([grad_q, grad_k, grad_v], axis=1)
    attn_in_pad = to_slots(attn_in, images, slot)
    grad_qkv = lax.dot_general(
        attn_in_pad, projected_grad, ROW_CONTRACT, preferred_element_type=jnp.float32
    )
    attn_in_grad = lax.dot_general(
        from_slots(projected_grad, images, slot),
        full_qkv,
        COL_CONTRACT,
        preferred_element_type=jnp.float32,
    )
    _, first_back = jax.vjp(layer_norm, token_f, gain_one)
    token_part, grad_gain_one = first_back(attn_in_grad)
    grad_tokens = (state_grad + token_part).astype(jnp.bfloat16)

    small = jnp.concatenate(
        [grad_router, grad_gain_one[:, None], grad_gain_two[:, None]], axis=1
    )
    small = jnp.pad(small, ((0, 0), (0, 128 - small.shape[1])))
    dense_grads = jnp.concatenate([grad_qkv, grad_wout, small], axis=1)
    dense_share = shard_reduce_scatter(dense_grads, "shard", 128 * (dense_grads.shape[1] // 256))
    dense_total = lax.psum(dense_share.astype(jnp.bfloat16), "expert").astype(jnp.float32)
    return (
        output,
        grad_tokens,
        dense_total[:, :qkv_cols],
        dense_total[:, qkv_cols : qkv_cols + width],
        dense_total[:, qkv_cols + width : qkv_cols + width + n_route],
        dense_total[:, qkv_cols + width + n_route],
        dense_total[:, qkv_cols + width + n_route + 1],
        grad_in_share,
        grad_back_share,
    )


def solution(mesh):
    return _mapped(mesh)


def _mapped(mesh):
    return jax.shard_map(
        shards,
        mesh=mesh,
        in_specs=(
            P(("expert", "shard"), None),
            P("expert", "shard"),
            P(("expert", "shard"), None),
            P("shard", None),
            P("shard", None),
            P("shard", None),
            P("shard"),
            P("shard"),
            P("expert", "shard", None),
            P("expert", "shard", None),
            P(("expert", "shard"), None),
        ),
        out_specs=(
            P(("expert", "shard"), None),
            P(("expert", "shard"), None),
            P("shard", None),
            P("shard", None),
            P("shard", None),
            P("shard"),
            P("shard"),
            P("expert", "shard", None),
            P("expert", "shard", None),
        ),
        check_vma=False,
    )
```

```python
import functools

import jax
import numpy as np
import jax.numpy as jnp
from jax import lax
from jax.experimental import pallas as pl
from jax.experimental.pallas import tpu as pltpu
from jax.sharding import PartitionSpec as P

HD = 64
SEQ = 197


EPSILON = 1e-06
ROW_CONTRACT = (((0,), (0,)), ((), ()))
COL_CONTRACT = (((1,), (1,)), ((), ()))


def _image_of(idx, images):
    count = jnp.zeros(idx.shape, jnp.int32)
    for i in range(1, images + 1):
        count = count + (idx >= i * SEQ).astype(jnp.int32)
    return count


def _same_image(size, images):
    rows = lax.broadcasted_iota(jnp.int32, (size, size), 0)
    cols = lax.broadcasted_iota(jnp.int32, (size, size), 1)
    return _image_of(rows, images) == _image_of(cols, images)


def _softmax_masked(qj, k, same):
    s = lax.dot_general(qj, k, COL_CONTRACT, preferred_element_type=jnp.float32) * (HD ** -0.5)
    s = jnp.where(same, s, -jnp.inf)
    top = jnp.max(s, axis=1, keepdims=True)
    e = jnp.exp(s - top)
    return e / jnp.sum(e, axis=1, keepdims=True)


def attn_fwd_kernel(q_ref, k_ref, v_ref, o_ref, *, images):
    R = q_ref.shape[0]
    q = q_ref[...]
    k = k_ref[...]
    v = v_ref[...]
    same = _same_image(R, images)
    lane = lax.broadcasted_iota(jnp.int32, (1, 2 * HD), 1)
    out = jnp.zeros((R, 2 * HD), jnp.float32)
    for j in range(2):
        in_head = (lane >= HD) == (j == 1)
        p = _softmax_masked(jnp.where(in_head, q, jnp.zeros_like(q)), k, same)
        o = jnp.dot(p.astype(jnp.bfloat16), v, preferred_element_type=jnp.float32)
        out = jnp.where(in_head, o, out)
    o_ref[...] = out.astype(o_ref.dtype)


def attn_bwd_kernel(q_ref, k_ref, v_ref, g_ref, dq_ref, dk_ref, dv_ref, *, images):
    R = q_ref.shape[0]
    q = q_ref[...]
    k = k_ref[...]
    v = v_ref[...]
    g = g_ref[...]
    same = _same_image(R, images)
    lane = lax.broadcasted_iota(jnp.int32, (1, 2 * HD), 1)
    dq = jnp.zeros((R, 2 * HD), jnp.float32)
    dk = jnp.zeros((R, 2 * HD), jnp.float32)
    dv = jnp.zeros((R, 2 * HD), jnp.float32)
    for j in range(2):
        in_head = (lane >= HD) == (j == 1)
        p = _softmax_masked(jnp.where(in_head, q, jnp.zeros_like(q)), k, same)
        gj = jnp.where(in_head, g, jnp.zeros_like(g))
        dp = lax.dot_general(gj, v, COL_CONTRACT, preferred_element_type=jnp.float32)
        ds = (p * (dp - jnp.sum(p * dp, axis=1, keepdims=True))).astype(jnp.bfloat16)
        dq_j = jnp.dot(ds, k, preferred_element_type=jnp.float32) * (HD ** -0.5)
        dk_j = lax.dot_general(ds, q, ROW_CONTRACT, preferred_element_type=jnp.float32) * (HD ** -0.5)
        dv_j = lax.dot_general(p.astype(jnp.bfloat16), g, ROW_CONTRACT, preferred_element_type=jnp.float32)
        dq = jnp.where(in_head, dq_j, dq)
        dk = jnp.where(in_head, dk_j, dk)
        dv = jnp.where(in_head, dv_j, dv)
    dq_ref[...] = dq.astype(dq_ref.dtype)
    dk_ref[...] = dk.astype(dk_ref.dtype)
    dv_ref[...] = dv.astype(dv_ref.dtype)


def attention_fwd(projected, images):
    R = projected.shape[0]
    W = projected.shape[1] // 3
    pairs = W // (2 * HD)
    blk = lambda off: pl.BlockSpec((R, 2 * HD), lambda h: (0, off + h))
    return pl.pallas_call(
        functools.partial(attn_fwd_kernel, images=images),
        grid=(pairs,),
        in_specs=[blk(0), blk(pairs), blk(2 * pairs)],
        out_specs=blk(0),
        out_shape=jax.ShapeDtypeStruct((R, W), jnp.bfloat16),
        compiler_params=pltpu.CompilerParams(vmem_limit_bytes=48 * 1024 * 1024),
    )(projected, projected, projected)


def attention_bwd(projected, mixed_grad, images):
    R = projected.shape[0]
    W = projected.shape[1] // 3
    pairs = W // (2 * HD)
    blk = lambda off: pl.BlockSpec((R, 2 * HD), lambda h: (0, off + h))
    out = jax.ShapeDtypeStruct((R, W), jnp.bfloat16)
    return pl.pallas_call(
        functools.partial(attn_bwd_kernel, images=images),
        grid=(pairs,),
        in_specs=[blk(0), blk(pairs), blk(2 * pairs), blk(0)],
        out_specs=[blk(0), blk(0), blk(0)],
        out_shape=[out, out, out],
        compiler_params=pltpu.CompilerParams(vmem_limit_bytes=48 * 1024 * 1024),
    )(projected, projected, projected, mixed_grad)


def _exchange(values, bits_left, bit, axis_name, size, index):
    axis = bits_left.index(bit)
    mine = (index >> bit) & 1
    keep = lax.dynamic_index_in_dim(values, mine, axis, keepdims=False)
    send = lax.dynamic_index_in_dim(values, 1 - mine, axis, keepdims=False)
    pairs = [(i, i ^ (1 << bit)) for i in range(size)]
    got = lax.ppermute(send.astype(jnp.bfloat16), axis_name, pairs)
    return keep + got.astype(jnp.float32), [b for b in bits_left if b != bit]


def shard_reduce_scatter(values, axis_name, split_col):
    size = lax.axis_size(axis_name)
    index = lax.axis_index(axis_name)
    n_bits = size.bit_length() - 1
    block = values.shape[0] // size
    bits = list(range(n_bits - 1, -1, -1))
    values = values.astype(jnp.float32).reshape([2] * n_bits + [block, values.shape[1]])
    values, bits = _exchange(values, bits, 0, axis_name, size, index)
    first, second = values[..., :split_col], values[..., split_col:]
    first_bits, second_bits = list(bits), list(bits)
    for up, down in zip(range(1, n_bits), range(n_bits - 1, 0, -1)):
        first, first_bits = _exchange(first, first_bits, up, axis_name, size, index)
        second, second_bits = _exchange(second, second_bits, down, axis_name, size, index)
    return jnp.concatenate([first, second], axis=-1)


def layer_norm(values, norm_gain):
    row_mean = jnp.mean(values, axis=-1, keepdims=True)
    centered = values - row_mean
    variance = jnp.mean(centered * centered, axis=-1, keepdims=True)
    return centered * lax.rsqrt(variance + EPSILON) * norm_gain


def normalize_rows(scores):
    row_top = jnp.max(scores, axis=-1, keepdims=True)
    exp_scores = jnp.exp(scores - row_top)
    return exp_scores / jnp.sum(exp_scores, axis=-1, keepdims=True)


def gelu_parts(values):
    sqrt_half = np.float32(np.sqrt(0.5))
    tail = lax.erfc(-values * sqrt_half)
    density = jnp.exp(-0.5 * values * values) * np.float32(1.0 / np.sqrt(2.0 * np.pi))
    return 0.5 * values * tail, 0.5 * tail + values * density


def shards(
    tokens,
    image_counts,
    routes,
    w_qkv,
    w_out,
    w_router,
    gain_attn,
    gain_moe,
    w_in,
    w_back,
    cotangent,
):
    rows, width = tokens.shape
    experts = lax.axis_size("expert")
    capacity = 8 * (5 * rows // (16 * experts)) + 8
    overflow = experts * capacity
    images = rows // SEQ
    qkv_cols = w_qkv.shape[1]
    n_route = w_router.shape[1]
    ff = w_in.shape[2]
    row_ids = jnp.arange(rows, dtype=jnp.int32)
    live_int = (row_ids // SEQ < image_counts[0, 0]).astype(jnp.int32)
    live_rows = live_int.astype(jnp.float32)

    dense_local = jnp.concatenate(
        [w_qkv, w_out, w_router, gain_attn[:, None], gain_moe[:, None]], axis=1
    )
    dense_full = lax.all_gather(dense_local, "shard", axis=0, tiled=True)
    full_qkv = dense_full[:, :qkv_cols]
    full_out = dense_full[:, qkv_cols : qkv_cols + width]
    full_router = dense_full[:, qkv_cols + width : qkv_cols + width + n_route]
    gain_one = dense_full[:, -2].astype(jnp.float32)
    gain_two = dense_full[:, -1].astype(jnp.float32)

    back_rows = w_back.shape[1]
    expert_local = jnp.stack(
        [w_in[0], w_back[0].reshape(back_rows * width // ff, ff)], axis=0
    )
    expert_full = lax.all_gather(expert_local, "shard", axis=1, tiled=True)
    expert_first = expert_full[0]
    expert_second = expert_full[1].reshape(ff, width)

    token_f = tokens.astype(jnp.float32)
    attn_in = lax.optimization_barrier(layer_norm(token_f, gain_one).astype(jnp.bfloat16))
    projected = jnp.dot(attn_in, full_qkv, preferred_element_type=jnp.float32).astype(jnp.bfloat16)
    pad_rows = -(-rows // 128) * 128
    projected_pad = jnp.pad(projected, ((0, pad_rows - rows), (0, 0)))
    mixed_rows = attention_fwd(projected_pad, images)[:rows]
    hidden_state = token_f + jnp.dot(mixed_rows, full_out, preferred_element_type=jnp.float32)
    moe_in = layer_norm(hidden_state, gain_two).astype(jnp.bfloat16)
    logits = jnp.dot(moe_in, full_router, preferred_element_type=jnp.float32)
    router_probs = normalize_rows(logits)
    expert_ids = jnp.arange(experts, dtype=jnp.int32)
    choose = (routes[:, :, None] == expert_ids).astype(jnp.float32)
    chosen = jnp.sum(choose * router_probs[:, None, :], axis=2)
    pick_table = (routes[:, :, None] == expert_ids).astype(jnp.int32) * live_int[:, None, None]
    flat_picks = pick_table.reshape(rows * 2, experts)
    before = jnp.cumsum(flat_picks, axis=0) - flat_picks
    slot_index = jnp.sum(before * flat_picks, axis=1).reshape(rows, 2)
    position = jnp.where(live_int[:, None] > 0, routes * capacity + slot_index, overflow)

    n_chunks = 2
    part_cap = 8 * ((capacity + 8 * n_chunks - 1) // (8 * n_chunks))
    chunk_sizes = [min(part_cap, capacity - k * part_cap) for k in range(n_chunks)]
    chunk_sizes = [size for size in chunk_sizes if size > 0]
    chunk_starts = [sum(chunk_sizes[:k]) for k in range(len(chunk_sizes))]
    slot_ids = jnp.concatenate(
        [
            (
                jnp.arange(experts, dtype=jnp.int32)[:, None] * capacity
                + start
                + jnp.arange(size, dtype=jnp.int32)[None, :]
            ).reshape(-1)
            for start, size in zip(chunk_starts, chunk_sizes)
        ]
    )[:, None]
    take_first = (slot_ids == position[None, :, 0]).astype(jnp.bfloat16)
    take_second = (slot_ids == position[None, :, 1]).astype(jnp.bfloat16)

    grad_out = cotangent.astype(jnp.float32) * live_rows[:, None]
    weighted = chosen * live_rows[:, None]
    grad_picked = (weighted[:, :, None] * grad_out[:, None, :]).astype(jnp.bfloat16)

    def dispatch_rows(low, high):
        first = take_first[low:high]
        second = take_second[low:high]
        sent_rows = jnp.dot(first + second, moe_in, preferred_element_type=jnp.float32)
        sent_grad = jnp.dot(
            first, grad_picked[:, 0], preferred_element_type=jnp.float32
        ) + jnp.dot(second, grad_picked[:, 1], preferred_element_type=jnp.float32)
        return jnp.concatenate([sent_rows, sent_grad], axis=1).astype(jnp.bfloat16)

    grad_first = None
    grad_second = None
    returned_parts = []
    for start, size in zip(chunk_starts, chunk_sizes):
        arrived = lax.all_to_all(
            dispatch_rows(experts * start, experts * (start + size)).reshape(
                experts, size, 2 * width
            ),
            "expert",
            split_axis=0,
            concat_axis=0,
            tiled=True,
        ).reshape(experts * size, 2 * width)
        flat_arrived = arrived[:, :width]
        flat_grad = arrived[:, width:]
        hidden_grad = lax.dot_general(
            flat_grad, expert_second, COL_CONTRACT, preferred_element_type=jnp.float32
        )
        pre_act = jnp.dot(flat_arrived, expert_first, preferred_element_type=jnp.float32)
        activated, slope = gelu_parts(pre_act)
        activated = activated.astype(jnp.bfloat16)
        pre_grad = (hidden_grad * slope).astype(jnp.bfloat16)
        produced = jnp.dot(
            activated, expert_second, preferred_element_type=jnp.float32
        ).astype(jnp.bfloat16)
        row_grad = lax.dot_general(
            pre_grad, expert_first, COL_CONTRACT, preferred_element_type=jnp.float32
        ).astype(jnp.bfloat16)
        part_second = lax.dot_general(
            activated, flat_grad, ROW_CONTRACT, preferred_element_type=jnp.float32
        )
        part_first = lax.dot_general(
            flat_arrived, pre_grad, ROW_CONTRACT, preferred_element_type=jnp.float32
        )
        grad_first = part_first if grad_first is None else grad_first + part_first
        grad_second = part_second if grad_second is None else grad_second + part_second
        returning = jnp.concatenate([produced, row_grad], axis=1).reshape(
            experts, size, 2 * width
        )
        returned_parts.append(
            lax.all_to_all(returning, "expert", split_axis=0, concat_axis=0, tiled=True)
        )

    expert_grads = jnp.stack(
        [grad_first, grad_second.reshape(width, ff)], axis=0
    ).astype(jnp.bfloat16)
    expert_share = lax.psum_scatter(expert_grads, "shard", scatter_dimension=1, tiled=True)
    expert_share = expert_share.astype(jnp.float32)
    grad_in_share = expert_share[0][None]
    grad_back_share = expert_share[1].reshape(back_rows, width)[None]

    picked_first = None
    picked_second = None
    for start, size, part in zip(chunk_starts, chunk_sizes, returned_parts):
        low, high = experts * start, experts * (start + size)
        part = part.reshape(-1, 2 * width)
        part_first = lax.dot_general(
            take_first[low:high], part, ROW_CONTRACT, preferred_element_type=jnp.float32
        )
        part_second = lax.dot_general(
            take_second[low:high], part, ROW_CONTRACT, preferred_element_type=jnp.float32
        )
        picked_first = part_first if picked_first is None else picked_first + part_first
        picked_second = part_second if picked_second is None else picked_second + part_second
    moe_out = (
        weighted[:, 0:1] * picked_first[:, :width] + weighted[:, 1:2] * picked_second[:, :width]
    )
    output = (live_rows[:, None] * (hidden_state + moe_out)).astype(jnp.bfloat16)
    grad_chosen = jnp.stack(
        [
            jnp.sum(grad_out * picked_first[:, :width], axis=1),
            jnp.sum(grad_out * picked_second[:, :width], axis=1),
        ],
        axis=1,
    ) * live_rows[:, None]
    expert_part = (picked_first[:, width:] + picked_second[:, width:]) * live_rows[:, None]
    prob_sum = jnp.sum(choose * grad_chosen[:, :, None], axis=1)
    logit_grad = (
        router_probs * (prob_sum - jnp.sum(router_probs * prob_sum, axis=-1, keepdims=True))
    ).astype(jnp.bfloat16)
    grad_router = lax.dot_general(
        moe_in, logit_grad, ROW_CONTRACT, preferred_element_type=jnp.float32
    )
    moe_in_grad = expert_part + lax.dot_general(
        logit_grad, full_router, COL_CONTRACT, preferred_element_type=jnp.float32
    )
    _, norm_back = jax.vjp(layer_norm, hidden_state, gain_two)
    state_part, grad_gain_two = norm_back(moe_in_grad)
    state_grad = grad_out + state_part
    branch_grad = state_grad.astype(jnp.bfloat16)
    grad_wout = lax.dot_general(
        mixed_rows, branch_grad, ROW_CONTRACT, preferred_element_type=jnp.float32
    )
    mixed_grad = lax.dot_general(
        branch_grad, full_out, COL_CONTRACT, preferred_element_type=jnp.float32
    )
    mixed_grad = jnp.pad(mixed_grad.astype(jnp.bfloat16), ((0, pad_rows - rows), (0, 0)))
    grad_q, grad_k, grad_v = attention_bwd(projected_pad, mixed_grad, images)
    projected_grad = jnp.concatenate([grad_q, grad_k, grad_v], axis=1)
    attn_in_pad = jnp.pad(attn_in, ((0, pad_rows - rows), (0, 0)))
    grad_qkv = lax.dot_general(
        attn_in_pad, projected_grad, ROW_CONTRACT, preferred_element_type=jnp.float32
    )
    attn_in_grad = lax.dot_general(
        projected_grad[:rows], full_qkv, COL_CONTRACT, preferred_element_type=jnp.float32
    )
    _, first_back = jax.vjp(layer_norm, token_f, gain_one)
    token_part, grad_gain_one = first_back(attn_in_grad)
    grad_tokens = (state_grad + token_part).astype(jnp.bfloat16)

    small = jnp.concatenate(
        [grad_router, grad_gain_one[:, None], grad_gain_two[:, None]], axis=1
    )
    small = jnp.pad(small, ((0, 0), (0, 128 - small.shape[1])))
    dense_grads = jnp.concatenate([grad_qkv, grad_wout, small], axis=1)
    dense_share = shard_reduce_scatter(dense_grads, "shard", 128 * (dense_grads.shape[1] // 256))
    dense_total = lax.psum(dense_share.astype(jnp.bfloat16), "expert").astype(jnp.float32)
    return (
        output,
        grad_tokens,
        dense_total[:, :qkv_cols],
        dense_total[:, qkv_cols : qkv_cols + width],
        dense_total[:, qkv_cols + width : qkv_cols + width + n_route],
        dense_total[:, qkv_cols + width + n_route],
        dense_total[:, qkv_cols + width + n_route + 1],
        grad_in_share,
        grad_back_share,
    )


def solution(mesh):
    return _mapped(mesh)


def _mapped(mesh):
    return jax.shard_map(
        shards,
        mesh=mesh,
        in_specs=(
            P(("expert", "shard"), None),
            P("expert", "shard"),
            P(("expert", "shard"), None),
            P("shard", None),
            P("shard", None),
            P("shard", None),
            P("shard"),
            P("shard"),
            P("expert", "shard", None),
            P("expert", "shard", None),
            P(("expert", "shard"), None),
        ),
        out_specs=(
            P(("expert", "shard"), None),
            P(("expert", "shard"), None),
            P("shard", None),
            P("shard", None),
            P("shard", None),
            P("shard"),
            P("shard"),
            P("expert", "shard", None),
            P("expert", "shard", None),
        ),
        check_vma=False,
    )
```

```python
import functools

import jax
import numpy as np
import jax.numpy as jnp
from jax import lax
from jax.experimental import pallas as pl
from jax.experimental.pallas import tpu as pltpu
from jax.sharding import PartitionSpec as P

HD = 64
SEQ = 197


EPSILON = 1e-06
ROW_CONTRACT = (((0,), (0,)), ((), ()))
COL_CONTRACT = (((1,), (1,)), ((), ()))


def _image_of(idx, images):
    count = jnp.zeros(idx.shape, jnp.int32)
    for i in range(1, images + 1):
        count = count + (idx >= i * SEQ).astype(jnp.int32)
    return count


def _same_image(size, images):
    rows = lax.broadcasted_iota(jnp.int32, (size, size), 0)
    cols = lax.broadcasted_iota(jnp.int32, (size, size), 1)
    return _image_of(rows, images) == _image_of(cols, images)


def _softmax_masked(qj, k, same):
    s = lax.dot_general(qj, k, COL_CONTRACT, preferred_element_type=jnp.float32) * (HD ** -0.5)
    s = jnp.where(same, s, -jnp.inf)
    top = jnp.max(s, axis=1, keepdims=True)
    e = jnp.exp(s - top)
    return e / jnp.sum(e, axis=1, keepdims=True)


def attn_fwd_kernel(q_ref, k_ref, v_ref, o_ref, *, images):
    R = q_ref.shape[0]
    q = q_ref[...]
    k = k_ref[...]
    v = v_ref[...]
    same = _same_image(R, images)
    lane = lax.broadcasted_iota(jnp.int32, (1, 2 * HD), 1)
    out = jnp.zeros((R, 2 * HD), jnp.float32)
    for j in range(2):
        in_head = (lane >= HD) == (j == 1)
        p = _softmax_masked(jnp.where(in_head, q, jnp.zeros_like(q)), k, same)
        o = jnp.dot(p.astype(jnp.bfloat16), v, preferred_element_type=jnp.float32)
        out = jnp.where(in_head, o, out)
    o_ref[...] = out.astype(o_ref.dtype)


def attn_bwd_kernel(q_ref, k_ref, v_ref, g_ref, dq_ref, dk_ref, dv_ref, *, images):
    R = q_ref.shape[0]
    q = q_ref[...]
    k = k_ref[...]
    v = v_ref[...]
    g = g_ref[...]
    same = _same_image(R, images)
    lane = lax.broadcasted_iota(jnp.int32, (1, 2 * HD), 1)
    dq = jnp.zeros((R, 2 * HD), jnp.float32)
    dk = jnp.zeros((R, 2 * HD), jnp.float32)
    dv = jnp.zeros((R, 2 * HD), jnp.float32)
    for j in range(2):
        in_head = (lane >= HD) == (j == 1)
        p = _softmax_masked(jnp.where(in_head, q, jnp.zeros_like(q)), k, same)
        gj = jnp.where(in_head, g, jnp.zeros_like(g))
        dp = lax.dot_general(gj, v, COL_CONTRACT, preferred_element_type=jnp.float32)
        ds = (p * (dp - jnp.sum(p * dp, axis=1, keepdims=True))).astype(jnp.bfloat16)
        dq_j = jnp.dot(ds, k, preferred_element_type=jnp.float32) * (HD ** -0.5)
        dk_j = lax.dot_general(ds, q, ROW_CONTRACT, preferred_element_type=jnp.float32) * (HD ** -0.5)
        dv_j = lax.dot_general(p.astype(jnp.bfloat16), g, ROW_CONTRACT, preferred_element_type=jnp.float32)
        dq = jnp.where(in_head, dq_j, dq)
        dk = jnp.where(in_head, dk_j, dk)
        dv = jnp.where(in_head, dv_j, dv)
    dq_ref[...] = dq.astype(dq_ref.dtype)
    dk_ref[...] = dk.astype(dk_ref.dtype)
    dv_ref[...] = dv.astype(dv_ref.dtype)


def attention_fwd(projected, images):
    R = projected.shape[0]
    W = projected.shape[1] // 3
    pairs = W // (2 * HD)
    blk = lambda off: pl.BlockSpec((R, 2 * HD), lambda h: (0, off + h))
    return pl.pallas_call(
        functools.partial(attn_fwd_kernel, images=images),
        grid=(pairs,),
        in_specs=[blk(0), blk(pairs), blk(2 * pairs)],
        out_specs=blk(0),
        out_shape=jax.ShapeDtypeStruct((R, W), jnp.bfloat16),
        compiler_params=pltpu.CompilerParams(vmem_limit_bytes=48 * 1024 * 1024),
    )(projected, projected, projected)


def attention_bwd(projected, mixed_grad, images):
    R = projected.shape[0]
    W = projected.shape[1] // 3
    pairs = W // (2 * HD)
    blk = lambda off: pl.BlockSpec((R, 2 * HD), lambda h: (0, off + h))
    out = jax.ShapeDtypeStruct((R, W), jnp.bfloat16)
    return pl.pallas_call(
        functools.partial(attn_bwd_kernel, images=images),
        grid=(pairs,),
        in_specs=[blk(0), blk(pairs), blk(2 * pairs), blk(0)],
        out_specs=[blk(0), blk(0), blk(0)],
        out_shape=[out, out, out],
        compiler_params=pltpu.CompilerParams(vmem_limit_bytes=48 * 1024 * 1024),
    )(projected, projected, projected, mixed_grad)


def _exchange(values, bits_left, bit, axis_name, size, index):
    axis = bits_left.index(bit)
    mine = (index >> bit) & 1
    keep = lax.dynamic_index_in_dim(values, mine, axis, keepdims=False)
    send = lax.dynamic_index_in_dim(values, 1 - mine, axis, keepdims=False)
    pairs = [(i, i ^ (1 << bit)) for i in range(size)]
    got = lax.ppermute(send.astype(jnp.bfloat16), axis_name, pairs)
    return keep + got.astype(jnp.float32), [b for b in bits_left if b != bit]


def shard_reduce_scatter(values, axis_name, split_col):
    size = lax.axis_size(axis_name)
    index = lax.axis_index(axis_name)
    n_bits = size.bit_length() - 1
    block = values.shape[0] // size
    bits = list(range(n_bits - 1, -1, -1))
    values = values.astype(jnp.float32).reshape([2] * n_bits + [block, values.shape[1]])
    values, bits = _exchange(values, bits, 0, axis_name, size, index)
    first, second = values[..., :split_col], values[..., split_col:]
    first_bits, second_bits = list(bits), list(bits)
    for up, down in zip(range(1, n_bits), range(n_bits - 1, 0, -1)):
        first, first_bits = _exchange(first, first_bits, up, axis_name, size, index)
        second, second_bits = _exchange(second, second_bits, down, axis_name, size, index)
    return jnp.concatenate([first, second], axis=-1)


def layer_norm(values, norm_gain):
    row_mean = jnp.mean(values, axis=-1, keepdims=True)
    centered = values - row_mean
    variance = jnp.mean(centered * centered, axis=-1, keepdims=True)
    return centered * lax.rsqrt(variance + EPSILON) * norm_gain


def normalize_rows(scores):
    row_top = jnp.max(scores, axis=-1, keepdims=True)
    exp_scores = jnp.exp(scores - row_top)
    return exp_scores / jnp.sum(exp_scores, axis=-1, keepdims=True)


def gelu_parts(values):
    sqrt_half = np.float32(np.sqrt(0.5))
    tail = lax.erfc(-values * sqrt_half)
    density = jnp.exp(-0.5 * values * values) * np.float32(1.0 / np.sqrt(2.0 * np.pi))
    return 0.5 * values * tail, 0.5 * tail + values * density


def shards(
    tokens,
    image_counts,
    routes,
    w_qkv,
    w_out,
    w_router,
    gain_attn,
    gain_moe,
    w_in,
    w_back,
    cotangent,
):
    rows, width = tokens.shape
    experts = lax.axis_size("expert")
    capacity = 8 * (5 * rows // (16 * experts)) + 8
    overflow = experts * capacity
    images = rows // SEQ
    qkv_cols = w_qkv.shape[1]
    n_route = w_router.shape[1]
    ff = w_in.shape[2]
    row_ids = jnp.arange(rows, dtype=jnp.int32)
    live_int = (row_ids // SEQ < image_counts[0, 0]).astype(jnp.int32)
    live_rows = live_int.astype(jnp.float32)

    dense_local = jnp.concatenate(
        [w_qkv, w_out, w_router, gain_attn[:, None], gain_moe[:, None]], axis=1
    )
    dense_full = lax.all_gather(dense_local, "shard", axis=0, tiled=True)
    full_qkv = dense_full[:, :qkv_cols]
    full_out = dense_full[:, qkv_cols : qkv_cols + width]
    full_router = dense_full[:, qkv_cols + width : qkv_cols + width + n_route]
    gain_one = dense_full[:, -2].astype(jnp.float32)
    gain_two = dense_full[:, -1].astype(jnp.float32)

    back_rows = w_back.shape[1]
    expert_local = jnp.stack(
        [w_in[0], w_back[0].reshape(back_rows * width // ff, ff)], axis=0
    )
    expert_full = lax.all_gather(expert_local, "shard", axis=1, tiled=True)
    expert_first = expert_full[0]
    expert_second = expert_full[1].reshape(ff, width)

    token_f = tokens.astype(jnp.float32)
    attn_in = lax.optimization_barrier(layer_norm(token_f, gain_one).astype(jnp.bfloat16))
    projected = jnp.dot(attn_in, full_qkv, preferred_element_type=jnp.float32).astype(jnp.bfloat16)
    pad_rows = -(-rows // 128) * 128
    projected_pad = jnp.pad(projected, ((0, pad_rows - rows), (0, 0)))
    mixed_rows = attention_fwd(projected_pad, images)[:rows]
    hidden_state = token_f + jnp.dot(mixed_rows, full_out, preferred_element_type=jnp.float32)
    moe_in = layer_norm(hidden_state, gain_two).astype(jnp.bfloat16)
    logits = jnp.dot(moe_in, full_router, preferred_element_type=jnp.float32)
    router_probs = normalize_rows(logits)
    expert_ids = jnp.arange(experts, dtype=jnp.int32)
    choose = (routes[:, :, None] == expert_ids).astype(jnp.float32)
    chosen = jnp.sum(choose * router_probs[:, None, :], axis=2)
    pick_table = (routes[:, :, None] == expert_ids).astype(jnp.int32) * live_int[:, None, None]
    flat_picks = pick_table.reshape(rows * 2, experts)
    before = jnp.cumsum(flat_picks, axis=0) - flat_picks
    slot_index = jnp.sum(before * flat_picks, axis=1).reshape(rows, 2)
    position = jnp.where(live_int[:, None] > 0, routes * capacity + slot_index, overflow)

    n_chunks = 2
    part_cap = 8 * ((capacity + 8 * n_chunks - 1) // (8 * n_chunks))
    chunk_sizes = [min(part_cap, capacity - k * part_cap) for k in range(n_chunks)]
    chunk_sizes = [size for size in chunk_sizes if size > 0]
    chunk_starts = [sum(chunk_sizes[:k]) for k in range(len(chunk_sizes))]
    slot_ids = jnp.concatenate(
        [
            (
                jnp.arange(experts, dtype=jnp.int32)[:, None] * capacity
                + start
                + jnp.arange(size, dtype=jnp.int32)[None, :]
            ).reshape(-1)
            for start, size in zip(chunk_starts, chunk_sizes)
        ]
    )[:, None]
    take_first = (slot_ids == position[None, :, 0]).astype(jnp.bfloat16)
    take_second = (slot_ids == position[None, :, 1]).astype(jnp.bfloat16)

    grad_out = cotangent.astype(jnp.float32) * live_rows[:, None]
    weighted = chosen * live_rows[:, None]
    grad_picked = (weighted[:, :, None] * grad_out[:, None, :]).astype(jnp.bfloat16)

    def dispatch_rows(low, high):
        first = take_first[low:high]
        second = take_second[low:high]
        sent_rows = jnp.dot(first + second, moe_in, preferred_element_type=jnp.float32)
        sent_grad = jnp.dot(
            first, grad_picked[:, 0], preferred_element_type=jnp.float32
        ) + jnp.dot(second, grad_picked[:, 1], preferred_element_type=jnp.float32)
        return jnp.concatenate([sent_rows, sent_grad], axis=1).astype(jnp.bfloat16)

    grad_first = None
    grad_second = None
    returned_parts = []
    for start, size in zip(chunk_starts, chunk_sizes):
        arrived = lax.all_to_all(
            dispatch_rows(experts * start, experts * (start + size)).reshape(
                experts, size, 2 * width
            ),
            "expert",
            split_axis=0,
            concat_axis=0,
            tiled=True,
        ).reshape(experts * size, 2 * width)
        flat_arrived = arrived[:, :width]
        flat_grad = arrived[:, width:]
        hidden_grad = lax.dot_general(
            flat_grad, expert_second, COL_CONTRACT, preferred_element_type=jnp.float32
        )
        pre_act = jnp.dot(flat_arrived, expert_first, preferred_element_type=jnp.float32)
        activated, slope = gelu_parts(pre_act)
        activated = activated.astype(jnp.bfloat16)
        pre_grad = (hidden_grad * slope).astype(jnp.bfloat16)
        produced = jnp.dot(
            activated, expert_second, preferred_element_type=jnp.float32
        ).astype(jnp.bfloat16)
        row_grad = lax.dot_general(
            pre_grad, expert_first, COL_CONTRACT, preferred_element_type=jnp.float32
        ).astype(jnp.bfloat16)
        part_second = lax.dot_general(
            activated, flat_grad, ROW_CONTRACT, preferred_element_type=jnp.float32
        )
        part_first = lax.dot_general(
            flat_arrived, pre_grad, ROW_CONTRACT, preferred_element_type=jnp.float32
        )
        grad_first = part_first if grad_first is None else grad_first + part_first
        grad_second = part_second if grad_second is None else grad_second + part_second
        returning = jnp.concatenate([produced, row_grad], axis=1).reshape(
            experts, size, 2 * width
        )
        returned_parts.append(
            lax.all_to_all(returning, "expert", split_axis=0, concat_axis=0, tiled=True)
        )

    in_share = lax.psum_scatter(
        grad_first.astype(jnp.bfloat16), "shard", scatter_dimension=0, tiled=True
    )
    back_share = lax.psum_scatter(
        grad_second.astype(jnp.bfloat16), "shard", scatter_dimension=0, tiled=True
    )
    grad_in_share = in_share.astype(jnp.float32)[None]
    grad_back_share = back_share.astype(jnp.float32)[None]

    picked_first = None
    picked_second = None
    for start, size, part in zip(chunk_starts, chunk_sizes, returned_parts):
        low, high = experts * start, experts * (start + size)
        part = part.reshape(-1, 2 * width)
        part_first = lax.dot_general(
            take_first[low:high], part, ROW_CONTRACT, preferred_element_type=jnp.float32
        )
        part_second = lax.dot_general(
            take_second[low:high], part, ROW_CONTRACT, preferred_element_type=jnp.float32
        )
        picked_first = part_first if picked_first is None else picked_first + part_first
        picked_second = part_second if picked_second is None else picked_second + part_second
    moe_out = (
        weighted[:, 0:1] * picked_first[:, :width] + weighted[:, 1:2] * picked_second[:, :width]
    )
    output = (live_rows[:, None] * (hidden_state + moe_out)).astype(jnp.bfloat16)
    grad_chosen = jnp.stack(
        [
            jnp.sum(grad_out * picked_first[:, :width], axis=1),
            jnp.sum(grad_out * picked_second[:, :width], axis=1),
        ],
        axis=1,
    ) * live_rows[:, None]
    expert_part = (picked_first[:, width:] + picked_second[:, width:]) * live_rows[:, None]
    prob_sum = jnp.sum(choose * grad_chosen[:, :, None], axis=1)
    logit_grad = (
        router_probs * (prob_sum - jnp.sum(router_probs * prob_sum, axis=-1, keepdims=True))
    ).astype(jnp.bfloat16)
    grad_router = lax.dot_general(
        moe_in, logit_grad, ROW_CONTRACT, preferred_element_type=jnp.float32
    )
    moe_in_grad = expert_part + lax.dot_general(
        logit_grad, full_router, COL_CONTRACT, preferred_element_type=jnp.float32
    )
    _, norm_back = jax.vjp(layer_norm, hidden_state, gain_two)
    state_part, grad_gain_two = norm_back(moe_in_grad)
    state_grad = grad_out + state_part
    branch_grad = state_grad.astype(jnp.bfloat16)
    grad_wout = lax.dot_general(
        mixed_rows, branch_grad, ROW_CONTRACT, preferred_element_type=jnp.float32
    )
    mixed_grad = lax.dot_general(
        branch_grad, full_out, COL_CONTRACT, preferred_element_type=jnp.float32
    )
    mixed_grad = jnp.pad(mixed_grad.astype(jnp.bfloat16), ((0, pad_rows - rows), (0, 0)))
    grad_q, grad_k, grad_v = attention_bwd(projected_pad, mixed_grad, images)
    projected_grad = jnp.concatenate([grad_q, grad_k, grad_v], axis=1)
    attn_in_pad = jnp.pad(attn_in, ((0, pad_rows - rows), (0, 0)))
    grad_qkv = lax.dot_general(
        attn_in_pad, projected_grad, ROW_CONTRACT, preferred_element_type=jnp.float32
    )
    attn_in_grad = lax.dot_general(
        projected_grad[:rows], full_qkv, COL_CONTRACT, preferred_element_type=jnp.float32
    )
    _, first_back = jax.vjp(layer_norm, token_f, gain_one)
    token_part, grad_gain_one = first_back(attn_in_grad)
    grad_tokens = (state_grad + token_part).astype(jnp.bfloat16)

    small = jnp.concatenate(
        [grad_router, grad_gain_one[:, None], grad_gain_two[:, None]], axis=1
    )
    small = jnp.pad(small, ((0, 0), (0, 128 - small.shape[1])))
    dense_grads = jnp.concatenate([grad_qkv, grad_wout, small], axis=1)
    dense_share = shard_reduce_scatter(dense_grads, "shard", 128 * (dense_grads.shape[1] // 256))
    dense_total = lax.psum(dense_share.astype(jnp.bfloat16), "expert").astype(jnp.float32)
    return (
        output,
        grad_tokens,
        dense_total[:, :qkv_cols],
        dense_total[:, qkv_cols : qkv_cols + width],
        dense_total[:, qkv_cols + width : qkv_cols + width + n_route],
        dense_total[:, qkv_cols + width + n_route],
        dense_total[:, qkv_cols + width + n_route + 1],
        grad_in_share,
        grad_back_share,
    )


def solution(mesh):
    return _mapped(mesh)


def _mapped(mesh):
    return jax.shard_map(
        shards,
        mesh=mesh,
        in_specs=(
            P(("expert", "shard"), None),
            P("expert", "shard"),
            P(("expert", "shard"), None),
            P("shard", None),
            P("shard", None),
            P("shard", None),
            P("shard"),
            P("shard"),
            P("expert", "shard", None),
            P("expert", "shard", None),
            P(("expert", "shard"), None),
        ),
        out_specs=(
            P(("expert", "shard"), None),
            P(("expert", "shard"), None),
            P("shard", None),
            P("shard", None),
            P("shard", None),
            P("shard"),
            P("shard"),
            P("expert", "shard", None),
            P("expert", "shard", None),
        ),
        check_vma=False,
    )
```

```python
import functools

import jax
import numpy as np
import jax.numpy as jnp
from jax import lax
from jax.experimental import pallas as pl
from jax.experimental.pallas import tpu as pltpu
from jax.sharding import PartitionSpec as P

HD = 64
SEQ = 197


EPSILON = 1e-06
ROW_CONTRACT = (((0,), (0,)), ((), ()))
COL_CONTRACT = (((1,), (1,)), ((), ()))


def _image_of(idx, images):
    count = jnp.zeros(idx.shape, jnp.int32)
    for i in range(1, images + 1):
        count = count + (idx >= i * SEQ).astype(jnp.int32)
    return count


def _same_image(size, images):
    rows = lax.broadcasted_iota(jnp.int32, (size, size), 0)
    cols = lax.broadcasted_iota(jnp.int32, (size, size), 1)
    return _image_of(rows, images) == _image_of(cols, images)


def _softmax_masked(qj, k, same):
    s = lax.dot_general(qj, k, COL_CONTRACT, preferred_element_type=jnp.float32) * (HD ** -0.5)
    s = jnp.where(same, s, -jnp.inf)
    top = jnp.max(s, axis=1, keepdims=True)
    e = jnp.exp(s - top)
    return e / jnp.sum(e, axis=1, keepdims=True)


def _two_heads(values, lane):
    zero = jnp.zeros_like(values)
    return jnp.concatenate(
        [jnp.where(lane < HD, values, zero), jnp.where(lane >= HD, values, zero)], axis=0
    )


def _pick_heads(stacked, lane, rows):
    return jnp.where(lane < HD, stacked[:rows], stacked[rows:])


def attn_fwd_kernel(q_ref, k_ref, v_ref, o_ref, *, images):
    R = q_ref.shape[0]
    same = _same_image(R, images)
    same = jnp.concatenate([same, same], axis=0)
    lane = lax.broadcasted_iota(jnp.int32, (1, 2 * HD), 1)
    p = _softmax_masked(_two_heads(q_ref[...], lane), k_ref[...], same)
    o = jnp.dot(p.astype(jnp.bfloat16), v_ref[...], preferred_element_type=jnp.float32)
    o_ref[...] = _pick_heads(o, lane, R).astype(o_ref.dtype)


def attn_bwd_kernel(q_ref, k_ref, v_ref, g_ref, dq_ref, dk_ref, dv_ref, *, images):
    R = q_ref.shape[0]
    k = k_ref[...]
    v = v_ref[...]
    same = _same_image(R, images)
    same = jnp.concatenate([same, same], axis=0)
    lane = lax.broadcasted_iota(jnp.int32, (1, 2 * HD), 1)
    q2 = _two_heads(q_ref[...], lane)
    g2 = _two_heads(g_ref[...], lane)
    p = _softmax_masked(q2, k, same)
    dp = lax.dot_general(g2, v, COL_CONTRACT, preferred_element_type=jnp.float32)
    ds = (p * (dp - jnp.sum(p * dp, axis=1, keepdims=True))).astype(jnp.bfloat16)
    dq = jnp.dot(ds, k, preferred_element_type=jnp.float32) * (HD ** -0.5)
    dk = lax.dot_general(ds, q2, ROW_CONTRACT, preferred_element_type=jnp.float32) * (HD ** -0.5)
    dv = lax.dot_general(p.astype(jnp.bfloat16), g2, ROW_CONTRACT, preferred_element_type=jnp.float32)
    dq_ref[...] = _pick_heads(dq, lane, R).astype(dq_ref.dtype)
    dk_ref[...] = dk.astype(dk_ref.dtype)
    dv_ref[...] = dv.astype(dv_ref.dtype)


def attention_fwd(projected, images):
    R = projected.shape[0]
    W = projected.shape[1] // 3
    pairs = W // (2 * HD)
    blk = lambda off: pl.BlockSpec((R, 2 * HD), lambda h: (0, off + h))
    return pl.pallas_call(
        functools.partial(attn_fwd_kernel, images=images),
        grid=(pairs,),
        in_specs=[blk(0), blk(pairs), blk(2 * pairs)],
        out_specs=blk(0),
        out_shape=jax.ShapeDtypeStruct((R, W), jnp.bfloat16),
        compiler_params=pltpu.CompilerParams(vmem_limit_bytes=48 * 1024 * 1024),
    )(projected, projected, projected)


def attention_bwd(projected, mixed_grad, images):
    R = projected.shape[0]
    W = projected.shape[1] // 3
    pairs = W // (2 * HD)
    blk = lambda off: pl.BlockSpec((R, 2 * HD), lambda h: (0, off + h))
    out = jax.ShapeDtypeStruct((R, W), jnp.bfloat16)
    return pl.pallas_call(
        functools.partial(attn_bwd_kernel, images=images),
        grid=(pairs,),
        in_specs=[blk(0), blk(pairs), blk(2 * pairs), blk(0)],
        out_specs=[blk(0), blk(0), blk(0)],
        out_shape=[out, out, out],
        compiler_params=pltpu.CompilerParams(vmem_limit_bytes=48 * 1024 * 1024),
    )(projected, projected, projected, mixed_grad)


def _exchange(values, bits_left, bit, axis_name, size, index):
    axis = bits_left.index(bit)
    mine = (index >> bit) & 1
    keep = lax.dynamic_index_in_dim(values, mine, axis, keepdims=False)
    send = lax.dynamic_index_in_dim(values, 1 - mine, axis, keepdims=False)
    pairs = [(i, i ^ (1 << bit)) for i in range(size)]
    got = lax.ppermute(send.astype(jnp.bfloat16), axis_name, pairs)
    return keep + got.astype(jnp.float32), [b for b in bits_left if b != bit]


def shard_reduce_scatter(values, axis_name, split_col):
    size = lax.axis_size(axis_name)
    index = lax.axis_index(axis_name)
    n_bits = size.bit_length() - 1
    block = values.shape[0] // size
    bits = list(range(n_bits - 1, -1, -1))
    values = values.astype(jnp.float32).reshape([2] * n_bits + [block, values.shape[1]])
    values, bits = _exchange(values, bits, 0, axis_name, size, index)
    first, second = values[..., :split_col], values[..., split_col:]
    first_bits, second_bits = list(bits), list(bits)
    for up, down in zip(range(1, n_bits), range(n_bits - 1, 0, -1)):
        first, first_bits = _exchange(first, first_bits, up, axis_name, size, index)
        second, second_bits = _exchange(second, second_bits, down, axis_name, size, index)
    return jnp.concatenate([first, second], axis=-1)


def layer_norm(values, norm_gain):
    row_mean = jnp.mean(values, axis=-1, keepdims=True)
    centered = values - row_mean
    variance = jnp.mean(centered * centered, axis=-1, keepdims=True)
    return centered * lax.rsqrt(variance + EPSILON) * norm_gain


def normalize_rows(scores):
    row_top = jnp.max(scores, axis=-1, keepdims=True)
    exp_scores = jnp.exp(scores - row_top)
    return exp_scores / jnp.sum(exp_scores, axis=-1, keepdims=True)


def gelu_parts(values):
    sqrt_half = np.float32(np.sqrt(0.5))
    tail = lax.erfc(-values * sqrt_half)
    density = jnp.exp(-0.5 * values * values) * np.float32(1.0 / np.sqrt(2.0 * np.pi))
    return 0.5 * values * tail, 0.5 * tail + values * density


def shards(
    tokens,
    image_counts,
    routes,
    w_qkv,
    w_out,
    w_router,
    gain_attn,
    gain_moe,
    w_in,
    w_back,
    cotangent,
):
    rows, width = tokens.shape
    experts = lax.axis_size("expert")
    capacity = 8 * (5 * rows // (16 * experts)) + 8
    overflow = experts * capacity
    images = rows // SEQ
    qkv_cols = w_qkv.shape[1]
    n_route = w_router.shape[1]
    ff = w_in.shape[2]
    row_ids = jnp.arange(rows, dtype=jnp.int32)
    live_int = (row_ids // SEQ < image_counts[0, 0]).astype(jnp.int32)
    live_rows = live_int.astype(jnp.float32)

    dense_local = jnp.concatenate(
        [w_qkv, w_out, w_router, gain_attn[:, None], gain_moe[:, None]], axis=1
    )
    dense_full = lax.all_gather(dense_local, "shard", axis=0, tiled=True)
    full_qkv = dense_full[:, :qkv_cols]
    full_out = dense_full[:, qkv_cols : qkv_cols + width]
    full_router = dense_full[:, qkv_cols + width : qkv_cols + width + n_route]
    gain_one = dense_full[:, -2].astype(jnp.float32)
    gain_two = dense_full[:, -1].astype(jnp.float32)

    back_rows = w_back.shape[1]
    expert_local = jnp.stack(
        [w_in[0], w_back[0].reshape(back_rows * width // ff, ff)], axis=0
    )
    expert_full = lax.all_gather(expert_local, "shard", axis=1, tiled=True)
    expert_first = expert_full[0]
    expert_second = expert_full[1].reshape(ff, width)

    token_f = tokens.astype(jnp.float32)
    attn_in = lax.optimization_barrier(layer_norm(token_f, gain_one).astype(jnp.bfloat16))
    projected = jnp.dot(attn_in, full_qkv, preferred_element_type=jnp.float32).astype(jnp.bfloat16)
    pad_rows = -(-rows // 128) * 128
    projected_pad = jnp.pad(projected, ((0, pad_rows - rows), (0, 0)))
    mixed_rows = attention_fwd(projected_pad, images)[:rows]
    hidden_state = token_f + jnp.dot(mixed_rows, full_out, preferred_element_type=jnp.float32)
    moe_in = layer_norm(hidden_state, gain_two).astype(jnp.bfloat16)
    logits = jnp.dot(moe_in, full_router, preferred_element_type=jnp.float32)
    router_probs = normalize_rows(logits)
    expert_ids = jnp.arange(experts, dtype=jnp.int32)
    choose = (routes[:, :, None] == expert_ids).astype(jnp.float32)
    chosen = jnp.sum(choose * router_probs[:, None, :], axis=2)
    pick_table = (routes[:, :, None] == expert_ids).astype(jnp.int32) * live_int[:, None, None]
    flat_picks = pick_table.reshape(rows * 2, experts)
    before = jnp.cumsum(flat_picks, axis=0) - flat_picks
    slot_index = jnp.sum(before * flat_picks, axis=1).reshape(rows, 2)
    position = jnp.where(live_int[:, None] > 0, routes * capacity + slot_index, overflow)

    n_chunks = 2
    part_cap = 8 * ((capacity + 8 * n_chunks - 1) // (8 * n_chunks))
    chunk_sizes = [min(part_cap, capacity - k * part_cap) for k in range(n_chunks)]
    chunk_sizes = [size for size in chunk_sizes if size > 0]
    chunk_starts = [sum(chunk_sizes[:k]) for k in range(len(chunk_sizes))]
    slot_ids = jnp.concatenate(
        [
            (
                jnp.arange(experts, dtype=jnp.int32)[:, None] * capacity
                + start
                + jnp.arange(size, dtype=jnp.int32)[None, :]
            ).reshape(-1)
            for start, size in zip(chunk_starts, chunk_sizes)
        ]
    )[:, None]
    take_first = (slot_ids == position[None, :, 0]).astype(jnp.bfloat16)
    take_second = (slot_ids == position[None, :, 1]).astype(jnp.bfloat16)

    grad_out = cotangent.astype(jnp.float32) * live_rows[:, None]
    weighted = chosen * live_rows[:, None]
    grad_picked = (weighted[:, :, None] * grad_out[:, None, :]).astype(jnp.bfloat16)

    def dispatch_rows(low, high):
        first = take_first[low:high]
        second = take_second[low:high]
        sent_rows = jnp.dot(first + second, moe_in, preferred_element_type=jnp.float32)
        sent_grad = jnp.dot(
            first, grad_picked[:, 0], preferred_element_type=jnp.float32
        ) + jnp.dot(second, grad_picked[:, 1], preferred_element_type=jnp.float32)
        return jnp.concatenate([sent_rows, sent_grad], axis=1).astype(jnp.bfloat16)

    grad_first = None
    grad_second = None
    returned_parts = []
    for start, size in zip(chunk_starts, chunk_sizes):
        arrived = lax.all_to_all(
            dispatch_rows(experts * start, experts * (start + size)).reshape(
                experts, size, 2 * width
            ),
            "expert",
            split_axis=0,
            concat_axis=0,
            tiled=True,
        ).reshape(experts * size, 2 * width)
        flat_arrived = arrived[:, :width]
        flat_grad = arrived[:, width:]
        hidden_grad = lax.dot_general(
            flat_grad, expert_second, COL_CONTRACT, preferred_element_type=jnp.float32
        )
        pre_act = jnp.dot(flat_arrived, expert_first, preferred_element_type=jnp.float32)
        activated, slope = gelu_parts(pre_act)
        activated = activated.astype(jnp.bfloat16)
        pre_grad = (hidden_grad * slope).astype(jnp.bfloat16)
        produced = jnp.dot(
            activated, expert_second, preferred_element_type=jnp.float32
        ).astype(jnp.bfloat16)
        row_grad = lax.dot_general(
            pre_grad, expert_first, COL_CONTRACT, preferred_element_type=jnp.float32
        ).astype(jnp.bfloat16)
        part_second = lax.dot_general(
            activated, flat_grad, ROW_CONTRACT, preferred_element_type=jnp.float32
        )
        part_first = lax.dot_general(
            flat_arrived, pre_grad, ROW_CONTRACT, preferred_element_type=jnp.float32
        )
        grad_first = part_first if grad_first is None else grad_first + part_first
        grad_second = part_second if grad_second is None else grad_second + part_second
        returning = jnp.concatenate([produced, row_grad], axis=1).reshape(
            experts, size, 2 * width
        )
        returned_parts.append(
            lax.all_to_all(returning, "expert", split_axis=0, concat_axis=0, tiled=True)
        )

    expert_grads = jnp.stack(
        [grad_first, grad_second.reshape(width, ff)], axis=0
    ).astype(jnp.bfloat16)
    expert_share = lax.psum_scatter(expert_grads, "shard", scatter_dimension=1, tiled=True)
    expert_share = expert_share.astype(jnp.float32)
    grad_in_share = expert_share[0][None]
    grad_back_share = expert_share[1].reshape(back_rows, width)[None]

    picked_first = None
    picked_second = None
    for start, size, part in zip(chunk_starts, chunk_sizes, returned_parts):
        low, high = experts * start, experts * (start + size)
        part = part.reshape(-1, 2 * width)
        part_first = lax.dot_general(
            take_first[low:high], part, ROW_CONTRACT, preferred_element_type=jnp.float32
        )
        part_second = lax.dot_general(
            take_second[low:high], part, ROW_CONTRACT, preferred_element_type=jnp.float32
        )
        picked_first = part_first if picked_first is None else picked_first + part_first
        picked_second = part_second if picked_second is None else picked_second + part_second
    moe_out = (
        weighted[:, 0:1] * picked_first[:, :width] + weighted[:, 1:2] * picked_second[:, :width]
    )
    output = (live_rows[:, None] * (hidden_state + moe_out)).astype(jnp.bfloat16)
    grad_chosen = jnp.stack(
        [
            jnp.sum(grad_out * picked_first[:, :width], axis=1),
            jnp.sum(grad_out * picked_second[:, :width], axis=1),
        ],
        axis=1,
    ) * live_rows[:, None]
    expert_part = (picked_first[:, width:] + picked_second[:, width:]) * live_rows[:, None]
    prob_sum = jnp.sum(choose * grad_chosen[:, :, None], axis=1)
    logit_grad = (
        router_probs * (prob_sum - jnp.sum(router_probs * prob_sum, axis=-1, keepdims=True))
    ).astype(jnp.bfloat16)
    grad_router = lax.dot_general(
        moe_in, logit_grad, ROW_CONTRACT, preferred_element_type=jnp.float32
    )
    moe_in_grad = expert_part + lax.dot_general(
        logit_grad, full_router, COL_CONTRACT, preferred_element_type=jnp.float32
    )
    _, norm_back = jax.vjp(layer_norm, hidden_state, gain_two)
    state_part, grad_gain_two = norm_back(moe_in_grad)
    state_grad = grad_out + state_part
    branch_grad = state_grad.astype(jnp.bfloat16)
    grad_wout = lax.dot_general(
        mixed_rows, branch_grad, ROW_CONTRACT, preferred_element_type=jnp.float32
    )
    mixed_grad = lax.dot_general(
        branch_grad, full_out, COL_CONTRACT, preferred_element_type=jnp.float32
    )
    mixed_grad = jnp.pad(mixed_grad.astype(jnp.bfloat16), ((0, pad_rows - rows), (0, 0)))
    grad_q, grad_k, grad_v = attention_bwd(projected_pad, mixed_grad, images)
    projected_grad = jnp.concatenate([grad_q, grad_k, grad_v], axis=1)
    attn_in_pad = jnp.pad(attn_in, ((0, pad_rows - rows), (0, 0)))
    grad_qkv = lax.dot_general(
        attn_in_pad, projected_grad, ROW_CONTRACT, preferred_element_type=jnp.float32
    )
    attn_in_grad = lax.dot_general(
        projected_grad[:rows], full_qkv, COL_CONTRACT, preferred_element_type=jnp.float32
    )
    _, first_back = jax.vjp(layer_norm, token_f, gain_one)
    token_part, grad_gain_one = first_back(attn_in_grad)
    grad_tokens = (state_grad + token_part).astype(jnp.bfloat16)

    small = jnp.concatenate(
        [grad_router, grad_gain_one[:, None], grad_gain_two[:, None]], axis=1
    )
    small = jnp.pad(small, ((0, 0), (0, 128 - small.shape[1])))
    dense_grads = jnp.concatenate([grad_qkv, grad_wout, small], axis=1)
    dense_share = shard_reduce_scatter(dense_grads, "shard", 128 * (dense_grads.shape[1] // 256))
    dense_total = lax.psum(dense_share.astype(jnp.bfloat16), "expert").astype(jnp.float32)
    return (
        output,
        grad_tokens,
        dense_total[:, :qkv_cols],
        dense_total[:, qkv_cols : qkv_cols + width],
        dense_total[:, qkv_cols + width : qkv_cols + width + n_route],
        dense_total[:, qkv_cols + width + n_route],
        dense_total[:, qkv_cols + width + n_route + 1],
        grad_in_share,
        grad_back_share,
    )


def solution(mesh):
    return _mapped(mesh)


def _mapped(mesh):
    return jax.shard_map(
        shards,
        mesh=mesh,
        in_specs=(
            P(("expert", "shard"), None),
            P("expert", "shard"),
            P(("expert", "shard"), None),
            P("shard", None),
            P("shard", None),
            P("shard", None),
            P("shard"),
            P("shard"),
            P("expert", "shard", None),
            P("expert", "shard", None),
            P(("expert", "shard"), None),
        ),
        out_specs=(
            P(("expert", "shard"), None),
            P(("expert", "shard"), None),
            P("shard", None),
            P("shard", None),
            P("shard", None),
            P("shard"),
            P("shard"),
            P("expert", "shard", None),
            P("expert", "shard", None),
        ),
        check_vma=False,
    )
```

```python
import functools

import jax
import numpy as np
import jax.numpy as jnp
from jax import lax
from jax.experimental import pallas as pl
from jax.experimental.pallas import tpu as pltpu
from jax.sharding import PartitionSpec as P

HD = 64
SEQ = 197


EPSILON = 1e-06
ROW_CONTRACT = (((0,), (0,)), ((), ()))
COL_CONTRACT = (((1,), (1,)), ((), ()))


def _image_of(idx, images):
    count = jnp.zeros(idx.shape, jnp.int32)
    for i in range(1, images + 1):
        count = count + (idx >= i * SEQ).astype(jnp.int32)
    return count


def _same_image(size, images):
    rows = lax.broadcasted_iota(jnp.int32, (size, size), 0)
    cols = lax.broadcasted_iota(jnp.int32, (size, size), 1)
    return _image_of(rows, images) == _image_of(cols, images)


def _softmax_masked(qj, k, same):
    s = lax.dot_general(qj, k, COL_CONTRACT, preferred_element_type=jnp.float32) * (HD ** -0.5)
    s = jnp.where(same, s, -jnp.inf)
    top = jnp.max(s, axis=1, keepdims=True)
    e = jnp.exp(s - top)
    return e / jnp.sum(e, axis=1, keepdims=True)


def attn_fwd_kernel(q_ref, k_ref, v_ref, o_ref, *, images):
    R = q_ref.shape[0]
    q = q_ref[...]
    k = k_ref[...]
    v = v_ref[...]
    same = _same_image(R, images)
    lane = lax.broadcasted_iota(jnp.int32, (1, 2 * HD), 1)
    out = jnp.zeros((R, 2 * HD), jnp.float32)
    for j in range(2):
        in_head = (lane >= HD) == (j == 1)
        p = _softmax_masked(jnp.where(in_head, q, jnp.zeros_like(q)), k, same)
        o = jnp.dot(p.astype(jnp.bfloat16), v, preferred_element_type=jnp.float32)
        out = jnp.where(in_head, o, out)
    o_ref[...] = out.astype(o_ref.dtype)


def attn_bwd_kernel(q_ref, k_ref, v_ref, g_ref, dq_ref, dk_ref, dv_ref, *, images):
    R = q_ref.shape[0]
    q = q_ref[...]
    k = k_ref[...]
    v = v_ref[...]
    g = g_ref[...]
    same = _same_image(R, images)
    lane = lax.broadcasted_iota(jnp.int32, (1, 2 * HD), 1)
    dq = jnp.zeros((R, 2 * HD), jnp.float32)
    dk = jnp.zeros((R, 2 * HD), jnp.float32)
    dv = jnp.zeros((R, 2 * HD), jnp.float32)
    for j in range(2):
        in_head = (lane >= HD) == (j == 1)
        p = _softmax_masked(jnp.where(in_head, q, jnp.zeros_like(q)), k, same)
        gj = jnp.where(in_head, g, jnp.zeros_like(g))
        dp = lax.dot_general(gj, v, COL_CONTRACT, preferred_element_type=jnp.float32)
        ds = (p * (dp - jnp.sum(p * dp, axis=1, keepdims=True))).astype(jnp.bfloat16)
        dq_j = jnp.dot(ds, k, preferred_element_type=jnp.float32) * (HD ** -0.5)
        dk_j = lax.dot_general(ds, q, ROW_CONTRACT, preferred_element_type=jnp.float32) * (HD ** -0.5)
        dv_j = lax.dot_general(p.astype(jnp.bfloat16), g, ROW_CONTRACT, preferred_element_type=jnp.float32)
        dq = jnp.where(in_head, dq_j, dq)
        dk = jnp.where(in_head, dk_j, dk)
        dv = jnp.where(in_head, dv_j, dv)
    dq_ref[...] = dq.astype(dq_ref.dtype)
    dk_ref[...] = dk.astype(dk_ref.dtype)
    dv_ref[...] = dv.astype(dv_ref.dtype)


def attention_fwd(projected, images):
    R = projected.shape[0]
    W = projected.shape[1] // 3
    pairs = W // (2 * HD)
    blk = lambda off: pl.BlockSpec((R, 2 * HD), lambda h: (0, off + h))
    return pl.pallas_call(
        functools.partial(attn_fwd_kernel, images=images),
        grid=(pairs,),
        in_specs=[blk(0), blk(pairs), blk(2 * pairs)],
        out_specs=blk(0),
        out_shape=jax.ShapeDtypeStruct((R, W), jnp.bfloat16),
        compiler_params=pltpu.CompilerParams(vmem_limit_bytes=48 * 1024 * 1024),
    )(projected, projected, projected)


def attention_bwd(projected, mixed_grad, images):
    R = projected.shape[0]
    W = projected.shape[1] // 3
    pairs = W // (2 * HD)
    blk = lambda off: pl.BlockSpec((R, 2 * HD), lambda h: (0, off + h))
    out = jax.ShapeDtypeStruct((R, W), jnp.bfloat16)
    return pl.pallas_call(
        functools.partial(attn_bwd_kernel, images=images),
        grid=(pairs,),
        in_specs=[blk(0), blk(pairs), blk(2 * pairs), blk(0)],
        out_specs=[blk(0), blk(0), blk(0)],
        out_shape=[out, out, out],
        compiler_params=pltpu.CompilerParams(vmem_limit_bytes=48 * 1024 * 1024),
    )(projected, projected, projected, mixed_grad)


def _exchange(values, bits_left, bit, axis_name, size, index):
    axis = bits_left.index(bit)
    mine = (index >> bit) & 1
    keep = lax.dynamic_index_in_dim(values, mine, axis, keepdims=False)
    send = lax.dynamic_index_in_dim(values, 1 - mine, axis, keepdims=False)
    pairs = [(i, i ^ (1 << bit)) for i in range(size)]
    got = lax.ppermute(send.astype(jnp.bfloat16), axis_name, pairs)
    return keep + got.astype(jnp.float32), [b for b in bits_left if b != bit]


def shard_reduce_scatter(values, axis_name, split_col):
    size = lax.axis_size(axis_name)
    index = lax.axis_index(axis_name)
    n_bits = size.bit_length() - 1
    block = values.shape[0] // size
    bits = list(range(n_bits - 1, -1, -1))
    values = values.astype(jnp.float32).reshape([2] * n_bits + [block, values.shape[1]])
    values, bits = _exchange(values, bits, 0, axis_name, size, index)
    first, second = values[..., :split_col], values[..., split_col:]
    first_bits, second_bits = list(bits), list(bits)
    for up, down in zip(range(1, n_bits), range(n_bits - 1, 0, -1)):
        first, first_bits = _exchange(first, first_bits, up, axis_name, size, index)
        second, second_bits = _exchange(second, second_bits, down, axis_name, size, index)
    return jnp.concatenate([first, second], axis=-1)


def _gather_back(values, bit, axis_name, size, index):
    n_bits = size.bit_length() - 1
    mine = (index >> bit) & 1
    pairs = [(i, i ^ (1 << bit)) for i in range(size)]
    got = lax.ppermute(values, axis_name, pairs)
    low = jnp.where(mine == 0, values, got)
    high = jnp.where(mine == 0, got, values)
    return jnp.stack([low, high], axis=n_bits - 1 - bit)


def expert_all_reduce(values, axis_name):
    size = lax.axis_size(axis_name)
    index = lax.axis_index(axis_name)
    n_bits = size.bit_length() - 1
    rows = values.shape[0]
    if rows % size:
        return lax.psum(values.astype(jnp.bfloat16), axis_name).astype(jnp.float32)
    bits = list(range(n_bits - 1, -1, -1))
    parts = values.astype(jnp.float32).reshape([2] * n_bits + [rows // size, values.shape[1]])
    for bit in range(n_bits):
        parts, bits = _exchange(parts, bits, bit, axis_name, size, index)
    parts = parts.astype(jnp.bfloat16)
    for bit in range(n_bits - 1, -1, -1):
        parts = _gather_back(parts, bit, axis_name, size, index)
    return parts.reshape(rows, values.shape[1]).astype(jnp.float32)


def layer_norm(values, norm_gain):
    row_mean = jnp.mean(values, axis=-1, keepdims=True)
    centered = values - row_mean
    variance = jnp.mean(centered * centered, axis=-1, keepdims=True)
    return centered * lax.rsqrt(variance + EPSILON) * norm_gain


def normalize_rows(scores):
    row_top = jnp.max(scores, axis=-1, keepdims=True)
    exp_scores = jnp.exp(scores - row_top)
    return exp_scores / jnp.sum(exp_scores, axis=-1, keepdims=True)


def gelu_parts(values):
    sqrt_half = np.float32(np.sqrt(0.5))
    tail = lax.erfc(-values * sqrt_half)
    density = jnp.exp(-0.5 * values * values) * np.float32(1.0 / np.sqrt(2.0 * np.pi))
    return 0.5 * values * tail, 0.5 * tail + values * density


def shards(
    tokens,
    image_counts,
    routes,
    w_qkv,
    w_out,
    w_router,
    gain_attn,
    gain_moe,
    w_in,
    w_back,
    cotangent,
):
    rows, width = tokens.shape
    experts = lax.axis_size("expert")
    capacity = 8 * (5 * rows // (16 * experts)) + 8
    overflow = experts * capacity
    images = rows // SEQ
    qkv_cols = w_qkv.shape[1]
    n_route = w_router.shape[1]
    ff = w_in.shape[2]
    row_ids = jnp.arange(rows, dtype=jnp.int32)
    live_int = (row_ids // SEQ < image_counts[0, 0]).astype(jnp.int32)
    live_rows = live_int.astype(jnp.float32)

    dense_local = jnp.concatenate(
        [w_qkv, w_out, w_router, gain_attn[:, None], gain_moe[:, None]], axis=1
    )
    dense_full = lax.all_gather(dense_local, "shard", axis=0, tiled=True)
    full_qkv = dense_full[:, :qkv_cols]
    full_out = dense_full[:, qkv_cols : qkv_cols + width]
    full_router = dense_full[:, qkv_cols + width : qkv_cols + width + n_route]
    gain_one = dense_full[:, -2].astype(jnp.float32)
    gain_two = dense_full[:, -1].astype(jnp.float32)

    back_rows = w_back.shape[1]
    expert_local = jnp.stack(
        [w_in[0], w_back[0].reshape(back_rows * width // ff, ff)], axis=0
    )
    expert_full = lax.all_gather(expert_local, "shard", axis=1, tiled=True)
    expert_first = expert_full[0]
    expert_second = expert_full[1].reshape(ff, width)

    token_f = tokens.astype(jnp.float32)
    attn_in = lax.optimization_barrier(layer_norm(token_f, gain_one).astype(jnp.bfloat16))
    projected = jnp.dot(attn_in, full_qkv, preferred_element_type=jnp.float32).astype(jnp.bfloat16)
    pad_rows = -(-rows // 128) * 128
    projected_pad = jnp.pad(projected, ((0, pad_rows - rows), (0, 0)))
    mixed_rows = attention_fwd(projected_pad, images)[:rows]
    hidden_state = token_f + jnp.dot(mixed_rows, full_out, preferred_element_type=jnp.float32)
    moe_in = layer_norm(hidden_state, gain_two).astype(jnp.bfloat16)
    logits = jnp.dot(moe_in, full_router, preferred_element_type=jnp.float32)
    router_probs = normalize_rows(logits)
    expert_ids = jnp.arange(experts, dtype=jnp.int32)
    choose = (routes[:, :, None] == expert_ids).astype(jnp.float32)
    chosen = jnp.sum(choose * router_probs[:, None, :], axis=2)
    pick_table = (routes[:, :, None] == expert_ids).astype(jnp.int32) * live_int[:, None, None]
    flat_picks = pick_table.reshape(rows * 2, experts)
    before = jnp.cumsum(flat_picks, axis=0) - flat_picks
    slot_index = jnp.sum(before * flat_picks, axis=1).reshape(rows, 2)
    position = jnp.where(live_int[:, None] > 0, routes * capacity + slot_index, overflow)

    n_chunks = 2
    part_cap = 8 * ((capacity + 8 * n_chunks - 1) // (8 * n_chunks))
    chunk_sizes = [min(part_cap, capacity - k * part_cap) for k in range(n_chunks)]
    chunk_sizes = [size for size in chunk_sizes if size > 0]
    chunk_starts = [sum(chunk_sizes[:k]) for k in range(len(chunk_sizes))]
    slot_ids = jnp.concatenate(
        [
            (
                jnp.arange(experts, dtype=jnp.int32)[:, None] * capacity
                + start
                + jnp.arange(size, dtype=jnp.int32)[None, :]
            ).reshape(-1)
            for start, size in zip(chunk_starts, chunk_sizes)
        ]
    )[:, None]
    take_first = (slot_ids == position[None, :, 0]).astype(jnp.bfloat16)
    take_second = (slot_ids == position[None, :, 1]).astype(jnp.bfloat16)

    grad_out = cotangent.astype(jnp.float32) * live_rows[:, None]
    weighted = chosen * live_rows[:, None]
    grad_picked = (weighted[:, :, None] * grad_out[:, None, :]).astype(jnp.bfloat16)

    def dispatch_rows(low, high):
        first = take_first[low:high]
        second = take_second[low:high]
        sent_rows = jnp.dot(first + second, moe_in, preferred_element_type=jnp.float32)
        sent_grad = jnp.dot(
            first, grad_picked[:, 0], preferred_element_type=jnp.float32
        ) + jnp.dot(second, grad_picked[:, 1], preferred_element_type=jnp.float32)
        return jnp.concatenate([sent_rows, sent_grad], axis=1).astype(jnp.bfloat16)

    grad_first = None
    grad_second = None
    returned_parts = []
    for start, size in zip(chunk_starts, chunk_sizes):
        arrived = lax.all_to_all(
            dispatch_rows(experts * start, experts * (start + size)).reshape(
                experts, size, 2 * width
            ),
            "expert",
            split_axis=0,
            concat_axis=0,
            tiled=True,
        ).reshape(experts * size, 2 * width)
        flat_arrived = arrived[:, :width]
        flat_grad = arrived[:, width:]
        hidden_grad = lax.dot_general(
            flat_grad, expert_second, COL_CONTRACT, preferred_element_type=jnp.float32
        )
        pre_act = jnp.dot(flat_arrived, expert_first, preferred_element_type=jnp.float32)
        activated, slope = gelu_parts(pre_act)
        activated = activated.astype(jnp.bfloat16)
        pre_grad = (hidden_grad * slope).astype(jnp.bfloat16)
        produced = jnp.dot(
            activated, expert_second, preferred_element_type=jnp.float32
        ).astype(jnp.bfloat16)
        row_grad = lax.dot_general(
            pre_grad, expert_first, COL_CONTRACT, preferred_element_type=jnp.float32
        ).astype(jnp.bfloat16)
        part_second = lax.dot_general(
            activated, flat_grad, ROW_CONTRACT, preferred_element_type=jnp.float32
        )
        part_first = lax.dot_general(
            flat_arrived, pre_grad, ROW_CONTRACT, preferred_element_type=jnp.float32
        )
        grad_first = part_first if grad_first is None else grad_first + part_first
        grad_second = part_second if grad_second is None else grad_second + part_second
        returning = jnp.concatenate([produced, row_grad], axis=1).reshape(
            experts, size, 2 * width
        )
        returned_parts.append(
            lax.all_to_all(returning, "expert", split_axis=0, concat_axis=0, tiled=True)
        )

    expert_grads = jnp.stack(
        [grad_first, grad_second.reshape(width, ff)], axis=0
    ).astype(jnp.bfloat16)
    expert_share = lax.psum_scatter(expert_grads, "shard", scatter_dimension=1, tiled=True)
    expert_share = expert_share.astype(jnp.float32)
    grad_in_share = expert_share[0][None]
    grad_back_share = expert_share[1].reshape(back_rows, width)[None]

    picked_first = None
    picked_second = None
    for start, size, part in zip(chunk_starts, chunk_sizes, returned_parts):
        low, high = experts * start, experts * (start + size)
        part = part.reshape(-1, 2 * width)
        part_first = lax.dot_general(
            take_first[low:high], part, ROW_CONTRACT, preferred_element_type=jnp.float32
        )
        part_second = lax.dot_general(
            take_second[low:high], part, ROW_CONTRACT, preferred_element_type=jnp.float32
        )
        picked_first = part_first if picked_first is None else picked_first + part_first
        picked_second = part_second if picked_second is None else picked_second + part_second
    moe_out = (
        weighted[:, 0:1] * picked_first[:, :width] + weighted[:, 1:2] * picked_second[:, :width]
    )
    output = (live_rows[:, None] * (hidden_state + moe_out)).astype(jnp.bfloat16)
    grad_chosen = jnp.stack(
        [
            jnp.sum(grad_out * picked_first[:, :width], axis=1),
            jnp.sum(grad_out * picked_second[:, :width], axis=1),
        ],
        axis=1,
    ) * live_rows[:, None]
    expert_part = (picked_first[:, width:] + picked_second[:, width:]) * live_rows[:, None]
    prob_sum = jnp.sum(choose * grad_chosen[:, :, None], axis=1)
    logit_grad = (
        router_probs * (prob_sum - jnp.sum(router_probs * prob_sum, axis=-1, keepdims=True))
    ).astype(jnp.bfloat16)
    grad_router = lax.dot_general(
        moe_in, logit_grad, ROW_CONTRACT, preferred_element_type=jnp.float32
    )
    moe_in_grad = expert_part + lax.dot_general(
        logit_grad, full_router, COL_CONTRACT, preferred_element_type=jnp.float32
    )
    _, norm_back = jax.vjp(layer_norm, hidden_state, gain_two)
    state_part, grad_gain_two = norm_back(moe_in_grad)
    state_grad = grad_out + state_part
    branch_grad = state_grad.astype(jnp.bfloat16)
    grad_wout = lax.dot_general(
        mixed_rows, branch_grad, ROW_CONTRACT, preferred_element_type=jnp.float32
    )
    mixed_grad = lax.dot_general(
        branch_grad, full_out, COL_CONTRACT, preferred_element_type=jnp.float32
    )
    mixed_grad = jnp.pad(mixed_grad.astype(jnp.bfloat16), ((0, pad_rows - rows), (0, 0)))
    grad_q, grad_k, grad_v = attention_bwd(projected_pad, mixed_grad, images)
    projected_grad = jnp.concatenate([grad_q, grad_k, grad_v], axis=1)
    attn_in_pad = jnp.pad(attn_in, ((0, pad_rows - rows), (0, 0)))
    grad_qkv = lax.dot_general(
        attn_in_pad, projected_grad, ROW_CONTRACT, preferred_element_type=jnp.float32
    )
    attn_in_grad = lax.dot_general(
        projected_grad[:rows], full_qkv, COL_CONTRACT, preferred_element_type=jnp.float32
    )
    _, first_back = jax.vjp(layer_norm, token_f, gain_one)
    token_part, grad_gain_one = first_back(attn_in_grad)
    grad_tokens = (state_grad + token_part).astype(jnp.bfloat16)

    small = jnp.concatenate(
        [grad_router, grad_gain_one[:, None], grad_gain_two[:, None]], axis=1
    )
    small = jnp.pad(small, ((0, 0), (0, 128 - small.shape[1])))
    dense_grads = jnp.concatenate([grad_qkv, grad_wout, small], axis=1)
    chunk_cols = 128 * (dense_grads.shape[1] // 256)
    dense_total = jnp.concatenate(
        [
            expert_all_reduce(
                shard_reduce_scatter(part, "shard", 128 * (part.shape[1] // 256)), "expert"
            )
            for part in (dense_grads[:, :chunk_cols], dense_grads[:, chunk_cols:])
        ],
        axis=1,
    )
    return (
        output,
        grad_tokens,
        dense_total[:, :qkv_cols],
        dense_total[:, qkv_cols : qkv_cols + width],
        dense_total[:, qkv_cols + width : qkv_cols + width + n_route],
        dense_total[:, qkv_cols + width + n_route],
        dense_total[:, qkv_cols + width + n_route + 1],
        grad_in_share,
        grad_back_share,
    )


def solution(mesh):
    return _mapped(mesh)


def _mapped(mesh):
    return jax.shard_map(
        shards,
        mesh=mesh,
        in_specs=(
            P(("expert", "shard"), None),
            P("expert", "shard"),
            P(("expert", "shard"), None),
            P("shard", None),
            P("shard", None),
            P("shard", None),
            P("shard"),
            P("shard"),
            P("expert", "shard", None),
            P("expert", "shard", None),
            P(("expert", "shard"), None),
        ),
        out_specs=(
            P(("expert", "shard"), None),
            P(("expert", "shard"), None),
            P("shard", None),
            P("shard", None),
            P("shard", None),
            P("shard"),
            P("shard"),
            P("expert", "shard", None),
            P("expert", "shard", None),
        ),
        check_vma=False,
    )
```

```python
import functools

import jax
import numpy as np
import jax.numpy as jnp
from jax import lax
from jax.experimental import pallas as pl
from jax.experimental.pallas import tpu as pltpu
from jax.sharding import PartitionSpec as P

HD = 64
SEQ = 197


EPSILON = 1e-06
ROW_CONTRACT = (((0,), (0,)), ((), ()))
COL_CONTRACT = (((1,), (1,)), ((), ()))


def _image_of(idx, images):
    count = jnp.zeros(idx.shape, jnp.int32)
    for i in range(1, images + 1):
        count = count + (idx >= i * SEQ).astype(jnp.int32)
    return count


def _same_image(size, images):
    rows = lax.broadcasted_iota(jnp.int32, (size, size), 0)
    cols = lax.broadcasted_iota(jnp.int32, (size, size), 1)
    return _image_of(rows, images) == _image_of(cols, images)


def _softmax_masked(qj, k, same):
    s = lax.dot_general(qj, k, COL_CONTRACT, preferred_element_type=jnp.float32) * (HD ** -0.5)
    s = jnp.where(same, s, -jnp.inf)
    top = jnp.max(s, axis=1, keepdims=True)
    e = jnp.exp(s - top)
    return e / jnp.sum(e, axis=1, keepdims=True)


def _two_heads(values, lane):
    zero = jnp.zeros_like(values)
    return jnp.concatenate(
        [jnp.where(lane < HD, values, zero), jnp.where(lane >= HD, values, zero)], axis=0
    )


def _pick_heads(stacked, lane, rows):
    return jnp.where(lane < HD, stacked[:rows], stacked[rows:])


def attn_fwd_kernel(q_ref, k_ref, v_ref, o_ref, p_ref, *, images):
    R = q_ref.shape[0]
    same = _same_image(R, images)
    same = jnp.concatenate([same, same], axis=0)
    lane = lax.broadcasted_iota(jnp.int32, (1, 2 * HD), 1)
    p = _softmax_masked(_two_heads(q_ref[...], lane), k_ref[...], same)
    p_ref[0] = p
    o = jnp.dot(p.astype(jnp.bfloat16), v_ref[...], preferred_element_type=jnp.float32)
    o_ref[...] = _pick_heads(o, lane, R).astype(o_ref.dtype)


def attn_bwd_kernel(q_ref, k_ref, v_ref, g_ref, p_ref, dq_ref, dk_ref, dv_ref):
    R = q_ref.shape[0]
    k = k_ref[...]
    v = v_ref[...]
    lane = lax.broadcasted_iota(jnp.int32, (1, 2 * HD), 1)
    q2 = _two_heads(q_ref[...], lane)
    g2 = _two_heads(g_ref[...], lane)
    p = p_ref[0]
    dp = lax.dot_general(g2, v, COL_CONTRACT, preferred_element_type=jnp.float32)
    ds = (p * (dp - jnp.sum(p * dp, axis=1, keepdims=True))).astype(jnp.bfloat16)
    dq = jnp.dot(ds, k, preferred_element_type=jnp.float32) * (HD ** -0.5)
    dk = lax.dot_general(ds, q2, ROW_CONTRACT, preferred_element_type=jnp.float32) * (HD ** -0.5)
    dv = lax.dot_general(p.astype(jnp.bfloat16), g2, ROW_CONTRACT, preferred_element_type=jnp.float32)
    dq_ref[...] = _pick_heads(dq, lane, R).astype(dq_ref.dtype)
    dk_ref[...] = dk.astype(dk_ref.dtype)
    dv_ref[...] = dv.astype(dv_ref.dtype)


def attention_fwd(projected, images):
    R = projected.shape[0]
    W = projected.shape[1] // 3
    pairs = W // (2 * HD)
    blk = lambda off: pl.BlockSpec((R, 2 * HD), lambda h: (0, off + h))
    probs = pl.BlockSpec((1, 2 * R, R), lambda h: (h, 0, 0))
    return pl.pallas_call(
        functools.partial(attn_fwd_kernel, images=images),
        grid=(pairs,),
        in_specs=[blk(0), blk(pairs), blk(2 * pairs)],
        out_specs=[blk(0), probs],
        out_shape=[
            jax.ShapeDtypeStruct((R, W), jnp.bfloat16),
            jax.ShapeDtypeStruct((pairs, 2 * R, R), jnp.float32),
        ],
        compiler_params=pltpu.CompilerParams(vmem_limit_bytes=48 * 1024 * 1024),
    )(projected, projected, projected)


def attention_bwd(projected, mixed_grad, probs):
    R = projected.shape[0]
    W = projected.shape[1] // 3
    pairs = W // (2 * HD)
    blk = lambda off: pl.BlockSpec((R, 2 * HD), lambda h: (0, off + h))
    out = jax.ShapeDtypeStruct((R, W), jnp.bfloat16)
    return pl.pallas_call(
        attn_bwd_kernel,
        grid=(pairs,),
        in_specs=[
            blk(0),
            blk(pairs),
            blk(2 * pairs),
            blk(0),
            pl.BlockSpec((1, 2 * R, R), lambda h: (h, 0, 0)),
        ],
        out_specs=[blk(0), blk(0), blk(0)],
        out_shape=[out, out, out],
        compiler_params=pltpu.CompilerParams(vmem_limit_bytes=48 * 1024 * 1024),
    )(projected, projected, projected, mixed_grad, probs)


def _exchange(values, bits_left, bit, axis_name, size, index):
    axis = bits_left.index(bit)
    mine = (index >> bit) & 1
    keep = lax.dynamic_index_in_dim(values, mine, axis, keepdims=False)
    send = lax.dynamic_index_in_dim(values, 1 - mine, axis, keepdims=False)
    pairs = [(i, i ^ (1 << bit)) for i in range(size)]
    got = lax.ppermute(send.astype(jnp.bfloat16), axis_name, pairs)
    return keep + got.astype(jnp.float32), [b for b in bits_left if b != bit]


def shard_reduce_scatter(values, axis_name, split_col):
    size = lax.axis_size(axis_name)
    index = lax.axis_index(axis_name)
    n_bits = size.bit_length() - 1
    block = values.shape[0] // size
    bits = list(range(n_bits - 1, -1, -1))
    values = values.astype(jnp.float32).reshape([2] * n_bits + [block, values.shape[1]])
    values, bits = _exchange(values, bits, 0, axis_name, size, index)
    first, second = values[..., :split_col], values[..., split_col:]
    first_bits, second_bits = list(bits), list(bits)
    for up, down in zip(range(1, n_bits), range(n_bits - 1, 0, -1)):
        first, first_bits = _exchange(first, first_bits, up, axis_name, size, index)
        second, second_bits = _exchange(second, second_bits, down, axis_name, size, index)
    return jnp.concatenate([first, second], axis=-1)


def _gather_back(values, bit, axis_name, size, index):
    n_bits = size.bit_length() - 1
    mine = (index >> bit) & 1
    pairs = [(i, i ^ (1 << bit)) for i in range(size)]
    got = lax.ppermute(values, axis_name, pairs)
    low = jnp.where(mine == 0, values, got)
    high = jnp.where(mine == 0, got, values)
    return jnp.stack([low, high], axis=n_bits - 1 - bit)


def expert_all_reduce(values, axis_name):
    size = lax.axis_size(axis_name)
    index = lax.axis_index(axis_name)
    n_bits = size.bit_length() - 1
    rows = values.shape[0]
    if rows % size:
        return lax.psum(values.astype(jnp.bfloat16), axis_name).astype(jnp.float32)
    bits = list(range(n_bits - 1, -1, -1))
    parts = values.astype(jnp.float32).reshape([2] * n_bits + [rows // size, values.shape[1]])
    for bit in range(n_bits):
        parts, bits = _exchange(parts, bits, bit, axis_name, size, index)
    parts = parts.astype(jnp.bfloat16)
    for bit in range(n_bits - 1, -1, -1):
        parts = _gather_back(parts, bit, axis_name, size, index)
    return parts.reshape(rows, values.shape[1]).astype(jnp.float32)


def layer_norm(values, norm_gain):
    row_mean = jnp.mean(values, axis=-1, keepdims=True)
    centered = values - row_mean
    variance = jnp.mean(centered * centered, axis=-1, keepdims=True)
    return centered * lax.rsqrt(variance + EPSILON) * norm_gain


def normalize_rows(scores):
    row_top = jnp.max(scores, axis=-1, keepdims=True)
    exp_scores = jnp.exp(scores - row_top)
    return exp_scores / jnp.sum(exp_scores, axis=-1, keepdims=True)


def gelu_parts(values):
    sqrt_half = np.float32(np.sqrt(0.5))
    tail = lax.erfc(-values * sqrt_half)
    density = jnp.exp(-0.5 * values * values) * np.float32(1.0 / np.sqrt(2.0 * np.pi))
    return 0.5 * values * tail, 0.5 * tail + values * density


def shards(
    tokens,
    image_counts,
    routes,
    w_qkv,
    w_out,
    w_router,
    gain_attn,
    gain_moe,
    w_in,
    w_back,
    cotangent,
):
    rows, width = tokens.shape
    experts = lax.axis_size("expert")
    capacity = 8 * (5 * rows // (16 * experts)) + 8
    overflow = experts * capacity
    images = rows // SEQ
    qkv_cols = w_qkv.shape[1]
    n_route = w_router.shape[1]
    ff = w_in.shape[2]
    row_ids = jnp.arange(rows, dtype=jnp.int32)
    live_int = (row_ids // SEQ < image_counts[0, 0]).astype(jnp.int32)
    live_rows = live_int.astype(jnp.float32)

    dense_local = jnp.concatenate(
        [w_qkv, w_out, w_router, gain_attn[:, None], gain_moe[:, None]], axis=1
    )
    dense_full = lax.all_gather(dense_local, "shard", axis=0, tiled=True)
    full_qkv = dense_full[:, :qkv_cols]
    full_out = dense_full[:, qkv_cols : qkv_cols + width]
    full_router = dense_full[:, qkv_cols + width : qkv_cols + width + n_route]
    gain_one = dense_full[:, -2].astype(jnp.float32)
    gain_two = dense_full[:, -1].astype(jnp.float32)

    back_rows = w_back.shape[1]
    expert_local = jnp.stack(
        [w_in[0], w_back[0].reshape(back_rows * width // ff, ff)], axis=0
    )
    expert_full = lax.all_gather(expert_local, "shard", axis=1, tiled=True)
    expert_first = expert_full[0]
    expert_second = expert_full[1].reshape(ff, width)

    token_f = tokens.astype(jnp.float32)
    attn_in = lax.optimization_barrier(layer_norm(token_f, gain_one).astype(jnp.bfloat16))
    projected = jnp.dot(attn_in, full_qkv, preferred_element_type=jnp.float32).astype(jnp.bfloat16)
    pad_rows = -(-rows // 128) * 128
    projected_pad = jnp.pad(projected, ((0, pad_rows - rows), (0, 0)))
    mixed_pad, attn_probs = attention_fwd(projected_pad, images)
    mixed_rows = mixed_pad[:rows]
    hidden_state = token_f + jnp.dot(mixed_rows, full_out, preferred_element_type=jnp.float32)
    moe_in = layer_norm(hidden_state, gain_two).astype(jnp.bfloat16)
    logits = jnp.dot(moe_in, full_router, preferred_element_type=jnp.float32)
    router_probs = normalize_rows(logits)
    expert_ids = jnp.arange(experts, dtype=jnp.int32)
    choose = (routes[:, :, None] == expert_ids).astype(jnp.float32)
    chosen = jnp.sum(choose * router_probs[:, None, :], axis=2)
    pick_table = (routes[:, :, None] == expert_ids).astype(jnp.int32) * live_int[:, None, None]
    flat_picks = pick_table.reshape(rows * 2, experts)
    before = jnp.cumsum(flat_picks, axis=0) - flat_picks
    slot_index = jnp.sum(before * flat_picks, axis=1).reshape(rows, 2)
    position = jnp.where(live_int[:, None] > 0, routes * capacity + slot_index, overflow)

    n_chunks = 2
    part_cap = 8 * ((capacity + 8 * n_chunks - 1) // (8 * n_chunks))
    chunk_sizes = [min(part_cap, capacity - k * part_cap) for k in range(n_chunks)]
    chunk_sizes = [size for size in chunk_sizes if size > 0]
    chunk_starts = [sum(chunk_sizes[:k]) for k in range(len(chunk_sizes))]
    slot_ids = jnp.concatenate(
        [
            (
                jnp.arange(experts, dtype=jnp.int32)[:, None] * capacity
                + start
                + jnp.arange(size, dtype=jnp.int32)[None, :]
            ).reshape(-1)
            for start, size in zip(chunk_starts, chunk_sizes)
        ]
    )[:, None]
    take_first = (slot_ids == position[None, :, 0]).astype(jnp.bfloat16)
    take_second = (slot_ids == position[None, :, 1]).astype(jnp.bfloat16)

    grad_out = cotangent.astype(jnp.float32) * live_rows[:, None]
    weighted = chosen * live_rows[:, None]
    grad_picked = (weighted[:, :, None] * grad_out[:, None, :]).astype(jnp.bfloat16)

    def dispatch_rows(low, high):
        first = take_first[low:high]
        second = take_second[low:high]
        sent_rows = jnp.dot(first + second, moe_in, preferred_element_type=jnp.float32)
        sent_grad = jnp.dot(
            first, grad_picked[:, 0], preferred_element_type=jnp.float32
        ) + jnp.dot(second, grad_picked[:, 1], preferred_element_type=jnp.float32)
        return jnp.concatenate([sent_rows, sent_grad], axis=1).astype(jnp.bfloat16)

    grad_first = None
    grad_second = None
    returned_parts = []
    for start, size in zip(chunk_starts, chunk_sizes):
        arrived = lax.all_to_all(
            dispatch_rows(experts * start, experts * (start + size)).reshape(
                experts, size, 2 * width
            ),
            "expert",
            split_axis=0,
            concat_axis=0,
            tiled=True,
        ).reshape(experts * size, 2 * width)
        flat_arrived = arrived[:, :width]
        flat_grad = arrived[:, width:]
        hidden_grad = lax.dot_general(
            flat_grad, expert_second, COL_CONTRACT, preferred_element_type=jnp.float32
        )
        pre_act = jnp.dot(flat_arrived, expert_first, preferred_element_type=jnp.float32)
        activated, slope = gelu_parts(pre_act)
        activated = activated.astype(jnp.bfloat16)
        pre_grad = (hidden_grad * slope).astype(jnp.bfloat16)
        produced = jnp.dot(
            activated, expert_second, preferred_element_type=jnp.float32
        ).astype(jnp.bfloat16)
        row_grad = lax.dot_general(
            pre_grad, expert_first, COL_CONTRACT, preferred_element_type=jnp.float32
        ).astype(jnp.bfloat16)
        part_second = lax.dot_general(
            activated, flat_grad, ROW_CONTRACT, preferred_element_type=jnp.float32
        )
        part_first = lax.dot_general(
            flat_arrived, pre_grad, ROW_CONTRACT, preferred_element_type=jnp.float32
        )
        grad_first = part_first if grad_first is None else grad_first + part_first
        grad_second = part_second if grad_second is None else grad_second + part_second
        returning = jnp.concatenate([produced, row_grad], axis=1).reshape(
            experts, size, 2 * width
        )
        returned_parts.append(
            lax.all_to_all(returning, "expert", split_axis=0, concat_axis=0, tiled=True)
        )

    expert_grads = jnp.stack(
        [grad_first, grad_second.reshape(width, ff)], axis=0
    ).astype(jnp.bfloat16)
    expert_share = lax.psum_scatter(expert_grads, "shard", scatter_dimension=1, tiled=True)
    expert_share = expert_share.astype(jnp.float32)
    grad_in_share = expert_share[0][None]
    grad_back_share = expert_share[1].reshape(back_rows, width)[None]

    picked_first = None
    picked_second = None
    for start, size, part in zip(chunk_starts, chunk_sizes, returned_parts):
        low, high = experts * start, experts * (start + size)
        part = part.reshape(-1, 2 * width)
        part_first = lax.dot_general(
            take_first[low:high], part, ROW_CONTRACT, preferred_element_type=jnp.float32
        )
        part_second = lax.dot_general(
            take_second[low:high], part, ROW_CONTRACT, preferred_element_type=jnp.float32
        )
        picked_first = part_first if picked_first is None else picked_first + part_first
        picked_second = part_second if picked_second is None else picked_second + part_second
    moe_out = (
        weighted[:, 0:1] * picked_first[:, :width] + weighted[:, 1:2] * picked_second[:, :width]
    )
    output = (live_rows[:, None] * (hidden_state + moe_out)).astype(jnp.bfloat16)
    grad_chosen = jnp.stack(
        [
            jnp.sum(grad_out * picked_first[:, :width], axis=1),
            jnp.sum(grad_out * picked_second[:, :width], axis=1),
        ],
        axis=1,
    ) * live_rows[:, None]
    expert_part = (picked_first[:, width:] + picked_second[:, width:]) * live_rows[:, None]
    prob_sum = jnp.sum(choose * grad_chosen[:, :, None], axis=1)
    logit_grad = (
        router_probs * (prob_sum - jnp.sum(router_probs * prob_sum, axis=-1, keepdims=True))
    ).astype(jnp.bfloat16)
    grad_router = lax.dot_general(
        moe_in, logit_grad, ROW_CONTRACT, preferred_element_type=jnp.float32
    )
    moe_in_grad = expert_part + lax.dot_general(
        logit_grad, full_router, COL_CONTRACT, preferred_element_type=jnp.float32
    )
    _, norm_back = jax.vjp(layer_norm, hidden_state, gain_two)
    state_part, grad_gain_two = norm_back(moe_in_grad)
    state_grad = grad_out + state_part
    branch_grad = state_grad.astype(jnp.bfloat16)
    grad_wout = lax.dot_general(
        mixed_rows, branch_grad, ROW_CONTRACT, preferred_element_type=jnp.float32
    )
    mixed_grad = lax.dot_general(
        branch_grad, full_out, COL_CONTRACT, preferred_element_type=jnp.float32
    )
    mixed_grad = jnp.pad(mixed_grad.astype(jnp.bfloat16), ((0, pad_rows - rows), (0, 0)))
    grad_q, grad_k, grad_v = attention_bwd(projected_pad, mixed_grad, attn_probs)
    projected_grad = jnp.concatenate([grad_q, grad_k, grad_v], axis=1)
    attn_in_pad = jnp.pad(attn_in, ((0, pad_rows - rows), (0, 0)))
    grad_qkv = lax.dot_general(
        attn_in_pad, projected_grad, ROW_CONTRACT, preferred_element_type=jnp.float32
    )
    attn_in_grad = lax.dot_general(
        projected_grad[:rows], full_qkv, COL_CONTRACT, preferred_element_type=jnp.float32
    )
    _, first_back = jax.vjp(layer_norm, token_f, gain_one)
    token_part, grad_gain_one = first_back(attn_in_grad)
    grad_tokens = (state_grad + token_part).astype(jnp.bfloat16)

    small = jnp.concatenate(
        [grad_router, grad_gain_one[:, None], grad_gain_two[:, None]], axis=1
    )
    small = jnp.pad(small, ((0, 0), (0, 128 - small.shape[1])))
    dense_grads = jnp.concatenate([grad_qkv, grad_wout, small], axis=1)
    chunk_cols = 128 * (dense_grads.shape[1] // 256)
    dense_total = jnp.concatenate(
        [
            expert_all_reduce(
                shard_reduce_scatter(part, "shard", 128 * (part.shape[1] // 256)), "expert"
            )
            for part in (dense_grads[:, :chunk_cols], dense_grads[:, chunk_cols:])
        ],
        axis=1,
    )
    return (
        output,
        grad_tokens,
        dense_total[:, :qkv_cols],
        dense_total[:, qkv_cols : qkv_cols + width],
        dense_total[:, qkv_cols + width : qkv_cols + width + n_route],
        dense_total[:, qkv_cols + width + n_route],
        dense_total[:, qkv_cols + width + n_route + 1],
        grad_in_share,
        grad_back_share,
    )


def solution(mesh):
    return _mapped(mesh)


def _mapped(mesh):
    return jax.shard_map(
        shards,
        mesh=mesh,
        in_specs=(
            P(("expert", "shard"), None),
            P("expert", "shard"),
            P(("expert", "shard"), None),
            P("shard", None),
            P("shard", None),
            P("shard", None),
            P("shard"),
            P("shard"),
            P("expert", "shard", None),
            P("expert", "shard", None),
            P(("expert", "shard"), None),
        ),
        out_specs=(
            P(("expert", "shard"), None),
            P(("expert", "shard"), None),
            P("shard", None),
            P("shard", None),
            P("shard", None),
            P("shard"),
            P("shard"),
            P("expert", "shard", None),
            P("expert", "shard", None),
        ),
        check_vma=False,
    )
```

```python
import functools

import jax
import numpy as np
import jax.numpy as jnp
from jax import lax
from jax.experimental import pallas as pl
from jax.experimental.pallas import tpu as pltpu
from jax.sharding import PartitionSpec as P

HD = 64
SEQ = 197


EPSILON = 1e-06
ROW_CONTRACT = (((0,), (0,)), ((), ()))
COL_CONTRACT = (((1,), (1,)), ((), ()))


def _image_of(idx, images):
    count = jnp.zeros(idx.shape, jnp.int32)
    for i in range(1, images + 1):
        count = count + (idx >= i * SEQ).astype(jnp.int32)
    return count


def _same_image(size, images):
    rows = lax.broadcasted_iota(jnp.int32, (size, size), 0)
    cols = lax.broadcasted_iota(jnp.int32, (size, size), 1)
    return _image_of(rows, images) == _image_of(cols, images)


def _softmax_masked(qj, k, same):
    s = lax.dot_general(qj, k, COL_CONTRACT, preferred_element_type=jnp.float32) * (HD ** -0.5)
    s = jnp.where(same, s, -jnp.inf)
    top = jnp.max(s, axis=1, keepdims=True)
    e = jnp.exp(s - top)
    return e / jnp.sum(e, axis=1, keepdims=True)


def attn_fwd_kernel(q_ref, k_ref, v_ref, o_ref, *, images):
    R = q_ref.shape[0]
    q = q_ref[...]
    k = k_ref[...]
    v = v_ref[...]
    same = _same_image(R, images)
    lane = lax.broadcasted_iota(jnp.int32, (1, 2 * HD), 1)
    out = jnp.zeros((R, 2 * HD), jnp.float32)
    for j in range(2):
        in_head = (lane >= HD) == (j == 1)
        p = _softmax_masked(jnp.where(in_head, q, jnp.zeros_like(q)), k, same)
        o = jnp.dot(p.astype(jnp.bfloat16), v, preferred_element_type=jnp.float32)
        out = jnp.where(in_head, o, out)
    o_ref[...] = out.astype(o_ref.dtype)


def attn_bwd_kernel(q_ref, k_ref, v_ref, g_ref, dq_ref, dk_ref, dv_ref, *, images):
    R = q_ref.shape[0]
    q = q_ref[...]
    k = k_ref[...]
    v = v_ref[...]
    g = g_ref[...]
    same = _same_image(R, images)
    lane = lax.broadcasted_iota(jnp.int32, (1, 2 * HD), 1)
    dq = jnp.zeros((R, 2 * HD), jnp.float32)
    dk = jnp.zeros((R, 2 * HD), jnp.float32)
    dv = jnp.zeros((R, 2 * HD), jnp.float32)
    for j in range(2):
        in_head = (lane >= HD) == (j == 1)
        p = _softmax_masked(jnp.where(in_head, q, jnp.zeros_like(q)), k, same)
        gj = jnp.where(in_head, g, jnp.zeros_like(g))
        dp = lax.dot_general(gj, v, COL_CONTRACT, preferred_element_type=jnp.float32)
        ds = (p * (dp - jnp.sum(p * dp, axis=1, keepdims=True))).astype(jnp.bfloat16)
        dq_j = jnp.dot(ds, k, preferred_element_type=jnp.float32) * (HD ** -0.5)
        dk_j = lax.dot_general(ds, q, ROW_CONTRACT, preferred_element_type=jnp.float32) * (HD ** -0.5)
        dv_j = lax.dot_general(p.astype(jnp.bfloat16), g, ROW_CONTRACT, preferred_element_type=jnp.float32)
        dq = jnp.where(in_head, dq_j, dq)
        dk = jnp.where(in_head, dk_j, dk)
        dv = jnp.where(in_head, dv_j, dv)
    dq_ref[...] = dq.astype(dq_ref.dtype)
    dk_ref[...] = dk.astype(dk_ref.dtype)
    dv_ref[...] = dv.astype(dv_ref.dtype)


def attention_fwd(projected, images):
    R = projected.shape[0]
    W = projected.shape[1] // 3
    pairs = W // (2 * HD)
    blk = lambda off: pl.BlockSpec((R, 2 * HD), lambda h: (0, off + h))
    return pl.pallas_call(
        functools.partial(attn_fwd_kernel, images=images),
        grid=(pairs,),
        in_specs=[blk(0), blk(pairs), blk(2 * pairs)],
        out_specs=blk(0),
        out_shape=jax.ShapeDtypeStruct((R, W), jnp.bfloat16),
        compiler_params=pltpu.CompilerParams(vmem_limit_bytes=48 * 1024 * 1024),
    )(projected, projected, projected)


def attention_bwd(projected, mixed_grad, images):
    R = projected.shape[0]
    W = projected.shape[1] // 3
    pairs = W // (2 * HD)
    blk = lambda off: pl.BlockSpec((R, 2 * HD), lambda h: (0, off + h))
    out = jax.ShapeDtypeStruct((R, W), jnp.bfloat16)
    return pl.pallas_call(
        functools.partial(attn_bwd_kernel, images=images),
        grid=(pairs,),
        in_specs=[blk(0), blk(pairs), blk(2 * pairs), blk(0)],
        out_specs=[blk(0), blk(0), blk(0)],
        out_shape=[out, out, out],
        compiler_params=pltpu.CompilerParams(vmem_limit_bytes=48 * 1024 * 1024),
    )(projected, projected, projected, mixed_grad)


def _exchange(values, bits_left, bit, axis_name, size, index):
    axis = bits_left.index(bit)
    mine = (index >> bit) & 1
    keep = lax.dynamic_index_in_dim(values, mine, axis, keepdims=False)
    send = lax.dynamic_index_in_dim(values, 1 - mine, axis, keepdims=False)
    pairs = [(i, i ^ (1 << bit)) for i in range(size)]
    got = lax.ppermute(send.astype(jnp.bfloat16), axis_name, pairs)
    return keep + got.astype(jnp.float32), [b for b in bits_left if b != bit]


def shard_reduce_scatter(values, axis_name, split_col):
    size = lax.axis_size(axis_name)
    index = lax.axis_index(axis_name)
    n_bits = size.bit_length() - 1
    block = values.shape[0] // size
    bits = list(range(n_bits - 1, -1, -1))
    values = values.astype(jnp.float32).reshape([2] * n_bits + [block, values.shape[1]])
    values, bits = _exchange(values, bits, 0, axis_name, size, index)
    first, second = values[..., :split_col], values[..., split_col:]
    first_bits, second_bits = list(bits), list(bits)
    for up, down in zip(range(1, n_bits), range(n_bits - 1, 0, -1)):
        first, first_bits = _exchange(first, first_bits, up, axis_name, size, index)
        second, second_bits = _exchange(second, second_bits, down, axis_name, size, index)
    return jnp.concatenate([first, second], axis=-1)


def _gather_back(values, bit, axis_name, size, index):
    n_bits = size.bit_length() - 1
    mine = (index >> bit) & 1
    pairs = [(i, i ^ (1 << bit)) for i in range(size)]
    got = lax.ppermute(values, axis_name, pairs)
    low = jnp.where(mine == 0, values, got)
    high = jnp.where(mine == 0, got, values)
    return jnp.stack([low, high], axis=n_bits - 1 - bit)


def expert_all_reduce(values, axis_name):
    size = lax.axis_size(axis_name)
    index = lax.axis_index(axis_name)
    n_bits = size.bit_length() - 1
    rows = values.shape[0]
    if rows % size:
        return lax.psum(values.astype(jnp.bfloat16), axis_name).astype(jnp.float32)
    bits = list(range(n_bits - 1, -1, -1))
    parts = values.astype(jnp.float32).reshape([2] * n_bits + [rows // size, values.shape[1]])
    for bit in range(n_bits):
        parts, bits = _exchange(parts, bits, bit, axis_name, size, index)
    parts = parts.astype(jnp.bfloat16)
    for bit in range(n_bits - 1, -1, -1):
        parts = _gather_back(parts, bit, axis_name, size, index)
    return parts.reshape(rows, values.shape[1]).astype(jnp.float32)


def layer_norm(values, norm_gain):
    row_mean = jnp.mean(values, axis=-1, keepdims=True)
    centered = values - row_mean
    variance = jnp.mean(centered * centered, axis=-1, keepdims=True)
    return centered * lax.rsqrt(variance + EPSILON) * norm_gain


def normalize_rows(scores):
    row_top = jnp.max(scores, axis=-1, keepdims=True)
    exp_scores = jnp.exp(scores - row_top)
    return exp_scores / jnp.sum(exp_scores, axis=-1, keepdims=True)


def gelu_parts(values):
    sqrt_half = np.float32(np.sqrt(0.5))
    tail = lax.erfc(-values * sqrt_half)
    density = jnp.exp(-0.5 * values * values) * np.float32(1.0 / np.sqrt(2.0 * np.pi))
    return 0.5 * values * tail, 0.5 * tail + values * density


def shards(
    tokens,
    image_counts,
    routes,
    w_qkv,
    w_out,
    w_router,
    gain_attn,
    gain_moe,
    w_in,
    w_back,
    cotangent,
):
    rows, width = tokens.shape
    experts = lax.axis_size("expert")
    capacity = 8 * (5 * rows // (16 * experts)) + 8
    overflow = experts * capacity
    images = rows // SEQ
    qkv_cols = w_qkv.shape[1]
    n_route = w_router.shape[1]
    ff = w_in.shape[2]
    row_ids = jnp.arange(rows, dtype=jnp.int32)
    live_int = (row_ids // SEQ < image_counts[0, 0]).astype(jnp.int32)
    live_rows = live_int.astype(jnp.float32)

    dense_local = jnp.concatenate(
        [w_qkv, w_out, w_router, gain_attn[:, None], gain_moe[:, None]], axis=1
    )
    dense_full = lax.all_gather(dense_local, "shard", axis=0, tiled=True)
    full_qkv = dense_full[:, :qkv_cols]
    full_out = dense_full[:, qkv_cols : qkv_cols + width]
    full_router = dense_full[:, qkv_cols + width : qkv_cols + width + n_route]
    gain_one = dense_full[:, -2].astype(jnp.float32)
    gain_two = dense_full[:, -1].astype(jnp.float32)

    back_rows = w_back.shape[1]
    expert_local = jnp.stack(
        [w_in[0], w_back[0].reshape(back_rows * width // ff, ff)], axis=0
    )
    expert_full = lax.all_gather(expert_local, "shard", axis=1, tiled=True)
    expert_first = expert_full[0]
    expert_second = expert_full[1].reshape(ff, width)

    token_f = tokens.astype(jnp.float32)
    attn_in = lax.optimization_barrier(layer_norm(token_f, gain_one).astype(jnp.bfloat16))
    projected = jnp.dot(attn_in, full_qkv, preferred_element_type=jnp.float32).astype(jnp.bfloat16)
    pad_rows = -(-rows // 128) * 128
    projected_pad = jnp.pad(projected, ((0, pad_rows - rows), (0, 0)))
    mixed_rows = attention_fwd(projected_pad, images)[:rows]
    hidden_state = token_f + jnp.dot(mixed_rows, full_out, preferred_element_type=jnp.float32)
    moe_in = layer_norm(hidden_state, gain_two).astype(jnp.bfloat16)
    logits = jnp.dot(moe_in, full_router, preferred_element_type=jnp.float32)
    router_probs = normalize_rows(logits)
    expert_ids = jnp.arange(experts, dtype=jnp.int32)
    choose = (routes[:, :, None] == expert_ids).astype(jnp.float32)
    chosen = jnp.sum(choose * router_probs[:, None, :], axis=2)
    pick_table = (routes[:, :, None] == expert_ids).astype(jnp.int32) * live_int[:, None, None]
    flat_picks = pick_table.reshape(rows * 2, experts)
    before = jnp.cumsum(flat_picks, axis=0) - flat_picks
    slot_index = jnp.sum(before * flat_picks, axis=1).reshape(rows, 2)
    position = jnp.where(live_int[:, None] > 0, routes * capacity + slot_index, overflow)

    n_chunks = 2
    part_cap = 8 * ((capacity + 8 * n_chunks - 1) // (8 * n_chunks))
    chunk_sizes = [min(part_cap, capacity - k * part_cap) for k in range(n_chunks)]
    chunk_sizes = [size for size in chunk_sizes if size > 0]
    chunk_starts = [sum(chunk_sizes[:k]) for k in range(len(chunk_sizes))]
    slot_ids = jnp.concatenate(
        [
            (
                jnp.arange(experts, dtype=jnp.int32)[:, None] * capacity
                + start
                + jnp.arange(size, dtype=jnp.int32)[None, :]
            ).reshape(-1)
            for start, size in zip(chunk_starts, chunk_sizes)
        ]
    )[:, None]
    take_first = (slot_ids == position[None, :, 0]).astype(jnp.bfloat16)
    take_second = (slot_ids == position[None, :, 1]).astype(jnp.bfloat16)

    grad_out = cotangent.astype(jnp.float32) * live_rows[:, None]
    weighted = chosen * live_rows[:, None]
    grad_picked = (weighted[:, :, None] * grad_out[:, None, :]).astype(jnp.bfloat16)

    def dispatch_rows(low, high):
        first = take_first[low:high]
        second = take_second[low:high]
        sent_rows = jnp.dot(first + second, moe_in, preferred_element_type=jnp.float32)
        sent_grad = jnp.dot(
            first, grad_picked[:, 0], preferred_element_type=jnp.float32
        ) + jnp.dot(second, grad_picked[:, 1], preferred_element_type=jnp.float32)
        return jnp.concatenate([sent_rows, sent_grad], axis=1).astype(jnp.bfloat16)

    grad_first = None
    grad_second = None
    returned_parts = []
    for start, size in zip(chunk_starts, chunk_sizes):
        arrived = lax.all_to_all(
            dispatch_rows(experts * start, experts * (start + size)).reshape(
                experts, size, 2 * width
            ),
            "expert",
            split_axis=0,
            concat_axis=0,
            tiled=True,
        ).reshape(experts * size, 2 * width)
        flat_arrived = arrived[:, :width]
        flat_grad = arrived[:, width:]
        hidden_grad = lax.dot_general(
            flat_grad, expert_second, COL_CONTRACT, preferred_element_type=jnp.float32
        )
        pre_act = jnp.dot(flat_arrived, expert_first, preferred_element_type=jnp.float32)
        activated, slope = gelu_parts(pre_act)
        activated = activated.astype(jnp.bfloat16)
        pre_grad = (hidden_grad * slope).astype(jnp.bfloat16)
        produced = jnp.dot(
            activated, expert_second, preferred_element_type=jnp.float32
        ).astype(jnp.bfloat16)
        row_grad = lax.dot_general(
            pre_grad, expert_first, COL_CONTRACT, preferred_element_type=jnp.float32
        ).astype(jnp.bfloat16)
        part_second = lax.dot_general(
            activated, flat_grad, ROW_CONTRACT, preferred_element_type=jnp.float32
        )
        part_first = lax.dot_general(
            flat_arrived, pre_grad, ROW_CONTRACT, preferred_element_type=jnp.float32
        )
        grad_first = part_first if grad_first is None else grad_first + part_first
        grad_second = part_second if grad_second is None else grad_second + part_second
        returning = jnp.concatenate([produced, row_grad], axis=1).reshape(
            experts, size, 2 * width
        )
        returned_parts.append(
            lax.all_to_all(returning, "expert", split_axis=0, concat_axis=0, tiled=True)
        )

    expert_grads = jnp.stack(
        [grad_first, grad_second.reshape(width, ff)], axis=0
    ).astype(jnp.bfloat16)
    expert_share = lax.psum_scatter(expert_grads, "shard", scatter_dimension=1, tiled=True)
    expert_share = expert_share.astype(jnp.float32)
    grad_in_share = expert_share[0][None]
    grad_back_share = expert_share[1].reshape(back_rows, width)[None]

    picked_first = None
    picked_second = None
    for start, size, part in zip(chunk_starts, chunk_sizes, returned_parts):
        low, high = experts * start, experts * (start + size)
        part = part.reshape(-1, 2 * width)
        part_first = lax.dot_general(
            take_first[low:high], part, ROW_CONTRACT, preferred_element_type=jnp.float32
        )
        part_second = lax.dot_general(
            take_second[low:high], part, ROW_CONTRACT, preferred_element_type=jnp.float32
        )
        picked_first = part_first if picked_first is None else picked_first + part_first
        picked_second = part_second if picked_second is None else picked_second + part_second
    moe_out = (
        weighted[:, 0:1] * picked_first[:, :width] + weighted[:, 1:2] * picked_second[:, :width]
    )
    output = (live_rows[:, None] * (hidden_state + moe_out)).astype(jnp.bfloat16)
    grad_chosen = jnp.stack(
        [
            jnp.sum(grad_out * picked_first[:, :width], axis=1),
            jnp.sum(grad_out * picked_second[:, :width], axis=1),
        ],
        axis=1,
    ) * live_rows[:, None]
    expert_part = (picked_first[:, width:] + picked_second[:, width:]) * live_rows[:, None]
    prob_sum = jnp.sum(choose * grad_chosen[:, :, None], axis=1)
    logit_grad = (
        router_probs * (prob_sum - jnp.sum(router_probs * prob_sum, axis=-1, keepdims=True))
    ).astype(jnp.bfloat16)
    grad_router = lax.dot_general(
        moe_in, logit_grad, ROW_CONTRACT, preferred_element_type=jnp.float32
    )
    moe_in_grad = expert_part + lax.dot_general(
        logit_grad, full_router, COL_CONTRACT, preferred_element_type=jnp.float32
    )
    _, norm_back = jax.vjp(layer_norm, hidden_state, gain_two)
    state_part, grad_gain_two = norm_back(moe_in_grad)
    state_grad = grad_out + state_part
    branch_grad = state_grad.astype(jnp.bfloat16)
    grad_wout = lax.dot_general(
        mixed_rows, branch_grad, ROW_CONTRACT, preferred_element_type=jnp.float32
    )
    mixed_grad = lax.dot_general(
        branch_grad, full_out, COL_CONTRACT, preferred_element_type=jnp.float32
    )
    mixed_grad = jnp.pad(mixed_grad.astype(jnp.bfloat16), ((0, pad_rows - rows), (0, 0)))
    grad_q, grad_k, grad_v = attention_bwd(projected_pad, mixed_grad, images)
    projected_grad = jnp.concatenate([grad_q, grad_k, grad_v], axis=1)
    attn_in_pad = jnp.pad(attn_in, ((0, pad_rows - rows), (0, 0)))
    grad_qkv = lax.dot_general(
        attn_in_pad, projected_grad, ROW_CONTRACT, preferred_element_type=jnp.float32
    )
    attn_in_grad = lax.dot_general(
        projected_grad[:rows], full_qkv, COL_CONTRACT, preferred_element_type=jnp.float32
    )
    _, first_back = jax.vjp(layer_norm, token_f, gain_one)
    token_part, grad_gain_one = first_back(attn_in_grad)
    grad_tokens = (state_grad + token_part).astype(jnp.bfloat16)

    small = jnp.concatenate(
        [grad_router, grad_gain_one[:, None], grad_gain_two[:, None]], axis=1
    )
    small = jnp.pad(small, ((0, 0), (0, 128 - small.shape[1])))
    dense_grads = jnp.concatenate([grad_qkv, grad_wout, small], axis=1)
    dense_total = expert_all_reduce(
        shard_reduce_scatter(dense_grads, "shard", 128 * (dense_grads.shape[1] // 256)), "expert"
    )
    return (
        output,
        grad_tokens,
        dense_total[:, :qkv_cols],
        dense_total[:, qkv_cols : qkv_cols + width],
        dense_total[:, qkv_cols + width : qkv_cols + width + n_route],
        dense_total[:, qkv_cols + width + n_route],
        dense_total[:, qkv_cols + width + n_route + 1],
        grad_in_share,
        grad_back_share,
    )


def solution(mesh):
    return _mapped(mesh)


def _mapped(mesh):
    return jax.shard_map(
        shards,
        mesh=mesh,
        in_specs=(
            P(("expert", "shard"), None),
            P("expert", "shard"),
            P(("expert", "shard"), None),
            P("shard", None),
            P("shard", None),
            P("shard", None),
            P("shard"),
            P("shard"),
            P("expert", "shard", None),
            P("expert", "shard", None),
            P(("expert", "shard"), None),
        ),
        out_specs=(
            P(("expert", "shard"), None),
            P(("expert", "shard"), None),
            P("shard", None),
            P("shard", None),
            P("shard", None),
            P("shard"),
            P("shard"),
            P("expert", "shard", None),
            P("expert", "shard", None),
        ),
        check_vma=False,
    )
```

```python
import functools

import jax
import numpy as np
import jax.numpy as jnp
from jax import lax
from jax.experimental import pallas as pl
from jax.experimental.pallas import tpu as pltpu
from jax.sharding import PartitionSpec as P

HD = 64
SEQ = 197


EPSILON = 1e-06
ROW_CONTRACT = (((0,), (0,)), ((), ()))
COL_CONTRACT = (((1,), (1,)), ((), ()))


def _image_of(idx, images):
    count = jnp.zeros(idx.shape, jnp.int32)
    for i in range(1, images + 1):
        count = count + (idx >= i * SEQ).astype(jnp.int32)
    return count


def _same_image(size, images):
    rows = lax.broadcasted_iota(jnp.int32, (size, size), 0)
    cols = lax.broadcasted_iota(jnp.int32, (size, size), 1)
    return _image_of(rows, images) == _image_of(cols, images)


def _softmax_masked(qj, k, same):
    s = lax.dot_general(qj, k, COL_CONTRACT, preferred_element_type=jnp.float32) * (HD ** -0.5)
    s = jnp.where(same, s, -jnp.inf)
    top = jnp.max(s, axis=1, keepdims=True)
    e = jnp.exp(s - top)
    return e / jnp.sum(e, axis=1, keepdims=True)


def attn_fwd_kernel(q_ref, k_ref, v_ref, o_ref, *, images):
    R = q_ref.shape[0]
    q = q_ref[...]
    k = k_ref[...]
    v = v_ref[...]
    same = _same_image(R, images)
    lane = lax.broadcasted_iota(jnp.int32, (1, 2 * HD), 1)
    out = jnp.zeros((R, 2 * HD), jnp.float32)
    for j in range(2):
        in_head = (lane >= HD) == (j == 1)
        p = _softmax_masked(jnp.where(in_head, q, jnp.zeros_like(q)), k, same)
        o = jnp.dot(p.astype(jnp.bfloat16), v, preferred_element_type=jnp.float32)
        out = jnp.where(in_head, o, out)
    o_ref[...] = out.astype(o_ref.dtype)


def attn_bwd_kernel(q_ref, k_ref, v_ref, g_ref, dq_ref, dk_ref, dv_ref, *, images):
    R = q_ref.shape[0]
    q = q_ref[...]
    k = k_ref[...]
    v = v_ref[...]
    g = g_ref[...]
    same = _same_image(R, images)
    lane = lax.broadcasted_iota(jnp.int32, (1, 2 * HD), 1)
    dq = jnp.zeros((R, 2 * HD), jnp.float32)
    dk = jnp.zeros((R, 2 * HD), jnp.float32)
    dv = jnp.zeros((R, 2 * HD), jnp.float32)
    for j in range(2):
        in_head = (lane >= HD) == (j == 1)
        p = _softmax_masked(jnp.where(in_head, q, jnp.zeros_like(q)), k, same)
        gj = jnp.where(in_head, g, jnp.zeros_like(g))
        dp = lax.dot_general(gj, v, COL_CONTRACT, preferred_element_type=jnp.float32)
        ds = (p * (dp - jnp.sum(p * dp, axis=1, keepdims=True))).astype(jnp.bfloat16)
        dq_j = jnp.dot(ds, k, preferred_element_type=jnp.float32) * (HD ** -0.5)
        dk_j = lax.dot_general(ds, q, ROW_CONTRACT, preferred_element_type=jnp.float32) * (HD ** -0.5)
        dv_j = lax.dot_general(p.astype(jnp.bfloat16), g, ROW_CONTRACT, preferred_element_type=jnp.float32)
        dq = jnp.where(in_head, dq_j, dq)
        dk = jnp.where(in_head, dk_j, dk)
        dv = jnp.where(in_head, dv_j, dv)
    dq_ref[...] = dq.astype(dq_ref.dtype)
    dk_ref[...] = dk.astype(dk_ref.dtype)
    dv_ref[...] = dv.astype(dv_ref.dtype)


def attention_fwd(projected, images):
    R = projected.shape[0]
    W = projected.shape[1] // 3
    pairs = W // (2 * HD)
    blk = lambda off: pl.BlockSpec((R, 2 * HD), lambda h: (0, off + h))
    return pl.pallas_call(
        functools.partial(attn_fwd_kernel, images=images),
        grid=(pairs,),
        in_specs=[blk(0), blk(pairs), blk(2 * pairs)],
        out_specs=blk(0),
        out_shape=jax.ShapeDtypeStruct((R, W), jnp.bfloat16),
        compiler_params=pltpu.CompilerParams(vmem_limit_bytes=48 * 1024 * 1024),
    )(projected, projected, projected)


def attention_bwd(projected, mixed_grad, images):
    R = projected.shape[0]
    W = projected.shape[1] // 3
    pairs = W // (2 * HD)
    blk = lambda off: pl.BlockSpec((R, 2 * HD), lambda h: (0, off + h))
    out = jax.ShapeDtypeStruct((R, W), jnp.bfloat16)
    return pl.pallas_call(
        functools.partial(attn_bwd_kernel, images=images),
        grid=(pairs,),
        in_specs=[blk(0), blk(pairs), blk(2 * pairs), blk(0)],
        out_specs=[blk(0), blk(0), blk(0)],
        out_shape=[out, out, out],
        compiler_params=pltpu.CompilerParams(vmem_limit_bytes=48 * 1024 * 1024),
    )(projected, projected, projected, mixed_grad)


def _exchange(values, bits_left, bit, axis_name, size, index):
    axis = bits_left.index(bit)
    mine = (index >> bit) & 1
    keep = lax.dynamic_index_in_dim(values, mine, axis, keepdims=False)
    send = lax.dynamic_index_in_dim(values, 1 - mine, axis, keepdims=False)
    pairs = [(i, i ^ (1 << bit)) for i in range(size)]
    got = lax.ppermute(send.astype(jnp.bfloat16), axis_name, pairs)
    return keep + got.astype(jnp.float32), [b for b in bits_left if b != bit]


def shard_reduce_scatter(values, axis_name, split_col):
    size = lax.axis_size(axis_name)
    index = lax.axis_index(axis_name)
    n_bits = size.bit_length() - 1
    block = values.shape[0] // size
    bits = list(range(n_bits - 1, -1, -1))
    values = values.astype(jnp.float32).reshape([2] * n_bits + [block, values.shape[1]])
    values, bits = _exchange(values, bits, 0, axis_name, size, index)
    first, second = values[..., :split_col], values[..., split_col:]
    first_bits, second_bits = list(bits), list(bits)
    for up, down in zip(range(1, n_bits), range(n_bits - 1, 0, -1)):
        first, first_bits = _exchange(first, first_bits, up, axis_name, size, index)
        second, second_bits = _exchange(second, second_bits, down, axis_name, size, index)
    return jnp.concatenate([first, second], axis=-1)


def _gather_back(values, bit, axis_name, size, index):
    n_bits = size.bit_length() - 1
    mine = (index >> bit) & 1
    pairs = [(i, i ^ (1 << bit)) for i in range(size)]
    got = lax.ppermute(values, axis_name, pairs)
    low = jnp.where(mine == 0, values, got)
    high = jnp.where(mine == 0, got, values)
    return jnp.stack([low, high], axis=n_bits - 1 - bit)


def expert_all_reduce(values, axis_name):
    size = lax.axis_size(axis_name)
    index = lax.axis_index(axis_name)
    n_bits = size.bit_length() - 1
    rows = values.shape[0]
    if rows % size:
        return lax.psum(values.astype(jnp.bfloat16), axis_name).astype(jnp.float32)
    bits = list(range(n_bits - 1, -1, -1))
    parts = values.astype(jnp.float32).reshape([2] * n_bits + [rows // size, values.shape[1]])
    for bit in range(n_bits):
        parts, bits = _exchange(parts, bits, bit, axis_name, size, index)
    parts = parts.astype(jnp.bfloat16)
    for bit in range(n_bits - 1, -1, -1):
        parts = _gather_back(parts, bit, axis_name, size, index)
    return parts.reshape(rows, values.shape[1]).astype(jnp.float32)


def layer_norm(values, norm_gain):
    row_mean = jnp.mean(values, axis=-1, keepdims=True)
    centered = values - row_mean
    variance = jnp.mean(centered * centered, axis=-1, keepdims=True)
    return centered * lax.rsqrt(variance + EPSILON) * norm_gain


def normalize_rows(scores):
    row_top = jnp.max(scores, axis=-1, keepdims=True)
    exp_scores = jnp.exp(scores - row_top)
    return exp_scores / jnp.sum(exp_scores, axis=-1, keepdims=True)


def gelu_parts(values):
    sqrt_half = np.float32(np.sqrt(0.5))
    tail = lax.erfc(-values * sqrt_half)
    density = jnp.exp(-0.5 * values * values) * np.float32(1.0 / np.sqrt(2.0 * np.pi))
    return 0.5 * values * tail, 0.5 * tail + values * density


def shards(
    tokens,
    image_counts,
    routes,
    w_qkv,
    w_out,
    w_router,
    gain_attn,
    gain_moe,
    w_in,
    w_back,
    cotangent,
):
    rows, width = tokens.shape
    experts = lax.axis_size("expert")
    capacity = 8 * (5 * rows // (16 * experts)) + 8
    overflow = experts * capacity
    images = rows // SEQ
    qkv_cols = w_qkv.shape[1]
    n_route = w_router.shape[1]
    ff = w_in.shape[2]
    row_ids = jnp.arange(rows, dtype=jnp.int32)
    live_int = (row_ids // SEQ < image_counts[0, 0]).astype(jnp.int32)
    live_rows = live_int.astype(jnp.float32)

    dense_local = jnp.concatenate(
        [w_qkv, w_out, w_router, gain_attn[:, None], gain_moe[:, None]], axis=1
    )
    dense_full = lax.all_gather(dense_local, "shard", axis=0, tiled=True)
    full_qkv = dense_full[:, :qkv_cols]
    full_out = dense_full[:, qkv_cols : qkv_cols + width]
    full_router = dense_full[:, qkv_cols + width : qkv_cols + width + n_route]
    gain_one = dense_full[:, -2].astype(jnp.float32)
    gain_two = dense_full[:, -1].astype(jnp.float32)

    back_rows = w_back.shape[1]
    expert_local = jnp.stack(
        [w_in[0], w_back[0].reshape(back_rows * width // ff, ff)], axis=0
    )
    expert_full = lax.all_gather(expert_local, "shard", axis=1, tiled=True)
    expert_first = expert_full[0]
    expert_second = expert_full[1].reshape(ff, width)

    token_f = tokens.astype(jnp.float32)
    attn_in = lax.optimization_barrier(layer_norm(token_f, gain_one).astype(jnp.bfloat16))
    projected = jnp.dot(attn_in, full_qkv, preferred_element_type=jnp.float32).astype(jnp.bfloat16)
    pad_rows = -(-rows // 128) * 128
    projected_pad = jnp.pad(projected, ((0, pad_rows - rows), (0, 0)))
    mixed_rows = attention_fwd(projected_pad, images)[:rows]
    hidden_state = token_f + jnp.dot(mixed_rows, full_out, preferred_element_type=jnp.float32)
    moe_in = layer_norm(hidden_state, gain_two).astype(jnp.bfloat16)
    logits = jnp.dot(moe_in, full_router, preferred_element_type=jnp.float32)
    router_probs = normalize_rows(logits)
    expert_ids = jnp.arange(experts, dtype=jnp.int32)
    choose = (routes[:, :, None] == expert_ids).astype(jnp.float32)
    chosen = jnp.sum(choose * router_probs[:, None, :], axis=2)
    pick_table = (routes[:, :, None] == expert_ids).astype(jnp.int32) * live_int[:, None, None]
    flat_picks = pick_table.reshape(rows * 2, experts)
    before = jnp.cumsum(flat_picks, axis=0) - flat_picks
    slot_index = jnp.sum(before * flat_picks, axis=1).reshape(rows, 2)
    position = jnp.where(live_int[:, None] > 0, routes * capacity + slot_index, overflow)

    n_chunks = 2
    part_cap = 8 * ((capacity + 8 * n_chunks - 1) // (8 * n_chunks))
    chunk_sizes = [min(part_cap, capacity - k * part_cap) for k in range(n_chunks)]
    chunk_sizes = [size for size in chunk_sizes if size > 0]
    chunk_starts = [sum(chunk_sizes[:k]) for k in range(len(chunk_sizes))]
    slot_ids = jnp.concatenate(
        [
            (
                jnp.arange(experts, dtype=jnp.int32)[:, None] * capacity
                + start
                + jnp.arange(size, dtype=jnp.int32)[None, :]
            ).reshape(-1)
            for start, size in zip(chunk_starts, chunk_sizes)
        ]
    )[:, None]
    take_first = (slot_ids == position[None, :, 0]).astype(jnp.bfloat16)
    take_second = (slot_ids == position[None, :, 1]).astype(jnp.bfloat16)

    grad_out = cotangent.astype(jnp.float32) * live_rows[:, None]
    weighted = chosen * live_rows[:, None]
    grad_picked = (weighted[:, :, None] * grad_out[:, None, :]).astype(jnp.bfloat16)

    def dispatch_rows(low, high):
        first = take_first[low:high]
        second = take_second[low:high]
        sent_rows = jnp.dot(first + second, moe_in, preferred_element_type=jnp.float32)
        sent_grad = jnp.dot(
            first, grad_picked[:, 0], preferred_element_type=jnp.float32
        ) + jnp.dot(second, grad_picked[:, 1], preferred_element_type=jnp.float32)
        return jnp.concatenate([sent_rows, sent_grad], axis=1).astype(jnp.bfloat16)

    grad_first = None
    grad_second = None
    returned_parts = []
    for start, size in zip(chunk_starts, chunk_sizes):
        arrived = lax.all_to_all(
            dispatch_rows(experts * start, experts * (start + size)).reshape(
                experts, size, 2 * width
            ),
            "expert",
            split_axis=0,
            concat_axis=0,
            tiled=True,
        ).reshape(experts * size, 2 * width)
        flat_arrived = arrived[:, :width]
        flat_grad = arrived[:, width:]
        hidden_grad = lax.dot_general(
            flat_grad, expert_second, COL_CONTRACT, preferred_element_type=jnp.float32
        )
        pre_act = jnp.dot(flat_arrived, expert_first, preferred_element_type=jnp.float32)
        activated, slope = gelu_parts(pre_act)
        activated = activated.astype(jnp.bfloat16)
        pre_grad = (hidden_grad * slope).astype(jnp.bfloat16)
        produced = jnp.dot(
            activated, expert_second, preferred_element_type=jnp.float32
        ).astype(jnp.bfloat16)
        row_grad = lax.dot_general(
            pre_grad, expert_first, COL_CONTRACT, preferred_element_type=jnp.float32
        ).astype(jnp.bfloat16)
        part_second = lax.dot_general(
            activated, flat_grad, ROW_CONTRACT, preferred_element_type=jnp.float32
        )
        part_first = lax.dot_general(
            flat_arrived, pre_grad, ROW_CONTRACT, preferred_element_type=jnp.float32
        )
        grad_first = part_first if grad_first is None else grad_first + part_first
        grad_second = part_second if grad_second is None else grad_second + part_second
        returning = jnp.concatenate([produced, row_grad], axis=1).reshape(
            experts, size, 2 * width
        )
        returned_parts.append(
            lax.all_to_all(returning, "expert", split_axis=0, concat_axis=0, tiled=True)
        )

    expert_grads = jnp.stack(
        [grad_first, grad_second.reshape(width, ff)], axis=0
    ).astype(jnp.bfloat16)
    expert_share = lax.psum_scatter(expert_grads, "shard", scatter_dimension=1, tiled=True)
    expert_share = expert_share.astype(jnp.float32)
    grad_in_share = expert_share[0][None]
    grad_back_share = expert_share[1].reshape(back_rows, width)[None]

    picked_first = None
    picked_second = None
    for start, size, part in zip(chunk_starts, chunk_sizes, returned_parts):
        low, high = experts * start, experts * (start + size)
        part = part.reshape(-1, 2 * width)
        part_first = lax.dot_general(
            take_first[low:high], part, ROW_CONTRACT, preferred_element_type=jnp.float32
        )
        part_second = lax.dot_general(
            take_second[low:high], part, ROW_CONTRACT, preferred_element_type=jnp.float32
        )
        picked_first = part_first if picked_first is None else picked_first + part_first
        picked_second = part_second if picked_second is None else picked_second + part_second
    moe_out = (
        weighted[:, 0:1] * picked_first[:, :width] + weighted[:, 1:2] * picked_second[:, :width]
    )
    output = (live_rows[:, None] * (hidden_state + moe_out)).astype(jnp.bfloat16)
    grad_chosen = jnp.stack(
        [
            jnp.sum(grad_out * picked_first[:, :width], axis=1),
            jnp.sum(grad_out * picked_second[:, :width], axis=1),
        ],
        axis=1,
    ) * live_rows[:, None]
    expert_part = (picked_first[:, width:] + picked_second[:, width:]) * live_rows[:, None]
    prob_sum = jnp.sum(choose * grad_chosen[:, :, None], axis=1)
    logit_grad = (
        router_probs * (prob_sum - jnp.sum(router_probs * prob_sum, axis=-1, keepdims=True))
    ).astype(jnp.bfloat16)
    grad_router = lax.dot_general(
        moe_in, logit_grad, ROW_CONTRACT, preferred_element_type=jnp.float32
    )
    moe_in_grad = expert_part + lax.dot_general(
        logit_grad, full_router, COL_CONTRACT, preferred_element_type=jnp.float32
    )
    _, norm_back = jax.vjp(layer_norm, hidden_state, gain_two)
    state_part, grad_gain_two = norm_back(moe_in_grad)
    state_grad = grad_out + state_part
    branch_grad = state_grad.astype(jnp.bfloat16)
    grad_wout = lax.dot_general(
        mixed_rows, branch_grad, ROW_CONTRACT, preferred_element_type=jnp.float32
    )
    mixed_grad = lax.dot_general(
        branch_grad, full_out, COL_CONTRACT, preferred_element_type=jnp.float32
    )
    mixed_grad = jnp.pad(mixed_grad.astype(jnp.bfloat16), ((0, pad_rows - rows), (0, 0)))
    grad_q, grad_k, grad_v = attention_bwd(projected_pad, mixed_grad, images)
    projected_grad = jnp.concatenate([grad_q, grad_k, grad_v], axis=1)
    attn_in_pad = jnp.pad(attn_in, ((0, pad_rows - rows), (0, 0)))
    grad_qkv = lax.dot_general(
        attn_in_pad, projected_grad, ROW_CONTRACT, preferred_element_type=jnp.float32
    )
    attn_in_grad = lax.dot_general(
        projected_grad[:rows], full_qkv, COL_CONTRACT, preferred_element_type=jnp.float32
    )
    _, first_back = jax.vjp(layer_norm, token_f, gain_one)
    token_part, grad_gain_one = first_back(attn_in_grad)
    grad_tokens = (state_grad + token_part).astype(jnp.bfloat16)

    small = jnp.concatenate(
        [grad_router, grad_gain_one[:, None], grad_gain_two[:, None]], axis=1
    )
    small = jnp.pad(small, ((0, 0), (0, 128 - small.shape[1])))
    dense_grads = jnp.concatenate([grad_qkv, grad_wout, small], axis=1)
    n_parts = 3
    bounds = [128 * (dense_grads.shape[1] * k // (128 * n_parts)) for k in range(n_parts)]
    bounds = bounds + [dense_grads.shape[1]]
    dense_total = jnp.concatenate(
        [
            expert_all_reduce(
                shard_reduce_scatter(part, "shard", 128 * (part.shape[1] // 256)), "expert"
            )
            for part in (dense_grads[:, low:high] for low, high in zip(bounds[:-1], bounds[1:]))
        ],
        axis=1,
    )
    return (
        output,
        grad_tokens,
        dense_total[:, :qkv_cols],
        dense_total[:, qkv_cols : qkv_cols + width],
        dense_total[:, qkv_cols + width : qkv_cols + width + n_route],
        dense_total[:, qkv_cols + width + n_route],
        dense_total[:, qkv_cols + width + n_route + 1],
        grad_in_share,
        grad_back_share,
    )


def solution(mesh):
    return _mapped(mesh)


def _mapped(mesh):
    return jax.shard_map(
        shards,
        mesh=mesh,
        in_specs=(
            P(("expert", "shard"), None),
            P("expert", "shard"),
            P(("expert", "shard"), None),
            P("shard", None),
            P("shard", None),
            P("shard", None),
            P("shard"),
            P("shard"),
            P("expert", "shard", None),
            P("expert", "shard", None),
            P(("expert", "shard"), None),
        ),
        out_specs=(
            P(("expert", "shard"), None),
            P(("expert", "shard"), None),
            P("shard", None),
            P("shard", None),
            P("shard", None),
            P("shard"),
            P("shard"),
            P("expert", "shard", None),
            P("expert", "shard", None),
        ),
        check_vma=False,
    )
```

```python
import functools

import jax
import numpy as np
import jax.numpy as jnp
from jax import lax
from jax.experimental import pallas as pl
from jax.experimental.pallas import tpu as pltpu
from jax.sharding import PartitionSpec as P

HD = 64
SEQ = 197


EPSILON = 1e-06
ROW_CONTRACT = (((0,), (0,)), ((), ()))
COL_CONTRACT = (((1,), (1,)), ((), ()))


def _image_of(idx, images):
    count = jnp.zeros(idx.shape, jnp.int32)
    for i in range(1, images + 1):
        count = count + (idx >= i * SEQ).astype(jnp.int32)
    return count


def _same_image(size, images):
    rows = lax.broadcasted_iota(jnp.int32, (size, size), 0)
    cols = lax.broadcasted_iota(jnp.int32, (size, size), 1)
    return _image_of(rows, images) == _image_of(cols, images)


def _softmax_masked(qj, k, same):
    s = lax.dot_general(qj, k, COL_CONTRACT, preferred_element_type=jnp.float32) * (HD ** -0.5)
    s = jnp.where(same, s, -jnp.inf)
    top = jnp.max(s, axis=1, keepdims=True)
    e = jnp.exp(s - top)
    return e / jnp.sum(e, axis=1, keepdims=True)


def attn_fwd_kernel(q_ref, k_ref, v_ref, o_ref, *, images):
    R = q_ref.shape[0]
    q = q_ref[...]
    k = k_ref[...]
    v = v_ref[...]
    same = _same_image(R, images)
    lane = lax.broadcasted_iota(jnp.int32, (1, 2 * HD), 1)
    out = jnp.zeros((R, 2 * HD), jnp.float32)
    for j in range(2):
        in_head = (lane >= HD) == (j == 1)
        p = _softmax_masked(jnp.where(in_head, q, jnp.zeros_like(q)), k, same)
        o = jnp.dot(p.astype(jnp.bfloat16), v, preferred_element_type=jnp.float32)
        out = jnp.where(in_head, o, out)
    o_ref[...] = out.astype(o_ref.dtype)


def attn_bwd_kernel(q_ref, k_ref, v_ref, g_ref, dq_ref, dk_ref, dv_ref, *, images):
    R = q_ref.shape[0]
    q = q_ref[...]
    k = k_ref[...]
    v = v_ref[...]
    g = g_ref[...]
    same = _same_image(R, images)
    lane = lax.broadcasted_iota(jnp.int32, (1, 2 * HD), 1)
    dq = jnp.zeros((R, 2 * HD), jnp.float32)
    dk = jnp.zeros((R, 2 * HD), jnp.float32)
    dv = jnp.zeros((R, 2 * HD), jnp.float32)
    for j in range(2):
        in_head = (lane >= HD) == (j == 1)
        p = _softmax_masked(jnp.where(in_head, q, jnp.zeros_like(q)), k, same)
        gj = jnp.where(in_head, g, jnp.zeros_like(g))
        dp = lax.dot_general(gj, v, COL_CONTRACT, preferred_element_type=jnp.float32)
        ds = (p * (dp - jnp.sum(p * dp, axis=1, keepdims=True))).astype(jnp.bfloat16)
        dq_j = jnp.dot(ds, k, preferred_element_type=jnp.float32) * (HD ** -0.5)
        dk_j = lax.dot_general(ds, q, ROW_CONTRACT, preferred_element_type=jnp.float32) * (HD ** -0.5)
        dv_j = lax.dot_general(p.astype(jnp.bfloat16), g, ROW_CONTRACT, preferred_element_type=jnp.float32)
        dq = jnp.where(in_head, dq_j, dq)
        dk = jnp.where(in_head, dk_j, dk)
        dv = jnp.where(in_head, dv_j, dv)
    dq_ref[...] = dq.astype(dq_ref.dtype)
    dk_ref[...] = dk.astype(dk_ref.dtype)
    dv_ref[...] = dv.astype(dv_ref.dtype)


def attention_fwd(projected, images):
    R = projected.shape[0]
    W = projected.shape[1] // 3
    pairs = W // (2 * HD)
    blk = lambda off: pl.BlockSpec((R, 2 * HD), lambda h: (0, off + h))
    return pl.pallas_call(
        functools.partial(attn_fwd_kernel, images=images),
        grid=(pairs,),
        in_specs=[blk(0), blk(pairs), blk(2 * pairs)],
        out_specs=blk(0),
        out_shape=jax.ShapeDtypeStruct((R, W), jnp.bfloat16),
        compiler_params=pltpu.CompilerParams(vmem_limit_bytes=48 * 1024 * 1024),
    )(projected, projected, projected)


def attention_bwd(projected, mixed_grad, images):
    R = projected.shape[0]
    W = projected.shape[1] // 3
    pairs = W // (2 * HD)
    blk = lambda off: pl.BlockSpec((R, 2 * HD), lambda h: (0, off + h))
    out = jax.ShapeDtypeStruct((R, W), jnp.bfloat16)
    return pl.pallas_call(
        functools.partial(attn_bwd_kernel, images=images),
        grid=(pairs,),
        in_specs=[blk(0), blk(pairs), blk(2 * pairs), blk(0)],
        out_specs=[blk(0), blk(0), blk(0)],
        out_shape=[out, out, out],
        compiler_params=pltpu.CompilerParams(vmem_limit_bytes=48 * 1024 * 1024),
    )(projected, projected, projected, mixed_grad)


def _exchange(values, bits_left, bit, axis_name, size, index):
    axis = bits_left.index(bit)
    mine = (index >> bit) & 1
    keep = lax.dynamic_index_in_dim(values, mine, axis, keepdims=False)
    send = lax.dynamic_index_in_dim(values, 1 - mine, axis, keepdims=False)
    pairs = [(i, i ^ (1 << bit)) for i in range(size)]
    got = lax.ppermute(send.astype(jnp.bfloat16), axis_name, pairs)
    return keep + got.astype(jnp.float32), [b for b in bits_left if b != bit]


def shard_reduce_scatter(values, axis_name, split_col):
    size = lax.axis_size(axis_name)
    index = lax.axis_index(axis_name)
    n_bits = size.bit_length() - 1
    block = values.shape[0] // size
    bits = list(range(n_bits - 1, -1, -1))
    values = values.astype(jnp.float32).reshape([2] * n_bits + [block, values.shape[1]])
    values, bits = _exchange(values, bits, 0, axis_name, size, index)
    first, second = values[..., :split_col], values[..., split_col:]
    first_bits, second_bits = list(bits), list(bits)
    for up, down in zip(range(1, n_bits), range(n_bits - 1, 0, -1)):
        first, first_bits = _exchange(first, first_bits, up, axis_name, size, index)
        second, second_bits = _exchange(second, second_bits, down, axis_name, size, index)
    return jnp.concatenate([first, second], axis=-1)


def _gather_back(values, bit, axis_name, size, index):
    n_bits = size.bit_length() - 1
    mine = (index >> bit) & 1
    pairs = [(i, i ^ (1 << bit)) for i in range(size)]
    got = lax.ppermute(values, axis_name, pairs)
    low = jnp.where(mine == 0, values, got)
    high = jnp.where(mine == 0, got, values)
    return jnp.stack([low, high], axis=n_bits - 1 - bit)


def expert_all_reduce(values, axis_name):
    size = lax.axis_size(axis_name)
    index = lax.axis_index(axis_name)
    n_bits = size.bit_length() - 1
    rows = values.shape[0]
    if rows % size:
        return lax.psum(values.astype(jnp.bfloat16), axis_name).astype(jnp.float32)
    bits = list(range(n_bits - 1, -1, -1))
    parts = values.astype(jnp.float32).reshape([2] * n_bits + [rows // size, values.shape[1]])
    for bit in range(n_bits):
        parts, bits = _exchange(parts, bits, bit, axis_name, size, index)
    parts = parts.astype(jnp.bfloat16)
    for bit in range(n_bits - 1, -1, -1):
        parts = _gather_back(parts, bit, axis_name, size, index)
    return parts.reshape(rows, values.shape[1]).astype(jnp.float32)


def layer_norm(values, norm_gain):
    row_mean = jnp.mean(values, axis=-1, keepdims=True)
    centered = values - row_mean
    variance = jnp.mean(centered * centered, axis=-1, keepdims=True)
    return centered * lax.rsqrt(variance + EPSILON) * norm_gain


def normalize_rows(scores):
    row_top = jnp.max(scores, axis=-1, keepdims=True)
    exp_scores = jnp.exp(scores - row_top)
    return exp_scores / jnp.sum(exp_scores, axis=-1, keepdims=True)


def gelu_parts(values):
    sqrt_half = np.float32(np.sqrt(0.5))
    tail = lax.erfc(-values * sqrt_half)
    density = jnp.exp(-0.5 * values * values) * np.float32(1.0 / np.sqrt(2.0 * np.pi))
    return 0.5 * values * tail, 0.5 * tail + values * density


def shards(
    tokens,
    image_counts,
    routes,
    w_qkv,
    w_out,
    w_router,
    gain_attn,
    gain_moe,
    w_in,
    w_back,
    cotangent,
):
    rows, width = tokens.shape
    experts = lax.axis_size("expert")
    capacity = 8 * (5 * rows // (16 * experts)) + 8
    overflow = experts * capacity
    images = rows // SEQ
    qkv_cols = w_qkv.shape[1]
    n_route = w_router.shape[1]
    ff = w_in.shape[2]
    row_ids = jnp.arange(rows, dtype=jnp.int32)
    live_int = (row_ids // SEQ < image_counts[0, 0]).astype(jnp.int32)
    live_rows = live_int.astype(jnp.float32)

    dense_local = jnp.concatenate(
        [w_qkv, w_out, w_router, gain_attn[:, None], gain_moe[:, None]], axis=1
    )
    dense_full = lax.all_gather(dense_local, "shard", axis=0, tiled=True)
    full_qkv = dense_full[:, :qkv_cols]
    full_out = dense_full[:, qkv_cols : qkv_cols + width]
    full_router = dense_full[:, qkv_cols + width : qkv_cols + width + n_route]
    gain_one = dense_full[:, -2].astype(jnp.float32)
    gain_two = dense_full[:, -1].astype(jnp.float32)

    back_rows = w_back.shape[1]
    expert_local = jnp.stack(
        [w_in[0], w_back[0].reshape(back_rows * width // ff, ff)], axis=0
    )
    expert_full = lax.all_gather(expert_local, "shard", axis=1, tiled=True)
    expert_first = expert_full[0]
    expert_second = expert_full[1].reshape(ff, width)

    token_f = tokens.astype(jnp.float32)
    attn_in = lax.optimization_barrier(layer_norm(token_f, gain_one).astype(jnp.bfloat16))
    projected = jnp.dot(attn_in, full_qkv, preferred_element_type=jnp.float32).astype(jnp.bfloat16)
    pad_rows = -(-rows // 128) * 128
    projected_pad = jnp.pad(projected, ((0, pad_rows - rows), (0, 0)))
    mixed_rows = attention_fwd(projected_pad, images)[:rows]
    hidden_state = token_f + jnp.dot(mixed_rows, full_out, preferred_element_type=jnp.float32)
    moe_in = layer_norm(hidden_state, gain_two).astype(jnp.bfloat16)
    logits = jnp.dot(moe_in, full_router, preferred_element_type=jnp.float32)
    router_probs = normalize_rows(logits)
    expert_ids = jnp.arange(experts, dtype=jnp.int32)
    choose = (routes[:, :, None] == expert_ids).astype(jnp.float32)
    chosen = jnp.sum(choose * router_probs[:, None, :], axis=2)
    pick_table = (routes[:, :, None] == expert_ids).astype(jnp.int32) * live_int[:, None, None]
    flat_picks = pick_table.reshape(rows * 2, experts)
    before = jnp.cumsum(flat_picks, axis=0) - flat_picks
    slot_index = jnp.sum(before * flat_picks, axis=1).reshape(rows, 2)
    position = jnp.where(live_int[:, None] > 0, routes * capacity + slot_index, overflow)

    n_chunks = 2
    part_cap = 8 * ((capacity + 8 * n_chunks - 1) // (8 * n_chunks))
    chunk_sizes = [min(part_cap, capacity - k * part_cap) for k in range(n_chunks)]
    chunk_sizes = [size for size in chunk_sizes if size > 0]
    chunk_starts = [sum(chunk_sizes[:k]) for k in range(len(chunk_sizes))]
    slot_ids = jnp.concatenate(
        [
            (
                jnp.arange(experts, dtype=jnp.int32)[:, None] * capacity
                + start
                + jnp.arange(size, dtype=jnp.int32)[None, :]
            ).reshape(-1)
            for start, size in zip(chunk_starts, chunk_sizes)
        ]
    )[:, None]
    take_first = (slot_ids == position[None, :, 0]).astype(jnp.bfloat16)
    take_second = (slot_ids == position[None, :, 1]).astype(jnp.bfloat16)

    grad_out = cotangent.astype(jnp.float32) * live_rows[:, None]
    weighted = chosen * live_rows[:, None]
    grad_picked = (weighted[:, :, None] * grad_out[:, None, :]).astype(jnp.bfloat16)

    def dispatch_rows(low, high):
        first = take_first[low:high]
        second = take_second[low:high]
        sent_rows = jnp.dot(first + second, moe_in, preferred_element_type=jnp.float32)
        sent_grad = jnp.dot(
            first, grad_picked[:, 0], preferred_element_type=jnp.float32
        ) + jnp.dot(second, grad_picked[:, 1], preferred_element_type=jnp.float32)
        return jnp.concatenate([sent_rows, sent_grad], axis=1).astype(jnp.bfloat16)

    grad_first = None
    grad_second = None
    returned_parts = []
    expert_index = lax.axis_index("expert")
    rotation = (expert_index + jnp.arange(experts, dtype=jnp.int32)) % experts
    restore = (jnp.arange(experts, dtype=jnp.int32) - expert_index) % experts

    def expert_block(rows_in):
        flat_arrived = rows_in[:, :width]
        flat_grad = rows_in[:, width:]
        hidden_grad = lax.dot_general(
            flat_grad, expert_second, COL_CONTRACT, preferred_element_type=jnp.float32
        )
        pre_act = jnp.dot(flat_arrived, expert_first, preferred_element_type=jnp.float32)
        activated, slope = gelu_parts(pre_act)
        activated = activated.astype(jnp.bfloat16)
        pre_grad = (hidden_grad * slope).astype(jnp.bfloat16)
        produced = jnp.dot(
            activated, expert_second, preferred_element_type=jnp.float32
        ).astype(jnp.bfloat16)
        row_grad = lax.dot_general(
            pre_grad, expert_first, COL_CONTRACT, preferred_element_type=jnp.float32
        ).astype(jnp.bfloat16)
        part_second = lax.dot_general(
            activated, flat_grad, ROW_CONTRACT, preferred_element_type=jnp.float32
        )
        part_first = lax.dot_general(
            flat_arrived, pre_grad, ROW_CONTRACT, preferred_element_type=jnp.float32
        )
        return jnp.concatenate([produced, row_grad], axis=1), part_first, part_second

    for start, size in zip(chunk_starts, chunk_sizes):
        sending = dispatch_rows(experts * start, experts * (start + size)).reshape(
            experts, size, 2 * width
        )
        own = lax.dynamic_index_in_dim(sending, expert_index, 0, keepdims=False)
        own_out, own_first, own_second = expert_block(own)
        arrived = lax.all_to_all(sending, "expert", split_axis=0, concat_axis=0, tiled=True)
        remote = jnp.take(arrived, rotation[1:], axis=0).reshape((experts - 1) * size, 2 * width)
        remote_out, remote_first, remote_second = expert_block(remote)
        part_first = own_first + remote_first
        part_second = own_second + remote_second
        grad_first = part_first if grad_first is None else grad_first + part_first
        grad_second = part_second if grad_second is None else grad_second + part_second
        rotated = jnp.concatenate(
            [own_out[None], remote_out.reshape(experts - 1, size, 2 * width)], axis=0
        )
        returning = jnp.take(rotated, restore, axis=0)
        returned_parts.append(
            lax.all_to_all(returning, "expert", split_axis=0, concat_axis=0, tiled=True)
        )

    expert_grads = jnp.stack(
        [grad_first, grad_second.reshape(width, ff)], axis=0
    ).astype(jnp.bfloat16)
    expert_share = lax.psum_scatter(expert_grads, "shard", scatter_dimension=1, tiled=True)
    expert_share = expert_share.astype(jnp.float32)
    grad_in_share = expert_share[0][None]
    grad_back_share = expert_share[1].reshape(back_rows, width)[None]

    picked_first = None
    picked_second = None
    for start, size, part in zip(chunk_starts, chunk_sizes, returned_parts):
        low, high = experts * start, experts * (start + size)
        part = part.reshape(-1, 2 * width)
        part_first = lax.dot_general(
            take_first[low:high], part, ROW_CONTRACT, preferred_element_type=jnp.float32
        )
        part_second = lax.dot_general(
            take_second[low:high], part, ROW_CONTRACT, preferred_element_type=jnp.float32
        )
        picked_first = part_first if picked_first is None else picked_first + part_first
        picked_second = part_second if picked_second is None else picked_second + part_second
    moe_out = (
        weighted[:, 0:1] * picked_first[:, :width] + weighted[:, 1:2] * picked_second[:, :width]
    )
    output = (live_rows[:, None] * (hidden_state + moe_out)).astype(jnp.bfloat16)
    grad_chosen = jnp.stack(
        [
            jnp.sum(grad_out * picked_first[:, :width], axis=1),
            jnp.sum(grad_out * picked_second[:, :width], axis=1),
        ],
        axis=1,
    ) * live_rows[:, None]
    expert_part = (picked_first[:, width:] + picked_second[:, width:]) * live_rows[:, None]
    prob_sum = jnp.sum(choose * grad_chosen[:, :, None], axis=1)
    logit_grad = (
        router_probs * (prob_sum - jnp.sum(router_probs * prob_sum, axis=-1, keepdims=True))
    ).astype(jnp.bfloat16)
    grad_router = lax.dot_general(
        moe_in, logit_grad, ROW_CONTRACT, preferred_element_type=jnp.float32
    )
    moe_in_grad = expert_part + lax.dot_general(
        logit_grad, full_router, COL_CONTRACT, preferred_element_type=jnp.float32
    )
    _, norm_back = jax.vjp(layer_norm, hidden_state, gain_two)
    state_part, grad_gain_two = norm_back(moe_in_grad)
    state_grad = grad_out + state_part
    branch_grad = state_grad.astype(jnp.bfloat16)
    grad_wout = lax.dot_general(
        mixed_rows, branch_grad, ROW_CONTRACT, preferred_element_type=jnp.float32
    )
    mixed_grad = lax.dot_general(
        branch_grad, full_out, COL_CONTRACT, preferred_element_type=jnp.float32
    )
    mixed_grad = jnp.pad(mixed_grad.astype(jnp.bfloat16), ((0, pad_rows - rows), (0, 0)))
    grad_q, grad_k, grad_v = attention_bwd(projected_pad, mixed_grad, images)
    projected_grad = jnp.concatenate([grad_q, grad_k, grad_v], axis=1)
    attn_in_pad = jnp.pad(attn_in, ((0, pad_rows - rows), (0, 0)))
    grad_qkv = lax.dot_general(
        attn_in_pad, projected_grad, ROW_CONTRACT, preferred_element_type=jnp.float32
    )
    attn_in_grad = lax.dot_general(
        projected_grad[:rows], full_qkv, COL_CONTRACT, preferred_element_type=jnp.float32
    )
    _, first_back = jax.vjp(layer_norm, token_f, gain_one)
    token_part, grad_gain_one = first_back(attn_in_grad)
    grad_tokens = (state_grad + token_part).astype(jnp.bfloat16)

    small = jnp.concatenate(
        [grad_router, grad_gain_one[:, None], grad_gain_two[:, None]], axis=1
    )
    small = jnp.pad(small, ((0, 0), (0, 128 - small.shape[1])))
    dense_grads = jnp.concatenate([grad_qkv, grad_wout, small], axis=1)
    n_parts = 3
    bounds = [128 * (dense_grads.shape[1] * k // (128 * n_parts)) for k in range(n_parts)]
    bounds = bounds + [dense_grads.shape[1]]
    dense_total = jnp.concatenate(
        [
            expert_all_reduce(
                shard_reduce_scatter(part, "shard", 128 * (part.shape[1] // 256)), "expert"
            )
            for part in (dense_grads[:, low:high] for low, high in zip(bounds[:-1], bounds[1:]))
        ],
        axis=1,
    )
    return (
        output,
        grad_tokens,
        dense_total[:, :qkv_cols],
        dense_total[:, qkv_cols : qkv_cols + width],
        dense_total[:, qkv_cols + width : qkv_cols + width + n_route],
        dense_total[:, qkv_cols + width + n_route],
        dense_total[:, qkv_cols + width + n_route + 1],
        grad_in_share,
        grad_back_share,
    )


def solution(mesh):
    return _mapped(mesh)


def _mapped(mesh):
    return jax.shard_map(
        shards,
        mesh=mesh,
        in_specs=(
            P(("expert", "shard"), None),
            P("expert", "shard"),
            P(("expert", "shard"), None),
            P("shard", None),
            P("shard", None),
            P("shard", None),
            P("shard"),
            P("shard"),
            P("expert", "shard", None),
            P("expert", "shard", None),
            P(("expert", "shard"), None),
        ),
        out_specs=(
            P(("expert", "shard"), None),
            P(("expert", "shard"), None),
            P("shard", None),
            P("shard", None),
            P("shard", None),
            P("shard"),
            P("shard"),
            P("expert", "shard", None),
            P("expert", "shard", None),
        ),
        check_vma=False,
    )
```

```python
import functools

import jax
import numpy as np
import jax.numpy as jnp
from jax import lax
from jax.experimental import pallas as pl
from jax.experimental.pallas import tpu as pltpu
from jax.sharding import PartitionSpec as P

HD = 64
SEQ = 197


EPSILON = 1e-06
ROW_CONTRACT = (((0,), (0,)), ((), ()))
COL_CONTRACT = (((1,), (1,)), ((), ()))


def _image_of(idx, images):
    count = jnp.zeros(idx.shape, jnp.int32)
    for i in range(1, images + 1):
        count = count + (idx >= i * SEQ).astype(jnp.int32)
    return count


def _same_image(size, images):
    rows = lax.broadcasted_iota(jnp.int32, (size, size), 0)
    cols = lax.broadcasted_iota(jnp.int32, (size, size), 1)
    return _image_of(rows, images) == _image_of(cols, images)


def _softmax_masked(qj, k, same):
    s = lax.dot_general(qj, k, COL_CONTRACT, preferred_element_type=jnp.float32) * (HD ** -0.5)
    s = jnp.where(same, s, -jnp.inf)
    top = jnp.max(s, axis=1, keepdims=True)
    e = jnp.exp(s - top)
    return e / jnp.sum(e, axis=1, keepdims=True)


def attn_fwd_kernel(q_ref, k_ref, v_ref, o_ref, *, images):
    R = q_ref.shape[0]
    q = q_ref[...]
    k = k_ref[...]
    v = v_ref[...]
    same = _same_image(R, images)
    lane = lax.broadcasted_iota(jnp.int32, (1, 2 * HD), 1)
    out = jnp.zeros((R, 2 * HD), jnp.float32)
    for j in range(2):
        in_head = (lane >= HD) == (j == 1)
        p = _softmax_masked(jnp.where(in_head, q, jnp.zeros_like(q)), k, same)
        o = jnp.dot(p.astype(jnp.bfloat16), v, preferred_element_type=jnp.float32)
        out = jnp.where(in_head, o, out)
    o_ref[...] = out.astype(o_ref.dtype)


def attn_bwd_kernel(q_ref, k_ref, v_ref, g_ref, dq_ref, dk_ref, dv_ref, *, images):
    R = q_ref.shape[0]
    q = q_ref[...]
    k = k_ref[...]
    v = v_ref[...]
    g = g_ref[...]
    same = _same_image(R, images)
    lane = lax.broadcasted_iota(jnp.int32, (1, 2 * HD), 1)
    dq = jnp.zeros((R, 2 * HD), jnp.float32)
    dk = jnp.zeros((R, 2 * HD), jnp.float32)
    dv = jnp.zeros((R, 2 * HD), jnp.float32)
    for j in range(2):
        in_head = (lane >= HD) == (j == 1)
        p = _softmax_masked(jnp.where(in_head, q, jnp.zeros_like(q)), k, same)
        gj = jnp.where(in_head, g, jnp.zeros_like(g))
        dp = lax.dot_general(gj, v, COL_CONTRACT, preferred_element_type=jnp.float32)
        ds = (p * (dp - jnp.sum(p * dp, axis=1, keepdims=True))).astype(jnp.bfloat16)
        dq_j = jnp.dot(ds, k, preferred_element_type=jnp.float32) * (HD ** -0.5)
        dk_j = lax.dot_general(ds, q, ROW_CONTRACT, preferred_element_type=jnp.float32) * (HD ** -0.5)
        dv_j = lax.dot_general(p.astype(jnp.bfloat16), g, ROW_CONTRACT, preferred_element_type=jnp.float32)
        dq = jnp.where(in_head, dq_j, dq)
        dk = jnp.where(in_head, dk_j, dk)
        dv = jnp.where(in_head, dv_j, dv)
    dq_ref[...] = dq.astype(dq_ref.dtype)
    dk_ref[...] = dk.astype(dk_ref.dtype)
    dv_ref[...] = dv.astype(dv_ref.dtype)


def attention_fwd(projected, images):
    R = projected.shape[0]
    W = projected.shape[1] // 3
    pairs = W // (2 * HD)
    blk = lambda off: pl.BlockSpec((R, 2 * HD), lambda h: (0, off + h))
    return pl.pallas_call(
        functools.partial(attn_fwd_kernel, images=images),
        grid=(pairs,),
        in_specs=[blk(0), blk(pairs), blk(2 * pairs)],
        out_specs=blk(0),
        out_shape=jax.ShapeDtypeStruct((R, W), jnp.bfloat16),
        compiler_params=pltpu.CompilerParams(vmem_limit_bytes=48 * 1024 * 1024),
    )(projected, projected, projected)


def attention_bwd(projected, mixed_grad, images):
    R = projected.shape[0]
    W = projected.shape[1] // 3
    pairs = W // (2 * HD)
    blk = lambda off: pl.BlockSpec((R, 2 * HD), lambda h: (0, off + h))
    out = jax.ShapeDtypeStruct((R, W), jnp.bfloat16)
    return pl.pallas_call(
        functools.partial(attn_bwd_kernel, images=images),
        grid=(pairs,),
        in_specs=[blk(0), blk(pairs), blk(2 * pairs), blk(0)],
        out_specs=[blk(0), blk(0), blk(0)],
        out_shape=[out, out, out],
        compiler_params=pltpu.CompilerParams(vmem_limit_bytes=48 * 1024 * 1024),
    )(projected, projected, projected, mixed_grad)


def _exchange(values, bits_left, bit, axis_name, size, index):
    axis = bits_left.index(bit)
    mine = (index >> bit) & 1
    keep = lax.dynamic_index_in_dim(values, mine, axis, keepdims=False)
    send = lax.dynamic_index_in_dim(values, 1 - mine, axis, keepdims=False)
    pairs = [(i, i ^ (1 << bit)) for i in range(size)]
    got = lax.ppermute(send.astype(jnp.bfloat16), axis_name, pairs)
    return keep + got.astype(jnp.float32), [b for b in bits_left if b != bit]


def shard_reduce_scatter(values, axis_name, split_col):
    del split_col
    size = lax.axis_size(axis_name)
    index = lax.axis_index(axis_name)
    n_bits = size.bit_length() - 1
    block = values.shape[0] // size
    bits = list(range(n_bits - 1, -1, -1))
    values = values.astype(jnp.float32).reshape([2] * n_bits + [block, values.shape[1]])
    values, bits = _exchange(values, bits, 0, axis_name, size, index)
    if n_bits == 1:
        return values
    rest = list(range(1, n_bits))
    half = (len(rest) + 1) // 2
    orders = (rest, rest[half:] + rest[:half])
    core = index & 1
    lead = n_bits - 1
    layouts = [[lead - b for b in reversed(order)] for order in orders]
    tail = list(range(lead, values.ndim))
    values = jnp.where(
        core == 0,
        jnp.transpose(values, layouts[0] + tail),
        jnp.transpose(values, layouts[1] + tail),
    )
    for step in range(len(rest)):
        axis = values.ndim - 3
        bit_0, bit_1 = orders[0][step], orders[1][step]
        mine = jnp.where(core == 0, (index >> bit_0) & 1, (index >> bit_1) & 1)
        keep = lax.dynamic_index_in_dim(values, mine, axis, keepdims=False)
        send = lax.dynamic_index_in_dim(values, 1 - mine, axis, keepdims=False)
        pairs = [(i, i ^ (1 << (bit_0 if i % 2 == 0 else bit_1))) for i in range(size)]
        got = lax.ppermute(send.astype(jnp.bfloat16), axis_name, pairs)
        values = keep + got.astype(jnp.float32)
    return values


def _gather_back(values, bit, axis_name, size, index):
    n_bits = size.bit_length() - 1
    mine = (index >> bit) & 1
    pairs = [(i, i ^ (1 << bit)) for i in range(size)]
    got = lax.ppermute(values, axis_name, pairs)
    low = jnp.where(mine == 0, values, got)
    high = jnp.where(mine == 0, got, values)
    return jnp.stack([low, high], axis=n_bits - 1 - bit)


def expert_all_reduce(values, axis_name):
    size = lax.axis_size(axis_name)
    index = lax.axis_index(axis_name)
    n_bits = size.bit_length() - 1
    rows = values.shape[0]
    if rows % size:
        return lax.psum(values.astype(jnp.bfloat16), axis_name).astype(jnp.float32)
    bits = list(range(n_bits - 1, -1, -1))
    parts = values.astype(jnp.float32).reshape([2] * n_bits + [rows // size, values.shape[1]])
    for bit in range(n_bits):
        parts, bits = _exchange(parts, bits, bit, axis_name, size, index)
    parts = parts.astype(jnp.bfloat16)
    for bit in range(n_bits - 1, -1, -1):
        parts = _gather_back(parts, bit, axis_name, size, index)
    return parts.reshape(rows, values.shape[1]).astype(jnp.float32)


def layer_norm(values, norm_gain):
    row_mean = jnp.mean(values, axis=-1, keepdims=True)
    centered = values - row_mean
    variance = jnp.mean(centered * centered, axis=-1, keepdims=True)
    return centered * lax.rsqrt(variance + EPSILON) * norm_gain


def normalize_rows(scores):
    row_top = jnp.max(scores, axis=-1, keepdims=True)
    exp_scores = jnp.exp(scores - row_top)
    return exp_scores / jnp.sum(exp_scores, axis=-1, keepdims=True)


def gelu_parts(values):
    sqrt_half = np.float32(np.sqrt(0.5))
    tail = lax.erfc(-values * sqrt_half)
    density = jnp.exp(-0.5 * values * values) * np.float32(1.0 / np.sqrt(2.0 * np.pi))
    return 0.5 * values * tail, 0.5 * tail + values * density


def shards(
    tokens,
    image_counts,
    routes,
    w_qkv,
    w_out,
    w_router,
    gain_attn,
    gain_moe,
    w_in,
    w_back,
    cotangent,
):
    rows, width = tokens.shape
    experts = lax.axis_size("expert")
    capacity = 8 * (5 * rows // (16 * experts)) + 8
    overflow = experts * capacity
    images = rows // SEQ
    qkv_cols = w_qkv.shape[1]
    n_route = w_router.shape[1]
    ff = w_in.shape[2]
    row_ids = jnp.arange(rows, dtype=jnp.int32)
    live_int = (row_ids // SEQ < image_counts[0, 0]).astype(jnp.int32)
    live_rows = live_int.astype(jnp.float32)

    dense_local = jnp.concatenate(
        [w_qkv, w_out, w_router, gain_attn[:, None], gain_moe[:, None]], axis=1
    )
    dense_full = lax.all_gather(dense_local, "shard", axis=0, tiled=True)
    full_qkv = dense_full[:, :qkv_cols]
    full_out = dense_full[:, qkv_cols : qkv_cols + width]
    full_router = dense_full[:, qkv_cols + width : qkv_cols + width + n_route]
    gain_one = dense_full[:, -2].astype(jnp.float32)
    gain_two = dense_full[:, -1].astype(jnp.float32)

    back_rows = w_back.shape[1]
    expert_local = jnp.stack(
        [w_in[0], w_back[0].reshape(back_rows * width // ff, ff)], axis=0
    )
    expert_full = lax.all_gather(expert_local, "shard", axis=1, tiled=True)
    expert_first = expert_full[0]
    expert_second = expert_full[1].reshape(ff, width)

    token_f = tokens.astype(jnp.float32)
    attn_in = lax.optimization_barrier(layer_norm(token_f, gain_one).astype(jnp.bfloat16))
    projected = jnp.dot(attn_in, full_qkv, preferred_element_type=jnp.float32).astype(jnp.bfloat16)
    pad_rows = -(-rows // 128) * 128
    projected_pad = jnp.pad(projected, ((0, pad_rows - rows), (0, 0)))
    mixed_rows = attention_fwd(projected_pad, images)[:rows]
    hidden_state = token_f + jnp.dot(mixed_rows, full_out, preferred_element_type=jnp.float32)
    moe_in = layer_norm(hidden_state, gain_two).astype(jnp.bfloat16)
    logits = jnp.dot(moe_in, full_router, preferred_element_type=jnp.float32)
    router_probs = normalize_rows(logits)
    expert_ids = jnp.arange(experts, dtype=jnp.int32)
    choose = (routes[:, :, None] == expert_ids).astype(jnp.float32)
    chosen = jnp.sum(choose * router_probs[:, None, :], axis=2)
    pick_table = (routes[:, :, None] == expert_ids).astype(jnp.int32) * live_int[:, None, None]
    flat_picks = pick_table.reshape(rows * 2, experts)
    before = jnp.cumsum(flat_picks, axis=0) - flat_picks
    slot_index = jnp.sum(before * flat_picks, axis=1).reshape(rows, 2)
    position = jnp.where(live_int[:, None] > 0, routes * capacity + slot_index, overflow)

    n_chunks = 2
    part_cap = 8 * ((capacity + 8 * n_chunks - 1) // (8 * n_chunks))
    chunk_sizes = [min(part_cap, capacity - k * part_cap) for k in range(n_chunks)]
    chunk_sizes = [size for size in chunk_sizes if size > 0]
    chunk_starts = [sum(chunk_sizes[:k]) for k in range(len(chunk_sizes))]
    slot_ids = jnp.concatenate(
        [
            (
                jnp.arange(experts, dtype=jnp.int32)[:, None] * capacity
                + start
                + jnp.arange(size, dtype=jnp.int32)[None, :]
            ).reshape(-1)
            for start, size in zip(chunk_starts, chunk_sizes)
        ]
    )[:, None]
    take_first = (slot_ids == position[None, :, 0]).astype(jnp.bfloat16)
    take_second = (slot_ids == position[None, :, 1]).astype(jnp.bfloat16)

    grad_out = cotangent.astype(jnp.float32) * live_rows[:, None]
    weighted = chosen * live_rows[:, None]
    grad_picked = (weighted[:, :, None] * grad_out[:, None, :]).astype(jnp.bfloat16)

    def dispatch_rows(low, high):
        first = take_first[low:high]
        second = take_second[low:high]
        sent_rows = jnp.dot(first + second, moe_in, preferred_element_type=jnp.float32)
        sent_grad = jnp.dot(
            first, grad_picked[:, 0], preferred_element_type=jnp.float32
        ) + jnp.dot(second, grad_picked[:, 1], preferred_element_type=jnp.float32)
        return jnp.concatenate([sent_rows, sent_grad], axis=1).astype(jnp.bfloat16)

    grad_first = None
    grad_second = None
    returned_parts = []
    for start, size in zip(chunk_starts, chunk_sizes):
        arrived = lax.all_to_all(
            dispatch_rows(experts * start, experts * (start + size)).reshape(
                experts, size, 2 * width
            ),
            "expert",
            split_axis=0,
            concat_axis=0,
            tiled=True,
        ).reshape(experts * size, 2 * width)
        flat_arrived = arrived[:, :width]
        flat_grad = arrived[:, width:]
        hidden_grad = lax.dot_general(
            flat_grad, expert_second, COL_CONTRACT, preferred_element_type=jnp.float32
        )
        pre_act = jnp.dot(flat_arrived, expert_first, preferred_element_type=jnp.float32)
        activated, slope = gelu_parts(pre_act)
        activated = activated.astype(jnp.bfloat16)
        pre_grad = (hidden_grad * slope).astype(jnp.bfloat16)
        produced = jnp.dot(
            activated, expert_second, preferred_element_type=jnp.float32
        ).astype(jnp.bfloat16)
        row_grad = lax.dot_general(
            pre_grad, expert_first, COL_CONTRACT, preferred_element_type=jnp.float32
        ).astype(jnp.bfloat16)
        part_second = lax.dot_general(
            activated, flat_grad, ROW_CONTRACT, preferred_element_type=jnp.float32
        )
        part_first = lax.dot_general(
            flat_arrived, pre_grad, ROW_CONTRACT, preferred_element_type=jnp.float32
        )
        grad_first = part_first if grad_first is None else grad_first + part_first
        grad_second = part_second if grad_second is None else grad_second + part_second
        returning = jnp.concatenate([produced, row_grad], axis=1).reshape(
            experts, size, 2 * width
        )
        returned_parts.append(
            lax.all_to_all(returning, "expert", split_axis=0, concat_axis=0, tiled=True)
        )

    expert_grads = jnp.stack(
        [grad_first, grad_second.reshape(width, ff)], axis=0
    ).astype(jnp.bfloat16)
    expert_share = lax.psum_scatter(expert_grads, "shard", scatter_dimension=1, tiled=True)
    expert_share = expert_share.astype(jnp.float32)
    grad_in_share = expert_share[0][None]
    grad_back_share = expert_share[1].reshape(back_rows, width)[None]

    picked_first = None
    picked_second = None
    for start, size, part in zip(chunk_starts, chunk_sizes, returned_parts):
        low, high = experts * start, experts * (start + size)
        part = part.reshape(-1, 2 * width)
        part_first = lax.dot_general(
            take_first[low:high], part, ROW_CONTRACT, preferred_element_type=jnp.float32
        )
        part_second = lax.dot_general(
            take_second[low:high], part, ROW_CONTRACT, preferred_element_type=jnp.float32
        )
        picked_first = part_first if picked_first is None else picked_first + part_first
        picked_second = part_second if picked_second is None else picked_second + part_second
    moe_out = (
        weighted[:, 0:1] * picked_first[:, :width] + weighted[:, 1:2] * picked_second[:, :width]
    )
    output = (live_rows[:, None] * (hidden_state + moe_out)).astype(jnp.bfloat16)
    grad_chosen = jnp.stack(
        [
            jnp.sum(grad_out * picked_first[:, :width], axis=1),
            jnp.sum(grad_out * picked_second[:, :width], axis=1),
        ],
        axis=1,
    ) * live_rows[:, None]
    expert_part = (picked_first[:, width:] + picked_second[:, width:]) * live_rows[:, None]
    prob_sum = jnp.sum(choose * grad_chosen[:, :, None], axis=1)
    logit_grad = (
        router_probs * (prob_sum - jnp.sum(router_probs * prob_sum, axis=-1, keepdims=True))
    ).astype(jnp.bfloat16)
    grad_router = lax.dot_general(
        moe_in, logit_grad, ROW_CONTRACT, preferred_element_type=jnp.float32
    )
    moe_in_grad = expert_part + lax.dot_general(
        logit_grad, full_router, COL_CONTRACT, preferred_element_type=jnp.float32
    )
    _, norm_back = jax.vjp(layer_norm, hidden_state, gain_two)
    state_part, grad_gain_two = norm_back(moe_in_grad)
    state_grad = grad_out + state_part
    branch_grad = state_grad.astype(jnp.bfloat16)
    grad_wout = lax.dot_general(
        mixed_rows, branch_grad, ROW_CONTRACT, preferred_element_type=jnp.float32
    )
    mixed_grad = lax.dot_general(
        branch_grad, full_out, COL_CONTRACT, preferred_element_type=jnp.float32
    )
    mixed_grad = jnp.pad(mixed_grad.astype(jnp.bfloat16), ((0, pad_rows - rows), (0, 0)))
    grad_q, grad_k, grad_v = attention_bwd(projected_pad, mixed_grad, images)
    projected_grad = jnp.concatenate([grad_q, grad_k, grad_v], axis=1)
    attn_in_pad = jnp.pad(attn_in, ((0, pad_rows - rows), (0, 0)))
    grad_qkv = lax.dot_general(
        attn_in_pad, projected_grad, ROW_CONTRACT, preferred_element_type=jnp.float32
    )
    attn_in_grad = lax.dot_general(
        projected_grad[:rows], full_qkv, COL_CONTRACT, preferred_element_type=jnp.float32
    )
    _, first_back = jax.vjp(layer_norm, token_f, gain_one)
    token_part, grad_gain_one = first_back(attn_in_grad)
    grad_tokens = (state_grad + token_part).astype(jnp.bfloat16)

    small = jnp.concatenate(
        [grad_router, grad_gain_one[:, None], grad_gain_two[:, None]], axis=1
    )
    small = jnp.pad(small, ((0, 0), (0, 128 - small.shape[1])))
    dense_grads = jnp.concatenate([grad_qkv, grad_wout, small], axis=1)
    n_parts = 3
    bounds = [128 * (dense_grads.shape[1] * k // (128 * n_parts)) for k in range(n_parts)]
    bounds = bounds + [dense_grads.shape[1]]
    dense_total = jnp.concatenate(
        [
            expert_all_reduce(
                shard_reduce_scatter(part, "shard", 128 * (part.shape[1] // 256)), "expert"
            )
            for part in (dense_grads[:, low:high] for low, high in zip(bounds[:-1], bounds[1:]))
        ],
        axis=1,
    )
    return (
        output,
        grad_tokens,
        dense_total[:, :qkv_cols],
        dense_total[:, qkv_cols : qkv_cols + width],
        dense_total[:, qkv_cols + width : qkv_cols + width + n_route],
        dense_total[:, qkv_cols + width + n_route],
        dense_total[:, qkv_cols + width + n_route + 1],
        grad_in_share,
        grad_back_share,
    )


def solution(mesh):
    return _mapped(mesh)


def _mapped(mesh):
    return jax.shard_map(
        shards,
        mesh=mesh,
        in_specs=(
            P(("expert", "shard"), None),
            P("expert", "shard"),
            P(("expert", "shard"), None),
            P("shard", None),
            P("shard", None),
            P("shard", None),
            P("shard"),
            P("shard"),
            P("expert", "shard", None),
            P("expert", "shard", None),
            P(("expert", "shard"), None),
        ),
        out_specs=(
            P(("expert", "shard"), None),
            P(("expert", "shard"), None),
            P("shard", None),
            P("shard", None),
            P("shard", None),
            P("shard"),
            P("shard"),
            P("expert", "shard", None),
            P("expert", "shard", None),
        ),
        check_vma=False,
    )
```

```python
import functools

import jax
import numpy as np
import jax.numpy as jnp
from jax import lax
from jax.experimental import pallas as pl
from jax.experimental.pallas import tpu as pltpu
from jax.sharding import PartitionSpec as P

HD = 64
SEQ = 197


EPSILON = 1e-06
ROW_CONTRACT = (((0,), (0,)), ((), ()))
COL_CONTRACT = (((1,), (1,)), ((), ()))


def _softmax_masked(qj, k, valid):
    s = lax.dot_general(qj, k, COL_CONTRACT, preferred_element_type=jnp.float32) * (HD ** -0.5)
    s = jnp.where(valid, s, -jnp.inf)
    top = jnp.max(s, axis=1, keepdims=True)
    e = jnp.exp(s - top)
    return e / jnp.sum(e, axis=1, keepdims=True)


def attn_fwd_kernel(q_ref, k_ref, v_ref, o_ref, *, images, slot):
    valid = lax.broadcasted_iota(jnp.int32, (slot, slot), 1) < SEQ
    lane = lax.broadcasted_iota(jnp.int32, (1, 2 * HD), 1)
    for i in range(images):
        rows = pl.ds(i * slot, slot)
        q = q_ref[rows, :]
        k = k_ref[rows, :]
        v = v_ref[rows, :]
        out = jnp.zeros((slot, 2 * HD), jnp.float32)
        for j in range(2):
            in_head = (lane >= HD) == (j == 1)
            p = _softmax_masked(jnp.where(in_head, q, jnp.zeros_like(q)), k, valid)
            o = jnp.dot(p.astype(jnp.bfloat16), v, preferred_element_type=jnp.float32)
            out = jnp.where(in_head, o, out)
        o_ref[rows, :] = out.astype(o_ref.dtype)


def attn_bwd_kernel(q_ref, k_ref, v_ref, g_ref, dq_ref, dk_ref, dv_ref, *, images, slot):
    valid = lax.broadcasted_iota(jnp.int32, (slot, slot), 1) < SEQ
    lane = lax.broadcasted_iota(jnp.int32, (1, 2 * HD), 1)
    for i in range(images):
        rows = pl.ds(i * slot, slot)
        q = q_ref[rows, :]
        k = k_ref[rows, :]
        v = v_ref[rows, :]
        g = g_ref[rows, :]
        dq = jnp.zeros((slot, 2 * HD), jnp.float32)
        dk = jnp.zeros((slot, 2 * HD), jnp.float32)
        dv = jnp.zeros((slot, 2 * HD), jnp.float32)
        for j in range(2):
            in_head = (lane >= HD) == (j == 1)
            p = _softmax_masked(jnp.where(in_head, q, jnp.zeros_like(q)), k, valid)
            gj = jnp.where(in_head, g, jnp.zeros_like(g))
            dp = lax.dot_general(gj, v, COL_CONTRACT, preferred_element_type=jnp.float32)
            ds = (p * (dp - jnp.sum(p * dp, axis=1, keepdims=True))).astype(jnp.bfloat16)
            dq_j = jnp.dot(ds, k, preferred_element_type=jnp.float32) * (HD ** -0.5)
            dk_j = lax.dot_general(ds, q, ROW_CONTRACT, preferred_element_type=jnp.float32) * (HD ** -0.5)
            dv_j = lax.dot_general(
                p.astype(jnp.bfloat16), g, ROW_CONTRACT, preferred_element_type=jnp.float32
            )
            dq = jnp.where(in_head, dq_j, dq)
            dk = jnp.where(in_head, dk_j, dk)
            dv = jnp.where(in_head, dv_j, dv)
        dq_ref[rows, :] = dq.astype(dq_ref.dtype)
        dk_ref[rows, :] = dk.astype(dk_ref.dtype)
        dv_ref[rows, :] = dv.astype(dv_ref.dtype)


def attention_fwd(projected, images, slot):
    R = projected.shape[0]
    W = projected.shape[1] // 3
    pairs = W // (2 * HD)
    blk = lambda off: pl.BlockSpec((R, 2 * HD), lambda h: (0, off + h))
    return pl.pallas_call(
        functools.partial(attn_fwd_kernel, images=images, slot=slot),
        grid=(pairs,),
        in_specs=[blk(0), blk(pairs), blk(2 * pairs)],
        out_specs=blk(0),
        out_shape=jax.ShapeDtypeStruct((R, W), jnp.bfloat16),
        compiler_params=pltpu.CompilerParams(vmem_limit_bytes=48 * 1024 * 1024),
    )(projected, projected, projected)


def attention_bwd(projected, mixed_grad, images, slot):
    R = projected.shape[0]
    W = projected.shape[1] // 3
    pairs = W // (2 * HD)
    blk = lambda off: pl.BlockSpec((R, 2 * HD), lambda h: (0, off + h))
    out = jax.ShapeDtypeStruct((R, W), jnp.bfloat16)
    return pl.pallas_call(
        functools.partial(attn_bwd_kernel, images=images, slot=slot),
        grid=(pairs,),
        in_specs=[blk(0), blk(pairs), blk(2 * pairs), blk(0)],
        out_specs=[blk(0), blk(0), blk(0)],
        out_shape=[out, out, out],
        compiler_params=pltpu.CompilerParams(vmem_limit_bytes=48 * 1024 * 1024),
    )(projected, projected, projected, mixed_grad)


def to_slots(values, images, slot):
    cols = values.shape[1]
    spaced = jnp.pad(values.reshape(images, SEQ, cols), ((0, 0), (0, slot - SEQ), (0, 0)))
    return spaced.reshape(images * slot, cols)


def from_slots(values, images, slot):
    cols = values.shape[1]
    return values.reshape(images, slot, cols)[:, :SEQ].reshape(images * SEQ, cols)


def _exchange(values, bits_left, bit, axis_name, size, index):
    axis = bits_left.index(bit)
    mine = (index >> bit) & 1
    keep = lax.dynamic_index_in_dim(values, mine, axis, keepdims=False)
    send = lax.dynamic_index_in_dim(values, 1 - mine, axis, keepdims=False)
    pairs = [(i, i ^ (1 << bit)) for i in range(size)]
    got = lax.ppermute(send.astype(jnp.bfloat16), axis_name, pairs)
    return keep + got.astype(jnp.float32), [b for b in bits_left if b != bit]


def shard_reduce_scatter(values, axis_name, split_col):
    size = lax.axis_size(axis_name)
    index = lax.axis_index(axis_name)
    n_bits = size.bit_length() - 1
    block = values.shape[0] // size
    bits = list(range(n_bits - 1, -1, -1))
    values = values.astype(jnp.float32).reshape([2] * n_bits + [block, values.shape[1]])
    values, bits = _exchange(values, bits, 0, axis_name, size, index)
    first, second = values[..., :split_col], values[..., split_col:]
    first_bits, second_bits = list(bits), list(bits)
    for up, down in zip(range(1, n_bits), range(n_bits - 1, 0, -1)):
        first, first_bits = _exchange(first, first_bits, up, axis_name, size, index)
        second, second_bits = _exchange(second, second_bits, down, axis_name, size, index)
    return jnp.concatenate([first, second], axis=-1)


def _gather_back(values, bit, axis_name, size, index):
    n_bits = size.bit_length() - 1
    mine = (index >> bit) & 1
    pairs = [(i, i ^ (1 << bit)) for i in range(size)]
    got = lax.ppermute(values, axis_name, pairs)
    low = jnp.where(mine == 0, values, got)
    high = jnp.where(mine == 0, got, values)
    return jnp.stack([low, high], axis=n_bits - 1 - bit)


def expert_all_reduce(values, axis_name):
    size = lax.axis_size(axis_name)
    index = lax.axis_index(axis_name)
    n_bits = size.bit_length() - 1
    rows = values.shape[0]
    if rows % size:
        return lax.psum(values.astype(jnp.bfloat16), axis_name).astype(jnp.float32)
    bits = list(range(n_bits - 1, -1, -1))
    parts = values.astype(jnp.float32).reshape([2] * n_bits + [rows // size, values.shape[1]])
    for bit in range(n_bits):
        parts, bits = _exchange(parts, bits, bit, axis_name, size, index)
    parts = parts.astype(jnp.bfloat16)
    for bit in range(n_bits - 1, -1, -1):
        parts = _gather_back(parts, bit, axis_name, size, index)
    return parts.reshape(rows, values.shape[1]).astype(jnp.float32)


def layer_norm(values, norm_gain):
    row_mean = jnp.mean(values, axis=-1, keepdims=True)
    centered = values - row_mean
    variance = jnp.mean(centered * centered, axis=-1, keepdims=True)
    return centered * lax.rsqrt(variance + EPSILON) * norm_gain


def normalize_rows(scores):
    row_top = jnp.max(scores, axis=-1, keepdims=True)
    exp_scores = jnp.exp(scores - row_top)
    return exp_scores / jnp.sum(exp_scores, axis=-1, keepdims=True)


def gelu_parts(values):
    sqrt_half = np.float32(np.sqrt(0.5))
    tail = lax.erfc(-values * sqrt_half)
    density = jnp.exp(-0.5 * values * values) * np.float32(1.0 / np.sqrt(2.0 * np.pi))
    return 0.5 * values * tail, 0.5 * tail + values * density


def shards(
    tokens,
    image_counts,
    routes,
    w_qkv,
    w_out,
    w_router,
    gain_attn,
    gain_moe,
    w_in,
    w_back,
    cotangent,
):
    rows, width = tokens.shape
    experts = lax.axis_size("expert")
    capacity = 8 * (5 * rows // (16 * experts)) + 8
    overflow = experts * capacity
    images = rows // SEQ
    qkv_cols = w_qkv.shape[1]
    n_route = w_router.shape[1]
    ff = w_in.shape[2]
    row_ids = jnp.arange(rows, dtype=jnp.int32)
    live_int = (row_ids // SEQ < image_counts[0, 0]).astype(jnp.int32)
    live_rows = live_int.astype(jnp.float32)

    dense_local = jnp.concatenate(
        [w_qkv, w_out, w_router, gain_attn[:, None], gain_moe[:, None]], axis=1
    )
    dense_full = lax.all_gather(dense_local, "shard", axis=0, tiled=True)
    full_qkv = dense_full[:, :qkv_cols]
    full_out = dense_full[:, qkv_cols : qkv_cols + width]
    full_router = dense_full[:, qkv_cols + width : qkv_cols + width + n_route]
    gain_one = dense_full[:, -2].astype(jnp.float32)
    gain_two = dense_full[:, -1].astype(jnp.float32)

    back_rows = w_back.shape[1]
    expert_local = jnp.stack(
        [w_in[0], w_back[0].reshape(back_rows * width // ff, ff)], axis=0
    )
    expert_full = lax.all_gather(expert_local, "shard", axis=1, tiled=True)
    expert_first = expert_full[0]
    expert_second = expert_full[1].reshape(ff, width)

    token_f = tokens.astype(jnp.float32)
    attn_in = lax.optimization_barrier(layer_norm(token_f, gain_one).astype(jnp.bfloat16))
    slot = -(-SEQ // 16) * 16
    attn_in_pad = to_slots(attn_in, images, slot)
    projected_pad = jnp.dot(
        attn_in_pad, full_qkv, preferred_element_type=jnp.float32
    ).astype(jnp.bfloat16)
    mixed_rows = from_slots(attention_fwd(projected_pad, images, slot), images, slot)
    hidden_state = token_f + jnp.dot(mixed_rows, full_out, preferred_element_type=jnp.float32)
    moe_in = layer_norm(hidden_state, gain_two).astype(jnp.bfloat16)
    logits = jnp.dot(moe_in, full_router, preferred_element_type=jnp.float32)
    router_probs = normalize_rows(logits)
    expert_ids = jnp.arange(experts, dtype=jnp.int32)
    choose = (routes[:, :, None] == expert_ids).astype(jnp.float32)
    chosen = jnp.sum(choose * router_probs[:, None, :], axis=2)
    pick_table = (routes[:, :, None] == expert_ids).astype(jnp.int32) * live_int[:, None, None]
    flat_picks = pick_table.reshape(rows * 2, experts)
    before = jnp.cumsum(flat_picks, axis=0) - flat_picks
    slot_index = jnp.sum(before * flat_picks, axis=1).reshape(rows, 2)
    position = jnp.where(live_int[:, None] > 0, routes * capacity + slot_index, overflow)

    n_chunks = 2
    part_cap = 8 * ((capacity + 8 * n_chunks - 1) // (8 * n_chunks))
    chunk_sizes = [min(part_cap, capacity - k * part_cap) for k in range(n_chunks)]
    chunk_sizes = [size for size in chunk_sizes if size > 0]
    chunk_starts = [sum(chunk_sizes[:k]) for k in range(len(chunk_sizes))]
    slot_ids = jnp.concatenate(
        [
            (
                jnp.arange(experts, dtype=jnp.int32)[:, None] * capacity
                + start
                + jnp.arange(size, dtype=jnp.int32)[None, :]
            ).reshape(-1)
            for start, size in zip(chunk_starts, chunk_sizes)
        ]
    )[:, None]
    take_first = (slot_ids == position[None, :, 0]).astype(jnp.bfloat16)
    take_second = (slot_ids == position[None, :, 1]).astype(jnp.bfloat16)

    grad_out = cotangent.astype(jnp.float32) * live_rows[:, None]
    weighted = chosen * live_rows[:, None]
    grad_picked = (weighted[:, :, None] * grad_out[:, None, :]).astype(jnp.bfloat16)

    def dispatch_rows(low, high):
        first = take_first[low:high]
        second = take_second[low:high]
        sent_rows = jnp.dot(first + second, moe_in, preferred_element_type=jnp.float32)
        sent_grad = jnp.dot(
            first, grad_picked[:, 0], preferred_element_type=jnp.float32
        ) + jnp.dot(second, grad_picked[:, 1], preferred_element_type=jnp.float32)
        return jnp.concatenate([sent_rows, sent_grad], axis=1).astype(jnp.bfloat16)

    grad_first = None
    grad_second = None
    returned_parts = []
    for start, size in zip(chunk_starts, chunk_sizes):
        arrived = lax.all_to_all(
            dispatch_rows(experts * start, experts * (start + size)).reshape(
                experts, size, 2 * width
            ),
            "expert",
            split_axis=0,
            concat_axis=0,
            tiled=True,
        ).reshape(experts * size, 2 * width)
        flat_arrived = arrived[:, :width]
        flat_grad = arrived[:, width:]
        hidden_grad = lax.dot_general(
            flat_grad, expert_second, COL_CONTRACT, preferred_element_type=jnp.float32
        )
        pre_act = jnp.dot(flat_arrived, expert_first, preferred_element_type=jnp.float32)
        activated, slope = gelu_parts(pre_act)
        activated = activated.astype(jnp.bfloat16)
        pre_grad = (hidden_grad * slope).astype(jnp.bfloat16)
        produced = jnp.dot(
            activated, expert_second, preferred_element_type=jnp.float32
        ).astype(jnp.bfloat16)
        row_grad = lax.dot_general(
            pre_grad, expert_first, COL_CONTRACT, preferred_element_type=jnp.float32
        ).astype(jnp.bfloat16)
        part_second = lax.dot_general(
            activated, flat_grad, ROW_CONTRACT, preferred_element_type=jnp.float32
        )
        part_first = lax.dot_general(
            flat_arrived, pre_grad, ROW_CONTRACT, preferred_element_type=jnp.float32
        )
        grad_first = part_first if grad_first is None else grad_first + part_first
        grad_second = part_second if grad_second is None else grad_second + part_second
        returning = jnp.concatenate([produced, row_grad], axis=1).reshape(
            experts, size, 2 * width
        )
        returned_parts.append(
            lax.all_to_all(returning, "expert", split_axis=0, concat_axis=0, tiled=True)
        )

    expert_grads = jnp.stack(
        [grad_first, grad_second.reshape(width, ff)], axis=0
    ).astype(jnp.bfloat16)
    expert_share = lax.psum_scatter(expert_grads, "shard", scatter_dimension=1, tiled=True)
    expert_share = expert_share.astype(jnp.float32)
    grad_in_share = expert_share[0][None]
    grad_back_share = expert_share[1].reshape(back_rows, width)[None]

    picked_first = None
    picked_second = None
    for start, size, part in zip(chunk_starts, chunk_sizes, returned_parts):
        low, high = experts * start, experts * (start + size)
        part = part.reshape(-1, 2 * width)
        part_first = lax.dot_general(
            take_first[low:high], part, ROW_CONTRACT, preferred_element_type=jnp.float32
        )
        part_second = lax.dot_general(
            take_second[low:high], part, ROW_CONTRACT, preferred_element_type=jnp.float32
        )
        picked_first = part_first if picked_first is None else picked_first + part_first
        picked_second = part_second if picked_second is None else picked_second + part_second
    moe_out = (
        weighted[:, 0:1] * picked_first[:, :width] + weighted[:, 1:2] * picked_second[:, :width]
    )
    output = (live_rows[:, None] * (hidden_state + moe_out)).astype(jnp.bfloat16)
    grad_chosen = jnp.stack(
        [
            jnp.sum(grad_out * picked_first[:, :width], axis=1),
            jnp.sum(grad_out * picked_second[:, :width], axis=1),
        ],
        axis=1,
    ) * live_rows[:, None]
    expert_part = (picked_first[:, width:] + picked_second[:, width:]) * live_rows[:, None]
    prob_sum = jnp.sum(choose * grad_chosen[:, :, None], axis=1)
    logit_grad = (
        router_probs * (prob_sum - jnp.sum(router_probs * prob_sum, axis=-1, keepdims=True))
    ).astype(jnp.bfloat16)
    grad_router = lax.dot_general(
        moe_in, logit_grad, ROW_CONTRACT, preferred_element_type=jnp.float32
    )
    moe_in_grad = expert_part + lax.dot_general(
        logit_grad, full_router, COL_CONTRACT, preferred_element_type=jnp.float32
    )
    _, norm_back = jax.vjp(layer_norm, hidden_state, gain_two)
    state_part, grad_gain_two = norm_back(moe_in_grad)
    state_grad = grad_out + state_part
    branch_grad = state_grad.astype(jnp.bfloat16)
    grad_wout = lax.dot_general(
        mixed_rows, branch_grad, ROW_CONTRACT, preferred_element_type=jnp.float32
    )
    mixed_grad = lax.dot_general(
        branch_grad, full_out, COL_CONTRACT, preferred_element_type=jnp.float32
    )
    mixed_grad = to_slots(mixed_grad.astype(jnp.bfloat16), images, slot)
    grad_q, grad_k, grad_v = attention_bwd(projected_pad, mixed_grad, images, slot)
    projected_grad = jnp.concatenate([grad_q, grad_k, grad_v], axis=1)
    grad_qkv = lax.dot_general(
        attn_in_pad, projected_grad, ROW_CONTRACT, preferred_element_type=jnp.float32
    )
    attn_in_grad = from_slots(
        lax.dot_general(
            projected_grad, full_qkv, COL_CONTRACT, preferred_element_type=jnp.float32
        ),
        images,
        slot,
    )
    _, first_back = jax.vjp(layer_norm, token_f, gain_one)
    token_part, grad_gain_one = first_back(attn_in_grad)
    grad_tokens = (state_grad + token_part).astype(jnp.bfloat16)

    small = jnp.concatenate(
        [grad_router, grad_gain_one[:, None], grad_gain_two[:, None]], axis=1
    )
    small = jnp.pad(small, ((0, 0), (0, 128 - small.shape[1])))
    dense_grads = jnp.concatenate([grad_qkv, grad_wout, small], axis=1)
    n_parts = 3
    bounds = [128 * (dense_grads.shape[1] * k // (128 * n_parts)) for k in range(n_parts)]
    bounds = bounds + [dense_grads.shape[1]]
    dense_total = jnp.concatenate(
        [
            expert_all_reduce(
                shard_reduce_scatter(part, "shard", 128 * (part.shape[1] // 256)), "expert"
            )
            for part in (dense_grads[:, low:high] for low, high in zip(bounds[:-1], bounds[1:]))
        ],
        axis=1,
    )
    return (
        output,
        grad_tokens,
        dense_total[:, :qkv_cols],
        dense_total[:, qkv_cols : qkv_cols + width],
        dense_total[:, qkv_cols + width : qkv_cols + width + n_route],
        dense_total[:, qkv_cols + width + n_route],
        dense_total[:, qkv_cols + width + n_route + 1],
        grad_in_share,
        grad_back_share,
    )


def solution(mesh):
    return _mapped(mesh)


def _mapped(mesh):
    return jax.shard_map(
        shards,
        mesh=mesh,
        in_specs=(
            P(("expert", "shard"), None),
            P("expert", "shard"),
            P(("expert", "shard"), None),
            P("shard", None),
            P("shard", None),
            P("shard", None),
            P("shard"),
            P("shard"),
            P("expert", "shard", None),
            P("expert", "shard", None),
            P(("expert", "shard"), None),
        ),
        out_specs=(
            P(("expert", "shard"), None),
            P(("expert", "shard"), None),
            P("shard", None),
            P("shard", None),
            P("shard", None),
            P("shard"),
            P("shard"),
            P("expert", "shard", None),
            P("expert", "shard", None),
        ),
        check_vma=False,
    )
```

```python
import functools

import jax
import numpy as np
import jax.numpy as jnp
from jax import lax
from jax.experimental import pallas as pl
from jax.experimental.pallas import tpu as pltpu
from jax.sharding import PartitionSpec as P

HD = 64
SEQ = 197


EPSILON = 1e-06
ROW_CONTRACT = (((0,), (0,)), ((), ()))
COL_CONTRACT = (((1,), (1,)), ((), ()))


def _image_of(idx, images):
    count = jnp.zeros(idx.shape, jnp.int32)
    for i in range(1, images + 1):
        count = count + (idx >= i * SEQ).astype(jnp.int32)
    return count


def _same_image(size, images):
    rows = lax.broadcasted_iota(jnp.int32, (size, size), 0)
    cols = lax.broadcasted_iota(jnp.int32, (size, size), 1)
    return _image_of(rows, images) == _image_of(cols, images)


def _softmax_masked(qj, k, same):
    s = lax.dot_general(qj, k, COL_CONTRACT, preferred_element_type=jnp.float32) * (HD ** -0.5)
    s = jnp.where(same, s, -jnp.inf)
    top = jnp.max(s, axis=1, keepdims=True)
    e = jnp.exp(s - top)
    return e / jnp.sum(e, axis=1, keepdims=True)


def attn_fwd_kernel(q_ref, k_ref, v_ref, o_ref, *, images):
    R = q_ref.shape[0]
    q = q_ref[...]
    k = k_ref[...]
    v = v_ref[...]
    same = _same_image(R, images)
    lane = lax.broadcasted_iota(jnp.int32, (1, 2 * HD), 1)
    out = jnp.zeros((R, 2 * HD), jnp.float32)
    for j in range(2):
        in_head = (lane >= HD) == (j == 1)
        p = _softmax_masked(jnp.where(in_head, q, jnp.zeros_like(q)), k, same)
        o = jnp.dot(p.astype(jnp.bfloat16), v, preferred_element_type=jnp.float32)
        out = jnp.where(in_head, o, out)
    o_ref[...] = out.astype(o_ref.dtype)


def attn_bwd_kernel(q_ref, k_ref, v_ref, g_ref, dq_ref, dk_ref, dv_ref, *, images):
    R = q_ref.shape[0]
    q = q_ref[...]
    k = k_ref[...]
    v = v_ref[...]
    g = g_ref[...]
    same = _same_image(R, images)
    lane = lax.broadcasted_iota(jnp.int32, (1, 2 * HD), 1)
    dq = jnp.zeros((R, 2 * HD), jnp.float32)
    dk = jnp.zeros((R, 2 * HD), jnp.float32)
    dv = jnp.zeros((R, 2 * HD), jnp.float32)
    for j in range(2):
        in_head = (lane >= HD) == (j == 1)
        p = _softmax_masked(jnp.where(in_head, q, jnp.zeros_like(q)), k, same)
        gj = jnp.where(in_head, g, jnp.zeros_like(g))
        dp = lax.dot_general(gj, v, COL_CONTRACT, preferred_element_type=jnp.float32)
        ds = (p * (dp - jnp.sum(p * dp, axis=1, keepdims=True))).astype(jnp.bfloat16)
        dq_j = jnp.dot(ds, k, preferred_element_type=jnp.float32) * (HD ** -0.5)
        dk_j = lax.dot_general(ds, q, ROW_CONTRACT, preferred_element_type=jnp.float32) * (HD ** -0.5)
        dv_j = lax.dot_general(p.astype(jnp.bfloat16), g, ROW_CONTRACT, preferred_element_type=jnp.float32)
        dq = jnp.where(in_head, dq_j, dq)
        dk = jnp.where(in_head, dk_j, dk)
        dv = jnp.where(in_head, dv_j, dv)
    dq_ref[...] = dq.astype(dq_ref.dtype)
    dk_ref[...] = dk.astype(dk_ref.dtype)
    dv_ref[...] = dv.astype(dv_ref.dtype)


def attention_fwd(projected, images):
    R = projected.shape[0]
    W = projected.shape[1] // 3
    pairs = W // (2 * HD)
    blk = lambda off: pl.BlockSpec((R, 2 * HD), lambda h: (0, off + h))
    return pl.pallas_call(
        functools.partial(attn_fwd_kernel, images=images),
        grid=(pairs,),
        in_specs=[blk(0), blk(pairs), blk(2 * pairs)],
        out_specs=blk(0),
        out_shape=jax.ShapeDtypeStruct((R, W), jnp.bfloat16),
        compiler_params=pltpu.CompilerParams(vmem_limit_bytes=48 * 1024 * 1024),
    )(projected, projected, projected)


def attention_bwd(projected, mixed_grad, images):
    R = projected.shape[0]
    W = projected.shape[1] // 3
    pairs = W // (2 * HD)
    blk = lambda off: pl.BlockSpec((R, 2 * HD), lambda h: (0, off + h))
    out = jax.ShapeDtypeStruct((R, W), jnp.bfloat16)
    return pl.pallas_call(
        functools.partial(attn_bwd_kernel, images=images),
        grid=(pairs,),
        in_specs=[blk(0), blk(pairs), blk(2 * pairs), blk(0)],
        out_specs=[blk(0), blk(0), blk(0)],
        out_shape=[out, out, out],
        compiler_params=pltpu.CompilerParams(vmem_limit_bytes=48 * 1024 * 1024),
    )(projected, projected, projected, mixed_grad)


def _exchange(values, bits_left, bit, axis_name, size, index):
    axis = bits_left.index(bit)
    mine = (index >> bit) & 1
    keep = lax.dynamic_index_in_dim(values, mine, axis, keepdims=False)
    send = lax.dynamic_index_in_dim(values, 1 - mine, axis, keepdims=False)
    pairs = [(i, i ^ (1 << bit)) for i in range(size)]
    got = lax.ppermute(send.astype(jnp.bfloat16), axis_name, pairs)
    return keep + got.astype(jnp.float32), [b for b in bits_left if b != bit]


def shard_reduce_scatter(values, axis_name, split_col):
    size = lax.axis_size(axis_name)
    index = lax.axis_index(axis_name)
    n_bits = size.bit_length() - 1
    block = values.shape[0] // size
    bits = list(range(n_bits - 1, -1, -1))
    values = values.astype(jnp.float32).reshape([2] * n_bits + [block, values.shape[1]])
    values, bits = _exchange(values, bits, 0, axis_name, size, index)
    first, second = values[..., :split_col], values[..., split_col:]
    first_bits, second_bits = list(bits), list(bits)
    for up, down in zip(range(1, n_bits), range(n_bits - 1, 0, -1)):
        first, first_bits = _exchange(first, first_bits, up, axis_name, size, index)
        second, second_bits = _exchange(second, second_bits, down, axis_name, size, index)
    return jnp.concatenate([first, second], axis=-1)


def expert_all_reduce_doubling(values, axis_name):
    size = lax.axis_size(axis_name)
    n_bits = size.bit_length() - 1
    total = values.astype(jnp.bfloat16)
    for bit in range(n_bits):
        pairs = [(i, i ^ (1 << bit)) for i in range(size)]
        got = lax.ppermute(total, axis_name, pairs)
        total = (total.astype(jnp.float32) + got.astype(jnp.float32)).astype(jnp.bfloat16)
    return total.astype(jnp.float32)


def layer_norm(values, norm_gain):
    row_mean = jnp.mean(values, axis=-1, keepdims=True)
    centered = values - row_mean
    variance = jnp.mean(centered * centered, axis=-1, keepdims=True)
    return centered * lax.rsqrt(variance + EPSILON) * norm_gain


def normalize_rows(scores):
    row_top = jnp.max(scores, axis=-1, keepdims=True)
    exp_scores = jnp.exp(scores - row_top)
    return exp_scores / jnp.sum(exp_scores, axis=-1, keepdims=True)


def gelu_parts(values):
    sqrt_half = np.float32(np.sqrt(0.5))
    tail = lax.erfc(-values * sqrt_half)
    density = jnp.exp(-0.5 * values * values) * np.float32(1.0 / np.sqrt(2.0 * np.pi))
    return 0.5 * values * tail, 0.5 * tail + values * density


def shards(
    tokens,
    image_counts,
    routes,
    w_qkv,
    w_out,
    w_router,
    gain_attn,
    gain_moe,
    w_in,
    w_back,
    cotangent,
):
    rows, width = tokens.shape
    experts = lax.axis_size("expert")
    capacity = 8 * (5 * rows // (16 * experts)) + 8
    overflow = experts * capacity
    images = rows // SEQ
    qkv_cols = w_qkv.shape[1]
    n_route = w_router.shape[1]
    ff = w_in.shape[2]
    row_ids = jnp.arange(rows, dtype=jnp.int32)
    live_int = (row_ids // SEQ < image_counts[0, 0]).astype(jnp.int32)
    live_rows = live_int.astype(jnp.float32)

    dense_local = jnp.concatenate(
        [w_qkv, w_out, w_router, gain_attn[:, None], gain_moe[:, None]], axis=1
    )
    dense_full = lax.all_gather(dense_local, "shard", axis=0, tiled=True)
    full_qkv = dense_full[:, :qkv_cols]
    full_out = dense_full[:, qkv_cols : qkv_cols + width]
    full_router = dense_full[:, qkv_cols + width : qkv_cols + width + n_route]
    gain_one = dense_full[:, -2].astype(jnp.float32)
    gain_two = dense_full[:, -1].astype(jnp.float32)

    back_rows = w_back.shape[1]
    expert_local = jnp.stack(
        [w_in[0], w_back[0].reshape(back_rows * width // ff, ff)], axis=0
    )
    expert_full = lax.all_gather(expert_local, "shard", axis=1, tiled=True)
    expert_first = expert_full[0]
    expert_second = expert_full[1].reshape(ff, width)

    token_f = tokens.astype(jnp.float32)
    attn_in = lax.optimization_barrier(layer_norm(token_f, gain_one).astype(jnp.bfloat16))
    projected = jnp.dot(attn_in, full_qkv, preferred_element_type=jnp.float32).astype(jnp.bfloat16)
    pad_rows = -(-rows // 128) * 128
    projected_pad = jnp.pad(projected, ((0, pad_rows - rows), (0, 0)))
    mixed_rows = attention_fwd(projected_pad, images)[:rows]
    hidden_state = token_f + jnp.dot(mixed_rows, full_out, preferred_element_type=jnp.float32)
    moe_in = layer_norm(hidden_state, gain_two).astype(jnp.bfloat16)
    logits = jnp.dot(moe_in, full_router, preferred_element_type=jnp.float32)
    router_probs = normalize_rows(logits)
    expert_ids = jnp.arange(experts, dtype=jnp.int32)
    choose = (routes[:, :, None] == expert_ids).astype(jnp.float32)
    chosen = jnp.sum(choose * router_probs[:, None, :], axis=2)
    pick_table = (routes[:, :, None] == expert_ids).astype(jnp.int32) * live_int[:, None, None]
    flat_picks = pick_table.reshape(rows * 2, experts)
    before = jnp.cumsum(flat_picks, axis=0) - flat_picks
    slot_index = jnp.sum(before * flat_picks, axis=1).reshape(rows, 2)
    position = jnp.where(live_int[:, None] > 0, routes * capacity + slot_index, overflow)

    first_cap = min(capacity, 8 * round(capacity * 0.47 / 8))
    chunk_sizes = [first_cap, capacity - first_cap]
    chunk_sizes = [size for size in chunk_sizes if size > 0]
    chunk_starts = [sum(chunk_sizes[:k]) for k in range(len(chunk_sizes))]
    slot_ids = jnp.concatenate(
        [
            (
                jnp.arange(experts, dtype=jnp.int32)[:, None] * capacity
                + start
                + jnp.arange(size, dtype=jnp.int32)[None, :]
            ).reshape(-1)
            for start, size in zip(chunk_starts, chunk_sizes)
        ]
    )[:, None]
    take_first = (slot_ids == position[None, :, 0]).astype(jnp.bfloat16)
    take_second = (slot_ids == position[None, :, 1]).astype(jnp.bfloat16)

    grad_out = cotangent.astype(jnp.float32) * live_rows[:, None]
    weighted = chosen * live_rows[:, None]
    grad_picked = (weighted[:, :, None] * grad_out[:, None, :]).astype(jnp.bfloat16)

    def dispatch_rows(low, high):
        first = take_first[low:high]
        second = take_second[low:high]
        sent_rows = jnp.dot(first + second, moe_in, preferred_element_type=jnp.float32)
        sent_grad = jnp.dot(
            first, grad_picked[:, 0], preferred_element_type=jnp.float32
        ) + jnp.dot(second, grad_picked[:, 1], preferred_element_type=jnp.float32)
        return jnp.concatenate([sent_rows, sent_grad], axis=1).astype(jnp.bfloat16)

    grad_first = None
    grad_second = None
    returned_parts = []
    for start, size in zip(chunk_starts, chunk_sizes):
        arrived = lax.all_to_all(
            dispatch_rows(experts * start, experts * (start + size)).reshape(
                experts, size, 2 * width
            ),
            "expert",
            split_axis=0,
            concat_axis=0,
            tiled=True,
        ).reshape(experts * size, 2 * width)
        flat_arrived = arrived[:, :width]
        flat_grad = arrived[:, width:]
        hidden_grad = lax.dot_general(
            flat_grad, expert_second, COL_CONTRACT, preferred_element_type=jnp.float32
        )
        pre_act = jnp.dot(flat_arrived, expert_first, preferred_element_type=jnp.float32)
        activated, slope = gelu_parts(pre_act)
        activated = activated.astype(jnp.bfloat16)
        pre_grad = (hidden_grad * slope).astype(jnp.bfloat16)
        produced = jnp.dot(
            activated, expert_second, preferred_element_type=jnp.float32
        ).astype(jnp.bfloat16)
        row_grad = lax.dot_general(
            pre_grad, expert_first, COL_CONTRACT, preferred_element_type=jnp.float32
        ).astype(jnp.bfloat16)
        part_second = lax.dot_general(
            activated, flat_grad, ROW_CONTRACT, preferred_element_type=jnp.float32
        )
        part_first = lax.dot_general(
            flat_arrived, pre_grad, ROW_CONTRACT, preferred_element_type=jnp.float32
        )
        grad_first = part_first if grad_first is None else grad_first + part_first
        grad_second = part_second if grad_second is None else grad_second + part_second
        returning = jnp.concatenate([produced, row_grad], axis=1).reshape(
            experts, size, 2 * width
        )
        returned_parts.append(
            lax.all_to_all(returning, "expert", split_axis=0, concat_axis=0, tiled=True)
        )

    expert_grads = jnp.stack(
        [grad_first, grad_second.reshape(width, ff)], axis=0
    ).astype(jnp.bfloat16)
    expert_share = lax.psum_scatter(expert_grads, "shard", scatter_dimension=1, tiled=True)
    expert_share = expert_share.astype(jnp.float32)
    grad_in_share = expert_share[0][None]
    grad_back_share = expert_share[1].reshape(back_rows, width)[None]

    picked_first = None
    picked_second = None
    for start, size, part in zip(chunk_starts, chunk_sizes, returned_parts):
        low, high = experts * start, experts * (start + size)
        part = part.reshape(-1, 2 * width)
        part_first = lax.dot_general(
            take_first[low:high], part, ROW_CONTRACT, preferred_element_type=jnp.float32
        )
        part_second = lax.dot_general(
            take_second[low:high], part, ROW_CONTRACT, preferred_element_type=jnp.float32
        )
        picked_first = part_first if picked_first is None else picked_first + part_first
        picked_second = part_second if picked_second is None else picked_second + part_second
    moe_out = (
        weighted[:, 0:1] * picked_first[:, :width] + weighted[:, 1:2] * picked_second[:, :width]
    )
    output = (live_rows[:, None] * (hidden_state + moe_out)).astype(jnp.bfloat16)
    grad_chosen = jnp.stack(
        [
            jnp.sum(grad_out * picked_first[:, :width], axis=1),
            jnp.sum(grad_out * picked_second[:, :width], axis=1),
        ],
        axis=1,
    ) * live_rows[:, None]
    expert_part = (picked_first[:, width:] + picked_second[:, width:]) * live_rows[:, None]
    prob_sum = jnp.sum(choose * grad_chosen[:, :, None], axis=1)
    logit_grad = (
        router_probs * (prob_sum - jnp.sum(router_probs * prob_sum, axis=-1, keepdims=True))
    ).astype(jnp.bfloat16)
    grad_router = lax.dot_general(
        moe_in, logit_grad, ROW_CONTRACT, preferred_element_type=jnp.float32
    )
    moe_in_grad = expert_part + lax.dot_general(
        logit_grad, full_router, COL_CONTRACT, preferred_element_type=jnp.float32
    )
    _, norm_back = jax.vjp(layer_norm, hidden_state, gain_two)
    state_part, grad_gain_two = norm_back(moe_in_grad)
    state_grad = grad_out + state_part
    branch_grad = state_grad.astype(jnp.bfloat16)
    grad_wout = lax.dot_general(
        mixed_rows, branch_grad, ROW_CONTRACT, preferred_element_type=jnp.float32
    )
    mixed_grad = lax.dot_general(
        branch_grad, full_out, COL_CONTRACT, preferred_element_type=jnp.float32
    )
    mixed_grad = jnp.pad(mixed_grad.astype(jnp.bfloat16), ((0, pad_rows - rows), (0, 0)))
    grad_q, grad_k, grad_v = attention_bwd(projected_pad, mixed_grad, images)
    projected_grad = jnp.concatenate([grad_q, grad_k, grad_v], axis=1)
    attn_in_pad = jnp.pad(attn_in, ((0, pad_rows - rows), (0, 0)))
    grad_qkv = lax.dot_general(
        attn_in_pad, projected_grad, ROW_CONTRACT, preferred_element_type=jnp.float32
    )
    attn_in_grad = lax.dot_general(
        projected_grad[:rows], full_qkv, COL_CONTRACT, preferred_element_type=jnp.float32
    )
    _, first_back = jax.vjp(layer_norm, token_f, gain_one)
    token_part, grad_gain_one = first_back(attn_in_grad)
    grad_tokens = (state_grad + token_part).astype(jnp.bfloat16)

    small = jnp.concatenate(
        [grad_router, grad_gain_one[:, None], grad_gain_two[:, None]], axis=1
    )
    small = jnp.pad(small, ((0, 0), (0, 128 - small.shape[1])))
    dense_grads = jnp.concatenate([grad_qkv, grad_wout, small], axis=1)
    n_parts = 3
    bounds = [128 * (dense_grads.shape[1] * k // (128 * n_parts)) for k in range(n_parts)]
    bounds = bounds + [dense_grads.shape[1]]
    dense_total = jnp.concatenate(
        [
            expert_all_reduce_doubling(
                shard_reduce_scatter(part, "shard", 128 * (part.shape[1] // 256)), "expert"
            )
            for part in (dense_grads[:, low:high] for low, high in zip(bounds[:-1], bounds[1:]))
        ],
        axis=1,
    )
    return (
        output,
        grad_tokens,
        dense_total[:, :qkv_cols],
        dense_total[:, qkv_cols : qkv_cols + width],
        dense_total[:, qkv_cols + width : qkv_cols + width + n_route],
        dense_total[:, qkv_cols + width + n_route],
        dense_total[:, qkv_cols + width + n_route + 1],
        grad_in_share,
        grad_back_share,
    )


def solution(mesh):
    return _mapped(mesh)


def _mapped(mesh):
    return jax.shard_map(
        shards,
        mesh=mesh,
        in_specs=(
            P(("expert", "shard"), None),
            P("expert", "shard"),
            P(("expert", "shard"), None),
            P("shard", None),
            P("shard", None),
            P("shard", None),
            P("shard"),
            P("shard"),
            P("expert", "shard", None),
            P("expert", "shard", None),
            P(("expert", "shard"), None),
        ),
        out_specs=(
            P(("expert", "shard"), None),
            P(("expert", "shard"), None),
            P("shard", None),
            P("shard", None),
            P("shard", None),
            P("shard"),
            P("shard"),
            P("expert", "shard", None),
            P("expert", "shard", None),
        ),
        check_vma=False,
    )
```

```python
import functools

import jax
import numpy as np
import jax.numpy as jnp
from jax import lax
from jax.experimental import pallas as pl
from jax.experimental.pallas import tpu as pltpu
from jax.sharding import PartitionSpec as P

HD = 64
SEQ = 197


EPSILON = 1e-06
ROW_CONTRACT = (((0,), (0,)), ((), ()))
COL_CONTRACT = (((1,), (1,)), ((), ()))


def _image_of(idx, images):
    count = jnp.zeros(idx.shape, jnp.int32)
    for i in range(1, images + 1):
        count = count + (idx >= i * SEQ).astype(jnp.int32)
    return count


def _same_image(size, images):
    rows = lax.broadcasted_iota(jnp.int32, (size, size), 0)
    cols = lax.broadcasted_iota(jnp.int32, (size, size), 1)
    return _image_of(rows, images) == _image_of(cols, images)


def _softmax_masked(qj, k, same):
    s = lax.dot_general(qj, k, COL_CONTRACT, preferred_element_type=jnp.float32) * (HD ** -0.5)
    s = jnp.where(same, s, -jnp.inf)
    top = jnp.max(s, axis=1, keepdims=True)
    e = jnp.exp(s - top)
    return e / jnp.sum(e, axis=1, keepdims=True)


def attn_fwd_kernel(q_ref, k_ref, v_ref, o_ref, *, images):
    R = q_ref.shape[0]
    q = q_ref[...]
    k = k_ref[...]
    v = v_ref[...]
    same = _same_image(R, images)
    lane = lax.broadcasted_iota(jnp.int32, (1, 2 * HD), 1)
    out = jnp.zeros((R, 2 * HD), jnp.float32)
    for j in range(2):
        in_head = (lane >= HD) == (j == 1)
        p = _softmax_masked(jnp.where(in_head, q, jnp.zeros_like(q)), k, same)
        o = jnp.dot(p.astype(jnp.bfloat16), v, preferred_element_type=jnp.float32)
        out = jnp.where(in_head, o, out)
    o_ref[...] = out.astype(o_ref.dtype)


def attn_bwd_kernel(q_ref, k_ref, v_ref, g_ref, dq_ref, dk_ref, dv_ref, *, images):
    R = q_ref.shape[0]
    q = q_ref[...]
    k = k_ref[...]
    v = v_ref[...]
    g = g_ref[...]
    same = _same_image(R, images)
    lane = lax.broadcasted_iota(jnp.int32, (1, 2 * HD), 1)
    dq = jnp.zeros((R, 2 * HD), jnp.float32)
    dk = jnp.zeros((R, 2 * HD), jnp.float32)
    dv = jnp.zeros((R, 2 * HD), jnp.float32)
    for j in range(2):
        in_head = (lane >= HD) == (j == 1)
        p = _softmax_masked(jnp.where(in_head, q, jnp.zeros_like(q)), k, same)
        gj = jnp.where(in_head, g, jnp.zeros_like(g))
        dp = lax.dot_general(gj, v, COL_CONTRACT, preferred_element_type=jnp.float32)
        ds = (p * (dp - jnp.sum(p * dp, axis=1, keepdims=True))).astype(jnp.bfloat16)
        dq_j = jnp.dot(ds, k, preferred_element_type=jnp.float32) * (HD ** -0.5)
        dk_j = lax.dot_general(ds, q, ROW_CONTRACT, preferred_element_type=jnp.float32) * (HD ** -0.5)
        dv_j = lax.dot_general(p.astype(jnp.bfloat16), g, ROW_CONTRACT, preferred_element_type=jnp.float32)
        dq = jnp.where(in_head, dq_j, dq)
        dk = jnp.where(in_head, dk_j, dk)
        dv = jnp.where(in_head, dv_j, dv)
    dq_ref[...] = dq.astype(dq_ref.dtype)
    dk_ref[...] = dk.astype(dk_ref.dtype)
    dv_ref[...] = dv.astype(dv_ref.dtype)


def attention_fwd(projected, images):
    R = projected.shape[0]
    W = projected.shape[1] // 3
    pairs = W // (2 * HD)
    blk = lambda off: pl.BlockSpec((R, 2 * HD), lambda h: (0, off + h))
    return pl.pallas_call(
        functools.partial(attn_fwd_kernel, images=images),
        grid=(pairs,),
        in_specs=[blk(0), blk(pairs), blk(2 * pairs)],
        out_specs=blk(0),
        out_shape=jax.ShapeDtypeStruct((R, W), jnp.bfloat16),
        compiler_params=pltpu.CompilerParams(vmem_limit_bytes=48 * 1024 * 1024),
    )(projected, projected, projected)


def attention_bwd(projected, mixed_grad, images):
    R = projected.shape[0]
    W = projected.shape[1] // 3
    pairs = W // (2 * HD)
    blk = lambda off: pl.BlockSpec((R, 2 * HD), lambda h: (0, off + h))
    out = jax.ShapeDtypeStruct((R, W), jnp.bfloat16)
    return pl.pallas_call(
        functools.partial(attn_bwd_kernel, images=images),
        grid=(pairs,),
        in_specs=[blk(0), blk(pairs), blk(2 * pairs), blk(0)],
        out_specs=[blk(0), blk(0), blk(0)],
        out_shape=[out, out, out],
        compiler_params=pltpu.CompilerParams(vmem_limit_bytes=48 * 1024 * 1024),
    )(projected, projected, projected, mixed_grad)


def _exchange(values, bits_left, bit, axis_name, size, index):
    axis = bits_left.index(bit)
    mine = (index >> bit) & 1
    keep = lax.dynamic_index_in_dim(values, mine, axis, keepdims=False)
    send = lax.dynamic_index_in_dim(values, 1 - mine, axis, keepdims=False)
    pairs = [(i, i ^ (1 << bit)) for i in range(size)]
    got = lax.ppermute(send.astype(jnp.bfloat16), axis_name, pairs)
    return keep + got.astype(jnp.float32), [b for b in bits_left if b != bit]


def shard_reduce_scatter(values, axis_name, split_col):
    size = lax.axis_size(axis_name)
    index = lax.axis_index(axis_name)
    n_bits = size.bit_length() - 1
    block = values.shape[0] // size
    bits = list(range(n_bits - 1, -1, -1))
    values = values.astype(jnp.float32).reshape([2] * n_bits + [block, values.shape[1]])
    values, bits = _exchange(values, bits, 0, axis_name, size, index)
    first, second = values[..., :split_col], values[..., split_col:]
    first_bits, second_bits = list(bits), list(bits)
    for up, down in zip(range(1, n_bits), range(n_bits - 1, 0, -1)):
        first, first_bits = _exchange(first, first_bits, up, axis_name, size, index)
        second, second_bits = _exchange(second, second_bits, down, axis_name, size, index)
    return jnp.concatenate([first, second], axis=-1)


def expert_all_reduce_doubling(values, axis_name):
    size = lax.axis_size(axis_name)
    n_bits = size.bit_length() - 1
    total = values.astype(jnp.bfloat16)
    for bit in range(n_bits):
        pairs = [(i, i ^ (1 << bit)) for i in range(size)]
        got = lax.ppermute(total, axis_name, pairs)
        total = (total.astype(jnp.float32) + got.astype(jnp.float32)).astype(jnp.bfloat16)
    return total.astype(jnp.float32)


def layer_norm(values, norm_gain):
    row_mean = jnp.mean(values, axis=-1, keepdims=True)
    centered = values - row_mean
    variance = jnp.mean(centered * centered, axis=-1, keepdims=True)
    return centered * lax.rsqrt(variance + EPSILON) * norm_gain


def normalize_rows(scores):
    row_top = jnp.max(scores, axis=-1, keepdims=True)
    exp_scores = jnp.exp(scores - row_top)
    return exp_scores / jnp.sum(exp_scores, axis=-1, keepdims=True)


def gelu_parts(values):
    sqrt_half = np.float32(np.sqrt(0.5))
    tail = lax.erfc(-values * sqrt_half)
    density = jnp.exp(-0.5 * values * values) * np.float32(1.0 / np.sqrt(2.0 * np.pi))
    return 0.5 * values * tail, 0.5 * tail + values * density


def shards(
    tokens,
    image_counts,
    routes,
    w_qkv,
    w_out,
    w_router,
    gain_attn,
    gain_moe,
    w_in,
    w_back,
    cotangent,
):
    rows, width = tokens.shape
    experts = lax.axis_size("expert")
    capacity = 8 * (5 * rows // (16 * experts)) + 8
    overflow = experts * capacity
    images = rows // SEQ
    qkv_cols = w_qkv.shape[1]
    n_route = w_router.shape[1]
    ff = w_in.shape[2]
    row_ids = jnp.arange(rows, dtype=jnp.int32)
    live_int = (row_ids // SEQ < image_counts[0, 0]).astype(jnp.int32)
    live_rows = live_int.astype(jnp.float32)

    dense_local = jnp.concatenate(
        [w_qkv, w_out, w_router, gain_attn[:, None], gain_moe[:, None]], axis=1
    )
    dense_full = lax.all_gather(dense_local, "shard", axis=0, tiled=True)
    full_qkv = dense_full[:, :qkv_cols]
    full_out = dense_full[:, qkv_cols : qkv_cols + width]
    full_router = dense_full[:, qkv_cols + width : qkv_cols + width + n_route]
    gain_one = dense_full[:, -2].astype(jnp.float32)
    gain_two = dense_full[:, -1].astype(jnp.float32)

    back_rows = w_back.shape[1]
    expert_local = jnp.stack(
        [w_in[0], w_back[0].reshape(back_rows * width // ff, ff)], axis=0
    )
    expert_full = lax.all_gather(expert_local, "shard", axis=1, tiled=True)
    expert_first = expert_full[0]
    expert_second = expert_full[1].reshape(ff, width)

    token_f = tokens.astype(jnp.float32)
    attn_in = lax.optimization_barrier(layer_norm(token_f, gain_one).astype(jnp.bfloat16))
    projected = jnp.dot(attn_in, full_qkv, preferred_element_type=jnp.float32).astype(jnp.bfloat16)
    pad_rows = -(-rows // 128) * 128
    projected_pad = jnp.pad(projected, ((0, pad_rows - rows), (0, 0)))
    mixed_rows = attention_fwd(projected_pad, images)[:rows]
    hidden_state = token_f + jnp.dot(mixed_rows, full_out, preferred_element_type=jnp.float32)
    moe_in = layer_norm(hidden_state, gain_two).astype(jnp.bfloat16)
    logits = jnp.dot(moe_in, full_router, preferred_element_type=jnp.float32)
    router_probs = normalize_rows(logits)
    expert_ids = jnp.arange(experts, dtype=jnp.int32)
    choose = (routes[:, :, None] == expert_ids).astype(jnp.float32)
    chosen = jnp.sum(choose * router_probs[:, None, :], axis=2)
    pick_table = (routes[:, :, None] == expert_ids).astype(jnp.int32) * live_int[:, None, None]
    flat_picks = pick_table.reshape(rows * 2, experts)
    before = jnp.cumsum(flat_picks, axis=0) - flat_picks
    slot_index = jnp.sum(before * flat_picks, axis=1).reshape(rows, 2)
    position = jnp.where(live_int[:, None] > 0, routes * capacity + slot_index, overflow)

    n_chunks = 2
    part_cap = 8 * ((capacity + 8 * n_chunks - 1) // (8 * n_chunks))
    chunk_sizes = [min(part_cap, capacity - k * part_cap) for k in range(n_chunks)]
    chunk_sizes = [size for size in chunk_sizes if size > 0]
    chunk_starts = [sum(chunk_sizes[:k]) for k in range(len(chunk_sizes))]
    slot_ids = jnp.concatenate(
        [
            (
                jnp.arange(experts, dtype=jnp.int32)[:, None] * capacity
                + start
                + jnp.arange(size, dtype=jnp.int32)[None, :]
            ).reshape(-1)
            for start, size in zip(chunk_starts, chunk_sizes)
        ]
    )[:, None]
    take_first = (slot_ids == position[None, :, 0]).astype(jnp.bfloat16)
    take_second = (slot_ids == position[None, :, 1]).astype(jnp.bfloat16)

    grad_out = cotangent.astype(jnp.float32) * live_rows[:, None]
    weighted = chosen * live_rows[:, None]
    grad_picked = (weighted[:, :, None] * grad_out[:, None, :]).astype(jnp.bfloat16)

    def dispatch_rows(low, high):
        first = take_first[low:high]
        second = take_second[low:high]
        sent_rows = jnp.dot(first + second, moe_in, preferred_element_type=jnp.float32)
        sent_grad = jnp.dot(
            first, grad_picked[:, 0], preferred_element_type=jnp.float32
        ) + jnp.dot(second, grad_picked[:, 1], preferred_element_type=jnp.float32)
        return jnp.concatenate([sent_rows, sent_grad], axis=1).astype(jnp.bfloat16)

    grad_first = None
    grad_second = None
    returned_parts = []
    for start, size in zip(chunk_starts, chunk_sizes):
        arrived = lax.all_to_all(
            dispatch_rows(experts * start, experts * (start + size)).reshape(
                experts, size, 2 * width
            ),
            "expert",
            split_axis=0,
            concat_axis=0,
            tiled=True,
        ).reshape(experts * size, 2 * width)
        flat_arrived = arrived[:, :width]
        flat_grad = arrived[:, width:]
        hidden_grad = lax.dot_general(
            flat_grad, expert_second, COL_CONTRACT, preferred_element_type=jnp.float32
        )
        pre_act = jnp.dot(flat_arrived, expert_first, preferred_element_type=jnp.float32)
        activated, slope = gelu_parts(pre_act)
        activated = activated.astype(jnp.bfloat16)
        pre_grad = (hidden_grad * slope).astype(jnp.bfloat16)
        produced = jnp.dot(
            activated, expert_second, preferred_element_type=jnp.float32
        ).astype(jnp.bfloat16)
        row_grad = lax.dot_general(
            pre_grad, expert_first, COL_CONTRACT, preferred_element_type=jnp.float32
        ).astype(jnp.bfloat16)
        part_second = lax.dot_general(
            activated, flat_grad, ROW_CONTRACT, preferred_element_type=jnp.float32
        )
        part_first = lax.dot_general(
            flat_arrived, pre_grad, ROW_CONTRACT, preferred_element_type=jnp.float32
        )
        grad_first = part_first if grad_first is None else grad_first + part_first
        grad_second = part_second if grad_second is None else grad_second + part_second
        returning = jnp.concatenate([produced, row_grad], axis=1).reshape(
            experts, size, 2 * width
        )
        returned_parts.append(
            lax.all_to_all(returning, "expert", split_axis=0, concat_axis=0, tiled=True)
        )

    expert_grads = jnp.stack(
        [grad_first, grad_second.reshape(width, ff)], axis=0
    ).astype(jnp.bfloat16)
    expert_share = lax.psum_scatter(expert_grads, "shard", scatter_dimension=1, tiled=True)
    expert_share = expert_share.astype(jnp.float32)
    grad_in_share = expert_share[0][None]
    grad_back_share = expert_share[1].reshape(back_rows, width)[None]

    picked_first = None
    picked_second = None
    for start, size, part in zip(chunk_starts, chunk_sizes, returned_parts):
        low, high = experts * start, experts * (start + size)
        part = part.reshape(-1, 2 * width)
        part_first = lax.dot_general(
            take_first[low:high], part, ROW_CONTRACT, preferred_element_type=jnp.float32
        )
        part_second = lax.dot_general(
            take_second[low:high], part, ROW_CONTRACT, preferred_element_type=jnp.float32
        )
        picked_first = part_first if picked_first is None else picked_first + part_first
        picked_second = part_second if picked_second is None else picked_second + part_second
    moe_out = (
        weighted[:, 0:1] * picked_first[:, :width] + weighted[:, 1:2] * picked_second[:, :width]
    )
    output = (live_rows[:, None] * (hidden_state + moe_out)).astype(jnp.bfloat16)
    grad_chosen = jnp.stack(
        [
            jnp.sum(grad_out * picked_first[:, :width], axis=1),
            jnp.sum(grad_out * picked_second[:, :width], axis=1),
        ],
        axis=1,
    ) * live_rows[:, None]
    expert_part = (picked_first[:, width:] + picked_second[:, width:]) * live_rows[:, None]
    prob_sum = jnp.sum(choose * grad_chosen[:, :, None], axis=1)
    logit_grad = (
        router_probs * (prob_sum - jnp.sum(router_probs * prob_sum, axis=-1, keepdims=True))
    ).astype(jnp.bfloat16)
    grad_router = lax.dot_general(
        moe_in, logit_grad, ROW_CONTRACT, preferred_element_type=jnp.float32
    )
    moe_in_grad = expert_part + lax.dot_general(
        logit_grad, full_router, COL_CONTRACT, preferred_element_type=jnp.float32
    )
    _, norm_back = jax.vjp(layer_norm, hidden_state, gain_two)
    state_part, grad_gain_two = norm_back(moe_in_grad)
    state_grad = grad_out + state_part
    branch_grad = state_grad.astype(jnp.bfloat16)
    grad_wout = lax.dot_general(
        mixed_rows, branch_grad, ROW_CONTRACT, preferred_element_type=jnp.float32
    )
    mixed_grad = lax.dot_general(
        branch_grad, full_out, COL_CONTRACT, preferred_element_type=jnp.float32
    )
    mixed_grad = jnp.pad(mixed_grad.astype(jnp.bfloat16), ((0, pad_rows - rows), (0, 0)))
    grad_q, grad_k, grad_v = attention_bwd(projected_pad, mixed_grad, images)
    projected_grad = jnp.concatenate([grad_q, grad_k, grad_v], axis=1)
    attn_in_pad = jnp.pad(attn_in, ((0, pad_rows - rows), (0, 0)))
    grad_qkv = lax.dot_general(
        attn_in_pad, projected_grad, ROW_CONTRACT, preferred_element_type=jnp.float32
    )
    attn_in_grad = lax.dot_general(
        projected_grad[:rows], full_qkv, COL_CONTRACT, preferred_element_type=jnp.float32
    )
    _, first_back = jax.vjp(layer_norm, token_f, gain_one)
    token_part, grad_gain_one = first_back(attn_in_grad)
    grad_tokens = (state_grad + token_part).astype(jnp.bfloat16)

    small = jnp.concatenate(
        [grad_router, grad_gain_one[:, None], grad_gain_two[:, None]], axis=1
    )
    small = jnp.pad(small, ((0, 0), (0, 128 - small.shape[1])))
    dense_grads = jnp.concatenate([grad_qkv, grad_wout, small], axis=1)
    n_parts = 4
    bounds = [128 * (dense_grads.shape[1] * k // (128 * n_parts)) for k in range(n_parts)]
    bounds = bounds + [dense_grads.shape[1]]
    dense_total = jnp.concatenate(
        [
            expert_all_reduce_doubling(
                shard_reduce_scatter(part, "shard", 128 * (part.shape[1] // 256)), "expert"
            )
            for part in (dense_grads[:, low:high] for low, high in zip(bounds[:-1], bounds[1:]))
        ],
        axis=1,
    )
    return (
        output,
        grad_tokens,
        dense_total[:, :qkv_cols],
        dense_total[:, qkv_cols : qkv_cols + width],
        dense_total[:, qkv_cols + width : qkv_cols + width + n_route],
        dense_total[:, qkv_cols + width + n_route],
        dense_total[:, qkv_cols + width + n_route + 1],
        grad_in_share,
        grad_back_share,
    )


def solution(mesh):
    return _mapped(mesh)


def _mapped(mesh):
    return jax.shard_map(
        shards,
        mesh=mesh,
        in_specs=(
            P(("expert", "shard"), None),
            P("expert", "shard"),
            P(("expert", "shard"), None),
            P("shard", None),
            P("shard", None),
            P("shard", None),
            P("shard"),
            P("shard"),
            P("expert", "shard", None),
            P("expert", "shard", None),
            P(("expert", "shard"), None),
        ),
        out_specs=(
            P(("expert", "shard"), None),
            P(("expert", "shard"), None),
            P("shard", None),
            P("shard", None),
            P("shard", None),
            P("shard"),
            P("shard"),
            P("expert", "shard", None),
            P("expert", "shard", None),
        ),
        check_vma=False,
    )
```

```python
import functools

import jax
import numpy as np
import jax.numpy as jnp
from jax import lax
from jax.experimental import pallas as pl
from jax.experimental.pallas import tpu as pltpu
from jax.sharding import PartitionSpec as P

HD = 64
SEQ = 197


EPSILON = 1e-06
ROW_CONTRACT = (((0,), (0,)), ((), ()))
COL_CONTRACT = (((1,), (1,)), ((), ()))


def _image_of(idx, images):
    count = jnp.zeros(idx.shape, jnp.int32)
    for i in range(1, images + 1):
        count = count + (idx >= i * SEQ).astype(jnp.int32)
    return count


def _same_image(size, images):
    rows = lax.broadcasted_iota(jnp.int32, (size, size), 0)
    cols = lax.broadcasted_iota(jnp.int32, (size, size), 1)
    return _image_of(rows, images) == _image_of(cols, images)


def _softmax_masked(qj, k, same):
    s = lax.dot_general(qj, k, COL_CONTRACT, preferred_element_type=jnp.float32) * (HD ** -0.5)
    s = jnp.where(same, s, -jnp.inf)
    top = jnp.max(s, axis=1, keepdims=True)
    e = jnp.exp(s - top)
    return e / jnp.sum(e, axis=1, keepdims=True)


def attn_fwd_kernel(q_ref, k_ref, v_ref, o_ref, *, images):
    R = q_ref.shape[0]
    q = q_ref[...]
    k = k_ref[...]
    v = v_ref[...]
    same = _same_image(R, images)
    lane = lax.broadcasted_iota(jnp.int32, (1, 2 * HD), 1)
    out = jnp.zeros((R, 2 * HD), jnp.float32)
    for j in range(2):
        in_head = (lane >= HD) == (j == 1)
        p = _softmax_masked(jnp.where(in_head, q, jnp.zeros_like(q)), k, same)
        o = jnp.dot(p.astype(jnp.bfloat16), v, preferred_element_type=jnp.float32)
        out = jnp.where(in_head, o, out)
    o_ref[...] = out.astype(o_ref.dtype)


def attn_bwd_kernel(q_ref, k_ref, v_ref, g_ref, dq_ref, dk_ref, dv_ref, *, images):
    R = q_ref.shape[0]
    q = q_ref[...]
    k = k_ref[...]
    v = v_ref[...]
    g = g_ref[...]
    same = _same_image(R, images)
    lane = lax.broadcasted_iota(jnp.int32, (1, 2 * HD), 1)
    dq = jnp.zeros((R, 2 * HD), jnp.float32)
    dk = jnp.zeros((R, 2 * HD), jnp.float32)
    dv = jnp.zeros((R, 2 * HD), jnp.float32)
    for j in range(2):
        in_head = (lane >= HD) == (j == 1)
        p = _softmax_masked(jnp.where(in_head, q, jnp.zeros_like(q)), k, same)
        gj = jnp.where(in_head, g, jnp.zeros_like(g))
        dp = lax.dot_general(gj, v, COL_CONTRACT, preferred_element_type=jnp.float32)
        ds = (p * (dp - jnp.sum(p * dp, axis=1, keepdims=True))).astype(jnp.bfloat16)
        dq_j = jnp.dot(ds, k, preferred_element_type=jnp.float32) * (HD ** -0.5)
        dk_j = lax.dot_general(ds, q, ROW_CONTRACT, preferred_element_type=jnp.float32) * (HD ** -0.5)
        dv_j = lax.dot_general(p.astype(jnp.bfloat16), g, ROW_CONTRACT, preferred_element_type=jnp.float32)
        dq = jnp.where(in_head, dq_j, dq)
        dk = jnp.where(in_head, dk_j, dk)
        dv = jnp.where(in_head, dv_j, dv)
    dq_ref[...] = dq.astype(dq_ref.dtype)
    dk_ref[...] = dk.astype(dk_ref.dtype)
    dv_ref[...] = dv.astype(dv_ref.dtype)


def attention_fwd(projected, images):
    R = projected.shape[0]
    W = projected.shape[1] // 3
    pairs = W // (2 * HD)
    blk = lambda off: pl.BlockSpec((R, 2 * HD), lambda h: (0, off + h))
    return pl.pallas_call(
        functools.partial(attn_fwd_kernel, images=images),
        grid=(pairs,),
        in_specs=[blk(0), blk(pairs), blk(2 * pairs)],
        out_specs=blk(0),
        out_shape=jax.ShapeDtypeStruct((R, W), jnp.bfloat16),
        compiler_params=pltpu.CompilerParams(vmem_limit_bytes=48 * 1024 * 1024),
    )(projected, projected, projected)


def attention_bwd(projected, mixed_grad, images):
    R = projected.shape[0]
    W = projected.shape[1] // 3
    pairs = W // (2 * HD)
    blk = lambda off: pl.BlockSpec((R, 2 * HD), lambda h: (0, off + h))
    out = jax.ShapeDtypeStruct((R, W), jnp.bfloat16)
    return pl.pallas_call(
        functools.partial(attn_bwd_kernel, images=images),
        grid=(pairs,),
        in_specs=[blk(0), blk(pairs), blk(2 * pairs), blk(0)],
        out_specs=[blk(0), blk(0), blk(0)],
        out_shape=[out, out, out],
        compiler_params=pltpu.CompilerParams(vmem_limit_bytes=48 * 1024 * 1024),
    )(projected, projected, projected, mixed_grad)


def _exchange(values, bits_left, bit, axis_name, size, index):
    axis = bits_left.index(bit)
    mine = (index >> bit) & 1
    keep = lax.dynamic_index_in_dim(values, mine, axis, keepdims=False)
    send = lax.dynamic_index_in_dim(values, 1 - mine, axis, keepdims=False)
    pairs = [(i, i ^ (1 << bit)) for i in range(size)]
    got = lax.ppermute(send.astype(jnp.bfloat16), axis_name, pairs)
    return keep + got.astype(jnp.float32), [b for b in bits_left if b != bit]


def shard_reduce_scatter(values, axis_name, split_col):
    size = lax.axis_size(axis_name)
    index = lax.axis_index(axis_name)
    n_bits = size.bit_length() - 1
    block = values.shape[0] // size
    bits = list(range(n_bits - 1, -1, -1))
    values = values.astype(jnp.float32).reshape([2] * n_bits + [block, values.shape[1]])
    values, bits = _exchange(values, bits, 0, axis_name, size, index)
    first, second = values[..., :split_col], values[..., split_col:]
    first_bits, second_bits = list(bits), list(bits)
    for up, down in zip(range(1, n_bits), range(n_bits - 1, 0, -1)):
        first, first_bits = _exchange(first, first_bits, up, axis_name, size, index)
        second, second_bits = _exchange(second, second_bits, down, axis_name, size, index)
    return jnp.concatenate([first, second], axis=-1)


def expert_all_reduce_doubling(values, axis_name):
    size = lax.axis_size(axis_name)
    n_bits = size.bit_length() - 1
    total = values.astype(jnp.bfloat16)
    for bit in range(n_bits):
        pairs = [(i, i ^ (1 << bit)) for i in range(size)]
        got = lax.ppermute(total, axis_name, pairs)
        total = (total.astype(jnp.float32) + got.astype(jnp.float32)).astype(jnp.bfloat16)
    return total.astype(jnp.float32)


def layer_norm(values, norm_gain):
    row_mean = jnp.mean(values, axis=-1, keepdims=True)
    centered = values - row_mean
    variance = jnp.mean(centered * centered, axis=-1, keepdims=True)
    return centered * lax.rsqrt(variance + EPSILON) * norm_gain


def normalize_rows(scores):
    row_top = jnp.max(scores, axis=-1, keepdims=True)
    exp_scores = jnp.exp(scores - row_top)
    return exp_scores / jnp.sum(exp_scores, axis=-1, keepdims=True)


def gelu_parts(values):
    sqrt_half = np.float32(np.sqrt(0.5))
    tail = lax.erfc(-values * sqrt_half)
    density = jnp.exp(-0.5 * values * values) * np.float32(1.0 / np.sqrt(2.0 * np.pi))
    return 0.5 * values * tail, 0.5 * tail + values * density


def shards(
    tokens,
    image_counts,
    routes,
    w_qkv,
    w_out,
    w_router,
    gain_attn,
    gain_moe,
    w_in,
    w_back,
    cotangent,
):
    rows, width = tokens.shape
    experts = lax.axis_size("expert")
    capacity = 8 * (5 * rows // (16 * experts)) + 8
    overflow = experts * capacity
    images = rows // SEQ
    qkv_cols = w_qkv.shape[1]
    n_route = w_router.shape[1]
    ff = w_in.shape[2]
    row_ids = jnp.arange(rows, dtype=jnp.int32)
    live_int = (row_ids // SEQ < image_counts[0, 0]).astype(jnp.int32)
    live_rows = live_int.astype(jnp.float32)

    small_local = jnp.concatenate([w_router, gain_attn[:, None], gain_moe[:, None]], axis=1)
    small_local = jnp.pad(small_local, ((0, 0), (0, -small_local.shape[1] % 128)))
    dense_local = jnp.concatenate([w_qkv, w_out, small_local], axis=1)
    dense_full = lax.all_gather(dense_local, "shard", axis=0, tiled=True)
    full_qkv = dense_full[:, :qkv_cols]
    full_out = dense_full[:, qkv_cols : qkv_cols + width]
    small_at = qkv_cols + width
    full_router = dense_full[:, small_at : small_at + n_route]
    gain_one = dense_full[:, small_at + n_route].astype(jnp.float32)
    gain_two = dense_full[:, small_at + n_route + 1].astype(jnp.float32)

    back_rows = w_back.shape[1]
    expert_local = jnp.stack(
        [w_in[0], w_back[0].reshape(back_rows * width // ff, ff)], axis=0
    )
    expert_full = lax.all_gather(expert_local, "shard", axis=1, tiled=True)
    expert_first = expert_full[0]
    expert_second = expert_full[1].reshape(ff, width)

    token_f = tokens.astype(jnp.float32)
    attn_in = lax.optimization_barrier(layer_norm(token_f, gain_one).astype(jnp.bfloat16))
    projected = jnp.dot(attn_in, full_qkv, preferred_element_type=jnp.float32).astype(jnp.bfloat16)
    pad_rows = -(-rows // 128) * 128
    projected_pad = jnp.pad(projected, ((0, pad_rows - rows), (0, 0)))
    mixed_rows = attention_fwd(projected_pad, images)[:rows]
    hidden_state = token_f + jnp.dot(mixed_rows, full_out, preferred_element_type=jnp.float32)
    moe_in = layer_norm(hidden_state, gain_two).astype(jnp.bfloat16)
    logits = jnp.dot(moe_in, full_router, preferred_element_type=jnp.float32)
    router_probs = normalize_rows(logits)
    expert_ids = jnp.arange(experts, dtype=jnp.int32)
    choose = (routes[:, :, None] == expert_ids).astype(jnp.float32)
    chosen = jnp.sum(choose * router_probs[:, None, :], axis=2)
    pick_table = (routes[:, :, None] == expert_ids).astype(jnp.int32) * live_int[:, None, None]
    flat_picks = pick_table.reshape(rows * 2, experts)
    before = jnp.cumsum(flat_picks, axis=0) - flat_picks
    slot_index = jnp.sum(before * flat_picks, axis=1).reshape(rows, 2)
    position = jnp.where(live_int[:, None] > 0, routes * capacity + slot_index, overflow)

    n_chunks = 2
    part_cap = 8 * ((capacity + 8 * n_chunks - 1) // (8 * n_chunks))
    chunk_sizes = [min(part_cap, capacity - k * part_cap) for k in range(n_chunks)]
    chunk_sizes = [size for size in chunk_sizes if size > 0]
    chunk_starts = [sum(chunk_sizes[:k]) for k in range(len(chunk_sizes))]
    slot_ids = jnp.concatenate(
        [
            (
                jnp.arange(experts, dtype=jnp.int32)[:, None] * capacity
                + start
                + jnp.arange(size, dtype=jnp.int32)[None, :]
            ).reshape(-1)
            for start, size in zip(chunk_starts, chunk_sizes)
        ]
    )[:, None]
    take_first = (slot_ids == position[None, :, 0]).astype(jnp.bfloat16)
    take_second = (slot_ids == position[None, :, 1]).astype(jnp.bfloat16)

    grad_out = cotangent.astype(jnp.float32) * live_rows[:, None]
    weighted = chosen * live_rows[:, None]
    grad_picked = (weighted[:, :, None] * grad_out[:, None, :]).astype(jnp.bfloat16)

    def dispatch_rows(low, high):
        first = take_first[low:high]
        second = take_second[low:high]
        sent_rows = jnp.dot(first + second, moe_in, preferred_element_type=jnp.float32)
        sent_grad = jnp.dot(
            first, grad_picked[:, 0], preferred_element_type=jnp.float32
        ) + jnp.dot(second, grad_picked[:, 1], preferred_element_type=jnp.float32)
        return jnp.concatenate([sent_rows, sent_grad], axis=1).astype(jnp.bfloat16)

    grad_first = None
    grad_second = None
    returned_parts = []
    for start, size in zip(chunk_starts, chunk_sizes):
        arrived = lax.all_to_all(
            dispatch_rows(experts * start, experts * (start + size)).reshape(
                experts, size, 2 * width
            ),
            "expert",
            split_axis=0,
            concat_axis=0,
            tiled=True,
        ).reshape(experts * size, 2 * width)
        flat_arrived = arrived[:, :width]
        flat_grad = arrived[:, width:]
        hidden_grad = lax.dot_general(
            flat_grad, expert_second, COL_CONTRACT, preferred_element_type=jnp.float32
        )
        pre_act = jnp.dot(flat_arrived, expert_first, preferred_element_type=jnp.float32)
        activated, slope = gelu_parts(pre_act)
        activated = activated.astype(jnp.bfloat16)
        pre_grad = (hidden_grad * slope).astype(jnp.bfloat16)
        produced = jnp.dot(
            activated, expert_second, preferred_element_type=jnp.float32
        ).astype(jnp.bfloat16)
        row_grad = lax.dot_general(
            pre_grad, expert_first, COL_CONTRACT, preferred_element_type=jnp.float32
        ).astype(jnp.bfloat16)
        part_second = lax.dot_general(
            activated, flat_grad, ROW_CONTRACT, preferred_element_type=jnp.float32
        )
        part_first = lax.dot_general(
            flat_arrived, pre_grad, ROW_CONTRACT, preferred_element_type=jnp.float32
        )
        grad_first = part_first if grad_first is None else grad_first + part_first
        grad_second = part_second if grad_second is None else grad_second + part_second
        returning = jnp.concatenate([produced, row_grad], axis=1).reshape(
            experts, size, 2 * width
        )
        returned_parts.append(
            lax.all_to_all(returning, "expert", split_axis=0, concat_axis=0, tiled=True)
        )

    expert_grads = jnp.stack(
        [grad_first, grad_second.reshape(width, ff)], axis=0
    ).astype(jnp.bfloat16)
    expert_share = lax.psum_scatter(expert_grads, "shard", scatter_dimension=1, tiled=True)
    expert_share = expert_share.astype(jnp.float32)
    grad_in_share = expert_share[0][None]
    grad_back_share = expert_share[1].reshape(back_rows, width)[None]

    picked_first = None
    picked_second = None
    for start, size, part in zip(chunk_starts, chunk_sizes, returned_parts):
        low, high = experts * start, experts * (start + size)
        part = part.reshape(-1, 2 * width)
        part_first = lax.dot_general(
            take_first[low:high], part, ROW_CONTRACT, preferred_element_type=jnp.float32
        )
        part_second = lax.dot_general(
            take_second[low:high], part, ROW_CONTRACT, preferred_element_type=jnp.float32
        )
        picked_first = part_first if picked_first is None else picked_first + part_first
        picked_second = part_second if picked_second is None else picked_second + part_second
    moe_out = (
        weighted[:, 0:1] * picked_first[:, :width] + weighted[:, 1:2] * picked_second[:, :width]
    )
    output = (live_rows[:, None] * (hidden_state + moe_out)).astype(jnp.bfloat16)
    grad_chosen = jnp.stack(
        [
            jnp.sum(grad_out * picked_first[:, :width], axis=1),
            jnp.sum(grad_out * picked_second[:, :width], axis=1),
        ],
        axis=1,
    ) * live_rows[:, None]
    expert_part = (picked_first[:, width:] + picked_second[:, width:]) * live_rows[:, None]
    prob_sum = jnp.sum(choose * grad_chosen[:, :, None], axis=1)
    logit_grad = (
        router_probs * (prob_sum - jnp.sum(router_probs * prob_sum, axis=-1, keepdims=True))
    ).astype(jnp.bfloat16)
    grad_router = lax.dot_general(
        moe_in, logit_grad, ROW_CONTRACT, preferred_element_type=jnp.float32
    )
    moe_in_grad = expert_part + lax.dot_general(
        logit_grad, full_router, COL_CONTRACT, preferred_element_type=jnp.float32
    )
    _, norm_back = jax.vjp(layer_norm, hidden_state, gain_two)
    state_part, grad_gain_two = norm_back(moe_in_grad)
    state_grad = grad_out + state_part
    branch_grad = state_grad.astype(jnp.bfloat16)
    grad_wout = lax.dot_general(
        mixed_rows, branch_grad, ROW_CONTRACT, preferred_element_type=jnp.float32
    )
    mixed_grad = lax.dot_general(
        branch_grad, full_out, COL_CONTRACT, preferred_element_type=jnp.float32
    )
    mixed_grad = jnp.pad(mixed_grad.astype(jnp.bfloat16), ((0, pad_rows - rows), (0, 0)))
    grad_q, grad_k, grad_v = attention_bwd(projected_pad, mixed_grad, images)
    projected_grad = jnp.concatenate([grad_q, grad_k, grad_v], axis=1)
    attn_in_pad = jnp.pad(attn_in, ((0, pad_rows - rows), (0, 0)))
    grad_qkv = lax.dot_general(
        attn_in_pad, projected_grad, ROW_CONTRACT, preferred_element_type=jnp.float32
    )
    attn_in_grad = lax.dot_general(
        projected_grad[:rows], full_qkv, COL_CONTRACT, preferred_element_type=jnp.float32
    )
    _, first_back = jax.vjp(layer_norm, token_f, gain_one)
    token_part, grad_gain_one = first_back(attn_in_grad)
    grad_tokens = (state_grad + token_part).astype(jnp.bfloat16)

    small = jnp.concatenate(
        [grad_router, grad_gain_one[:, None], grad_gain_two[:, None]], axis=1
    )
    small = jnp.pad(small, ((0, 0), (0, 128 - small.shape[1])))
    dense_grads = jnp.concatenate([grad_qkv, grad_wout, small], axis=1)
    n_parts = 3
    bounds = [128 * (dense_grads.shape[1] * k // (128 * n_parts)) for k in range(n_parts)]
    bounds = bounds + [dense_grads.shape[1]]
    dense_total = jnp.concatenate(
        [
            expert_all_reduce_doubling(
                shard_reduce_scatter(part, "shard", 128 * (part.shape[1] // 256)), "expert"
            )
            for part in (dense_grads[:, low:high] for low, high in zip(bounds[:-1], bounds[1:]))
        ],
        axis=1,
    )
    return (
        output,
        grad_tokens,
        dense_total[:, :qkv_cols],
        dense_total[:, qkv_cols : qkv_cols + width],
        dense_total[:, qkv_cols + width : qkv_cols + width + n_route],
        dense_total[:, qkv_cols + width + n_route],
        dense_total[:, qkv_cols + width + n_route + 1],
        grad_in_share,
        grad_back_share,
    )


def solution(mesh):
    return _mapped(mesh)


def _mapped(mesh):
    return jax.shard_map(
        shards,
        mesh=mesh,
        in_specs=(
            P(("expert", "shard"), None),
            P("expert", "shard"),
            P(("expert", "shard"), None),
            P("shard", None),
            P("shard", None),
            P("shard", None),
            P("shard"),
            P("shard"),
            P("expert", "shard", None),
            P("expert", "shard", None),
            P(("expert", "shard"), None),
        ),
        out_specs=(
            P(("expert", "shard"), None),
            P(("expert", "shard"), None),
            P("shard", None),
            P("shard", None),
            P("shard", None),
            P("shard"),
            P("shard"),
            P("expert", "shard", None),
            P("expert", "shard", None),
        ),
        check_vma=False,
    )
```
